32 devices in a mesh: slot: 8 (over y, x, core), head: 4 (over z).
Axes of the slice: x: 2, y: 2, z: 4, core: 2. Of those that a mesh axis runs over, the one named last changes fastest.
Arguments:
- activations: bfloat16 [4096, 6144], P('slot'), may hold values from -6 to 6
- mod_table: bfloat16 [8, 3, 6144], replicated, may hold values from -3 to 3
- step_index: int32 [8], replicated, may hold values from 0 to 7
- block_mask: int32 [8, 4, 32], replicated, may hold values 0 or 1
- cache_index: int32 [8, 6], replicated, may hold values from 0 to 7, as said below
- w_qkv: bfloat16 [6144, 3, 1536], P(None, None, 'head'), may hold values from -0.078125 to 0.078125
- q_gain: float32 [1536], P('head')
- k_gain: float32 [1536], P('head')
- pool_kv: bfloat16 [8, 512, 2, 1536], P('slot', None, None, 'head')
- w_out: bfloat16 [1536, 6144], P('head'), may hold values from -0.15625 to 0.15625
Outputs:
- result: float32 [4096, 6144], P('slot', 'head')
The draws below stay inside these ranges and needn't reach their ends.
Inputs may be any that keep to these rules, and one draw needn't show every extreme that they name: `cache_index`: the 6 entries of one row are distinct.
All inputs are finite; a program needn't handle non-finite values.
Results may differ from the reference program's by a relative error of at most 0.0065.
The reference program's roundings to bfloat16 on the way count: a program that leaves them out, or rounds other values in their place, can miss the bound.
Values may be sent and summed in bfloat16 or wider, within the bound.
No kernel may reach another device: no remote copies, remote signals or barrier semaphores. Data moves between devices by JAX's collectives and lax.ppermute only.
A program may use at most 128 MiB of HBM per device.

```python
import jax
import jax.numpy as jnp
from jax import lax

D = 6144
HD = 128
HEADS_DEV = 3
SPAN = 512
BLOCK = 128
CACHE = 6
STEPS = 8
SLOTS = 8
POOL = 8
HEADS = 12
TOKENS = 4096
N_HEAD = 4


def draw_cache_index(key, part):
    keys = jax.random.split(key, SLOTS)
    rows = jax.vmap(lambda single: jax.random.permutation(single, POOL)[:CACHE])(keys).astype(jnp.int32)
    middle = (jax.random.permutation(jax.random.fold_in(key, 7), POOL - 2)[:CACHE - 2] + 1).astype(jnp.int32)
    special = jnp.concatenate([jnp.array([0, POOL - 1], dtype=jnp.int32), middle])
    special = jax.random.permutation(jax.random.fold_in(key, 11), special).astype(jnp.int32)
    which = jax.random.randint(jax.random.fold_in(key, 13), (), 0, SLOTS)
    return rows.at[which].set(special)


def gain_values(key):
    base = jax.random.uniform(key, (HEADS * HD,), jnp.float32, 0.6, 1.6)
    return base


def draw_q_gain(key, part):
    return gain_values(jax.random.fold_in(key, 1))


def draw_k_gain(key, part):
    return gain_values(jax.random.fold_in(key, 2))


def draw_pool_kv(key, part):
    values = jax.random.normal(key, (POOL, SPAN, 2, HEADS * HD), jnp.float32)
    return values.astype(jnp.bfloat16)


def with_ends(values, key, smallest, largest):
    longest = values.shape.index(max(values.shape))
    spots = []
    for shift in (0, 1):
        where = [jax.random.randint(jax.random.fold_in(key, axis), (), 0, length) for axis, length in enumerate(values.shape)]
        where[longest] = (where[longest] + shift) % values.shape[longest]
        spots.append(tuple(where))
    return values.at[spots[0]].set(smallest).at[spots[1]].set(largest)


def levels(rng, extent, cuts, low, largest):
    factor_of = 1.0
    for axis_at, parts in cuts:
        heights = jax.random.uniform(jax.random.fold_in(jax.random.fold_in(rng, 6), axis_at), (parts,), jnp.float32, low / len(cuts), largest / len(cuts))
        factor_of = factor_of * jnp.repeat(jnp.exp(heights), extent[axis_at] // parts).reshape((-1,) + (1,) * (len(extent) - 1 - axis_at))
    return factor_of


def noise(rng, extent, deviation, reach, shards=(), held_as=jnp.bfloat16):
    result = jax.random.normal(rng, extent, jnp.float32) * deviation
    if len(shards) > 0:
        result = levels(rng, extent, shards, -0.22, 0.18) * result
    return jnp.clip(result, min=-reach, max=reach).astype(held_as)


def setup_inputs(seed: int = 0) -> dict:
    arg_keys = jax.random.split(jax.random.key(seed), 11)
    return {
        "activations": noise(arg_keys[0], (TOKENS, D), 1.0, 6.0, ((0, 8),)),
        "mod_table": noise(arg_keys[1], (STEPS, 3, D), 0.5, 3.0),
        "step_index": with_ends(jax.random.randint(arg_keys[2], (SLOTS,), 0, STEPS), jax.random.fold_in(arg_keys[2], 1), 0, STEPS - 1).astype(jnp.int32),
        "block_mask": with_ends((jax.random.randint(arg_keys[3], (SLOTS, SPAN // BLOCK, 8 * (SPAN // BLOCK)), 0, 4) < 3).astype(jnp.int32), jax.random.fold_in(arg_keys[3], 1), 0, 1),
        "cache_index": draw_cache_index(jax.random.fold_in(arg_keys[10], 71), 0),
        "w_qkv": noise(arg_keys[5], (D, 3, HEADS * HD), D ** -0.5, 0.078125, ((2, 4),)),
        "q_gain": draw_q_gain(jax.random.fold_in(arg_keys[10], 71), 0),
        "k_gain": draw_k_gain(jax.random.fold_in(arg_keys[10], 71), 0),
        "pool_kv": draw_pool_kv(jax.random.fold_in(arg_keys[10], 71), 0),
        "w_out": noise(arg_keys[9], (HEADS * HD, D), (HEADS * HD) ** -0.5, 0.15625, ((0, 4),)),
    }


def head_norm(values, gain):
    scaled = values * lax.rsqrt(lax.optimization_barrier(jnp.mean(values * values, axis=-1, keepdims=True)) + 1e-06)
    return scaled * gain.reshape(HEADS, HD)

def reference(activations, mod_table, step_index, block_mask, cache_index, w_qkv, q_gain, k_gain, pool_kv, w_out):
    onehot = (step_index[:, None] == jnp.arange(STEPS, dtype=jnp.int32)[None, :]).astype(jnp.float32)
    modulation = jnp.einsum('sn,nkd->skd', onehot, mod_table.astype(jnp.float32))
    inputs = activations.reshape(SLOTS, SPAN, D).astype(jnp.float32)
    normed = inputs * lax.rsqrt(lax.optimization_barrier(jnp.mean(inputs * inputs, axis=-1, keepdims=True)) + 1e-06)
    hidden = (normed * (1.0 + modulation[:, 1][:, None, :]) + modulation[:, 0][:, None, :]).astype(jnp.bfloat16)
    qkv = jnp.einsum('scd,dkh->sckh', hidden.astype(jnp.float32), w_qkv.astype(jnp.float32))
    queries = head_norm(qkv[:, :, 0].reshape(SLOTS, SPAN, HEADS, HD), q_gain).astype(jnp.bfloat16)
    keys = head_norm(qkv[:, :, 1].reshape(SLOTS, SPAN, HEADS, HD), k_gain).astype(jnp.bfloat16)
    values = qkv[:, :, 2].reshape(SLOTS, SPAN, HEADS, HD).astype(jnp.bfloat16)
    pool_keys = pool_kv[:, :, 0].reshape(POOL, SPAN, HEADS, HD)
    pool_values = pool_kv[:, :, 1].reshape(POOL, SPAN, HEADS, HD)
    out_weight = w_out.astype(jnp.float32).reshape(N_HEAD, HEADS_DEV * HD, D)
    blocks_q = SPAN // BLOCK
    scale = 1.0 / HD ** 0.5

    def one_slot(slot):
        before = (slot - 1) % SLOTS
        earlier = (slot - 2) % SLOTS
        chosen = cache_index[slot]
        all_keys = jnp.concatenate([keys[slot], keys[before], keys[earlier], pool_keys[chosen].reshape(CACHE * SPAN, HEADS, HD)], axis=0)
        all_values = jnp.concatenate([values[slot], values[before], values[earlier], pool_values[chosen].reshape(CACHE * SPAN, HEADS, HD)], axis=0)
        visible = jnp.concatenate([jnp.ones((blocks_q, blocks_q), jnp.int32), block_mask[slot]], axis=1)
        visible = jnp.repeat(jnp.repeat(visible, BLOCK, axis=0), BLOCK, axis=1) > 0
        scores = jnp.einsum('qhd,khd->hqk', queries[slot].astype(jnp.float32), all_keys.astype(jnp.float32)) * scale
        scores = jnp.where(visible[None], scores, -1e+30)
        highest = lax.optimization_barrier(jnp.max(scores, axis=-1, keepdims=True))
        weights = jnp.where(visible[None], jnp.exp(scores - highest), 0.0)
        totals = lax.optimization_barrier(jnp.sum(weights, axis=-1))
        rounded = weights.astype(jnp.bfloat16)
        mixed = jnp.einsum('hqk,khd->qhd', rounded.astype(jnp.float32), all_values.astype(jnp.float32))
        mixed = (mixed / jnp.transpose(totals)[:, :, None]).astype(jnp.bfloat16)
        grouped = mixed.reshape(SPAN, N_HEAD, HEADS_DEV * HD).astype(jnp.float32)
        terms = jnp.einsum('cgk,gkd->cgd', grouped, out_weight).astype(jnp.bfloat16)
        terms = lax.optimization_barrier(terms)
        attn = lax.optimization_barrier(jnp.sum(terms.astype(jnp.float32), axis=1))
        return inputs[slot] + modulation[slot, 2][None, :] * attn
    outputs = lax.map(one_slot, jnp.arange(SLOTS, dtype=jnp.int32))
    return outputs.reshape(SLOTS * SPAN, D)
```

```python
import jax
import jax.numpy as jnp
from jax import lax
from jax.sharding import PartitionSpec as P

HD = 128
BLOCK = 128


def from_behind(shard, axis, by):
    length = lax.axis_size(axis)
    return lax.ppermute(shard, axis, [(i, (i + by) % length) for i in range(length)])


def head_norm(values, gain, heads):
    shaped = values.reshape(values.shape[0], heads, HD)
    scaled = shaped * lax.rsqrt(jnp.mean(shaped * shaped, axis=-1, keepdims=True) + 1e-06)
    return scaled * gain.reshape(heads, HD)


def attend(state, queries, span_kv, visible_blocks):
    highest, totals, accum = state
    heads = queries.shape[1]
    span_keys = span_kv[:, 0].reshape(span_kv.shape[0], heads, HD)
    span_values = span_kv[:, 1].reshape(span_kv.shape[0], heads, HD)
    visible = jnp.repeat(jnp.repeat(visible_blocks, BLOCK, axis=0), BLOCK, axis=1) > 0
    scores = jnp.einsum("qhd,khd->hqk", queries, span_keys, preferred_element_type=jnp.float32) * (
        1.0 / HD**0.5
    )
    scores = jnp.where(visible[None], scores, -1e30)
    new_high = jnp.maximum(highest, jnp.max(scores, axis=-1))
    factor = jnp.exp(highest - new_high)
    weights = jnp.where(visible[None], jnp.exp(scores - new_high[..., None]), 0.0)
    totals = totals * factor + jnp.sum(weights, axis=-1)
    accum = accum * factor[..., None] + jnp.einsum(
        "hqk,khd->hqd",
        weights.astype(jnp.bfloat16),
        span_values,
        preferred_element_type=jnp.float32,
    )
    return (new_high, totals, accum)


def fetch_out_weight(w_out, head, core):
    groups = lax.axis_size("head")
    columns = w_out.shape[1] // groups
    half = columns // 2
    mine = []
    for shift in range(groups):
        dest = (head + shift) % groups
        block = lax.dynamic_slice_in_dim(w_out, dest * columns + core * half, half, 1)
        if shift:
            block = lax.ppermute(block, "head", [(i, (i + shift) % groups) for i in range(groups)])
        mine.append(block)
    own_full = lax.dynamic_slice_in_dim(w_out, head * columns, columns, 1)
    return own_full, mine


def local(
    activations,
    mod_table,
    step_index,
    block_mask,
    cache_index,
    w_qkv,
    q_gain,
    k_gain,
    pool_kv,
    w_out,
):
    slot = lax.axis_index("slot")
    head = lax.axis_index("head")
    core = slot % 2
    groups = lax.axis_size("head")
    span = activations.shape[0]
    heads = q_gain.shape[0] // HD
    blocks_q = span // BLOCK
    cache_len = cache_index.shape[1]

    own_full, mine = fetch_out_weight(w_out, head, core)
    piece = lax.all_gather(pool_kv, "slot", axis=0, tiled=True)

    onehot = (jnp.arange(mod_table.shape[0], dtype=jnp.int32) == step_index[slot]).astype(
        jnp.float32
    )
    modulation = jnp.einsum("n,nkd->kd", onehot, mod_table.astype(jnp.float32))
    inputs = activations.astype(jnp.float32)
    normed = inputs * lax.rsqrt(jnp.mean(inputs * inputs, axis=-1, keepdims=True) + 1e-06)
    hidden = (normed * (1.0 + modulation[1][None, :]) + modulation[0][None, :]).astype(jnp.bfloat16)
    qkv = jnp.einsum("td,dkh->tkh", hidden, w_qkv, preferred_element_type=jnp.float32)
    queries = head_norm(qkv[:, 0], q_gain, heads).astype(jnp.bfloat16)
    keys = head_norm(qkv[:, 1], k_gain, heads).astype(jnp.bfloat16)
    values = qkv[:, 2].astype(jnp.bfloat16)
    local_kv = jnp.stack([keys.reshape(span, heads * HD), values], axis=1)
    own_mask = lax.dynamic_index_in_dim(block_mask, slot, 0, keepdims=False)
    own_cache = lax.dynamic_index_in_dim(cache_index, slot, 0, keepdims=False)
    state = (
        jnp.full((heads, span), -1e30, jnp.float32),
        jnp.zeros((heads, span), jnp.float32),
        jnp.zeros((heads, span, HD), jnp.float32),
    )
    before = from_behind(local_kv, "slot", 1)
    earlier = from_behind(local_kv, "slot", 2)
    state = attend(state, queries, local_kv, jnp.ones((blocks_q, blocks_q), jnp.int32))
    state = attend(state, queries, before, own_mask[:, :blocks_q])
    state = attend(state, queries, earlier, own_mask[:, blocks_q : 2 * blocks_q])
    state, mine = lax.optimization_barrier((state, mine))

    def turn(place, inner):
        span_kv = lax.dynamic_index_in_dim(piece, own_cache[place], 0, keepdims=False)
        visible_blocks = lax.dynamic_slice_in_dim(own_mask, (2 + place) * blocks_q, blocks_q, 1)
        return attend(inner, queries, span_kv, visible_blocks)

    state = lax.fori_loop(0, cache_len, turn, state)
    slots = lax.axis_size("slot")
    sibling = lax.ppermute(
        jnp.stack(mine[1:]), "slot", [(i, i ^ 1) for i in range(slots)]
    )
    highest, totals, accum = state
    mixed = (accum / totals[..., None]).astype(jnp.bfloat16)
    mixed = jnp.transpose(mixed, (1, 0, 2)).reshape(span, heads * HD)

    gathered = lax.all_gather(mixed, "head", axis=0, tiled=False)
    columns = own_full.shape[1]
    half = columns // 2
    attn = jnp.dot(mixed, own_full, preferred_element_type=jnp.float32).astype(jnp.bfloat16).astype(jnp.float32)
    attn_mine = None
    attn_sib = None
    for shift in range(1, groups):
        group_o = lax.dynamic_index_in_dim(gathered, (head - shift) % groups, 0, keepdims=False)
        part = jnp.dot(group_o, mine[shift], preferred_element_type=jnp.float32)
        part = part.astype(jnp.bfloat16).astype(jnp.float32)
        attn_mine = part if attn_mine is None else attn_mine + part
        part = jnp.dot(group_o, sibling[shift - 1], preferred_element_type=jnp.float32)
        part = part.astype(jnp.bfloat16).astype(jnp.float32)
        attn_sib = part if attn_sib is None else attn_sib + part
    other = jnp.concatenate([attn_mine, attn_sib], axis=1)
    swapped = jnp.concatenate([attn_sib, attn_mine], axis=1)
    attn = attn + jnp.where(core == 0, other, swapped)

    offset = head * columns
    input_cols = lax.dynamic_slice_in_dim(inputs, offset, columns, 1)
    gate_cols = lax.dynamic_slice_in_dim(modulation[2], offset, columns, 0)
    return input_cols + gate_cols[None, :] * attn


def solution(mesh):
    placed = (
        P("slot", None),
        P(),
        P(),
        P(),
        P(),
        P(None, None, "head"),
        P("head"),
        P("head"),
        P("slot", None, None, "head"),
        P("head", None),
    )
    return jax.shard_map(
        local, mesh=mesh, in_specs=placed, out_specs=P("slot", "head"), check_vma=False
    )
```

```python
import jax
import jax.numpy as jnp
from jax import lax
from jax.sharding import PartitionSpec as P

HD = 128
BLOCK = 128


def from_behind(shard, axis, by):
    length = lax.axis_size(axis)
    return lax.ppermute(shard, axis, [(i, (i + by) % length) for i in range(length)])


def head_norm(values, gain, heads):
    shaped = values.reshape(values.shape[0], heads, HD)
    scaled = shaped * lax.rsqrt(jnp.mean(shaped * shaped, axis=-1, keepdims=True) + 1e-06)
    return scaled * gain.reshape(heads, HD)


def attend(state, queries, span_kv, visible_blocks):
    highest, totals, accum = state
    heads = queries.shape[1]
    span_keys = span_kv[:, 0].reshape(span_kv.shape[0], heads, HD)
    span_values = span_kv[:, 1].reshape(span_kv.shape[0], heads, HD)
    visible = jnp.repeat(jnp.repeat(visible_blocks, BLOCK, axis=0), BLOCK, axis=1) > 0
    scores = jnp.einsum("qhd,khd->hqk", queries, span_keys, preferred_element_type=jnp.float32) * (
        1.0 / HD**0.5
    )
    scores = jnp.where(visible[None], scores, -1e30)
    new_high = jnp.maximum(highest, jnp.max(scores, axis=-1))
    factor = jnp.exp(highest - new_high)
    weights = jnp.where(visible[None], jnp.exp(scores - new_high[..., None]), 0.0)
    totals = totals * factor + jnp.sum(weights, axis=-1)
    accum = accum * factor[..., None] + jnp.einsum(
        "hqk,khd->hqd",
        weights.astype(jnp.bfloat16),
        span_values,
        preferred_element_type=jnp.float32,
    )
    return (new_high, totals, accum)


def fetch_out_weight(w_out, head, core):
    groups = lax.axis_size("head")
    columns = w_out.shape[1] // groups
    half = columns // 2
    mine = []
    for shift in range(groups):
        dest = (head + shift) % groups
        block = lax.dynamic_slice_in_dim(w_out, dest * columns + core * half, half, 1)
        if shift:
            block = lax.ppermute(block, "head", [(i, (i + shift) % groups) for i in range(groups)])
        mine.append(block)
    own_full = lax.dynamic_slice_in_dim(w_out, head * columns, columns, 1)
    return own_full, mine


def local(
    activations,
    mod_table,
    step_index,
    block_mask,
    cache_index,
    w_qkv,
    q_gain,
    k_gain,
    pool_kv,
    w_out,
):
    slot = lax.axis_index("slot")
    head = lax.axis_index("head")
    core = slot % 2
    groups = lax.axis_size("head")
    span = activations.shape[0]
    heads = q_gain.shape[0] // HD
    blocks_q = span // BLOCK
    cache_len = cache_index.shape[1]

    own_full, mine = fetch_out_weight(w_out, head, core)
    piece = lax.all_gather(pool_kv, "slot", axis=0, tiled=True)

    onehot = (jnp.arange(mod_table.shape[0], dtype=jnp.int32) == step_index[slot]).astype(
        jnp.float32
    )
    modulation = jnp.einsum("n,nkd->kd", onehot, mod_table.astype(jnp.float32))
    inputs = activations.astype(jnp.float32)
    normed = inputs * lax.rsqrt(jnp.mean(inputs * inputs, axis=-1, keepdims=True) + 1e-06)
    hidden = (normed * (1.0 + modulation[1][None, :]) + modulation[0][None, :]).astype(jnp.bfloat16)
    qkv = jnp.einsum("td,dkh->tkh", hidden, w_qkv, preferred_element_type=jnp.float32)
    queries = head_norm(qkv[:, 0], q_gain, heads).astype(jnp.bfloat16)
    keys = head_norm(qkv[:, 1], k_gain, heads).astype(jnp.bfloat16)
    values = qkv[:, 2].astype(jnp.bfloat16)
    local_kv = jnp.stack([keys.reshape(span, heads * HD), values], axis=1)
    own_mask = lax.dynamic_index_in_dim(block_mask, slot, 0, keepdims=False)
    own_cache = lax.dynamic_index_in_dim(cache_index, slot, 0, keepdims=False)
    state = (
        jnp.full((heads, span), -1e30, jnp.float32),
        jnp.zeros((heads, span), jnp.float32),
        jnp.zeros((heads, span, HD), jnp.float32),
    )
    before = from_behind(local_kv, "slot", 1)
    earlier = from_behind(local_kv, "slot", 2)
    state = attend(state, queries, local_kv, jnp.ones((blocks_q, blocks_q), jnp.int32))
    state = attend(state, queries, before, own_mask[:, :blocks_q])
    state = attend(state, queries, earlier, own_mask[:, blocks_q : 2 * blocks_q])
    state, mine = lax.optimization_barrier((state, mine))

    def turn(place, inner):
        span_kv = lax.dynamic_index_in_dim(piece, own_cache[place], 0, keepdims=False)
        visible_blocks = lax.dynamic_slice_in_dim(own_mask, (2 + place) * blocks_q, blocks_q, 1)
        return attend(inner, queries, span_kv, visible_blocks)

    state = lax.fori_loop(0, cache_len, turn, state)
    slots = lax.axis_size("slot")
    sibling = lax.ppermute(
        jnp.stack(mine[1:]), "slot", [(i, i ^ 1) for i in range(slots)]
    )
    highest, totals, accum = state
    mixed = (accum / totals[..., None]).astype(jnp.bfloat16)
    mixed = jnp.transpose(mixed, (1, 0, 2)).reshape(span, heads * HD)

    received = [
        lax.ppermute(mixed, "head", [(i, (i + shift) % groups) for i in range(groups)])
        for shift in range(1, groups)
    ]
    columns = own_full.shape[1]
    half = columns // 2
    attn = jnp.dot(mixed, own_full, preferred_element_type=jnp.float32).astype(jnp.bfloat16).astype(jnp.float32)
    attn_mine = None
    attn_sib = None
    for shift in range(1, groups):
        group_o = received[shift - 1]
        part = jnp.dot(group_o, mine[shift], preferred_element_type=jnp.float32)
        part = part.astype(jnp.bfloat16).astype(jnp.float32)
        attn_mine = part if attn_mine is None else attn_mine + part
        part = jnp.dot(group_o, sibling[shift - 1], preferred_element_type=jnp.float32)
        part = part.astype(jnp.bfloat16).astype(jnp.float32)
        attn_sib = part if attn_sib is None else attn_sib + part
    other = jnp.concatenate([attn_mine, attn_sib], axis=1)
    swapped = jnp.concatenate([attn_sib, attn_mine], axis=1)
    attn = attn + jnp.where(core == 0, other, swapped)

    offset = head * columns
    input_cols = lax.dynamic_slice_in_dim(activations, offset, columns, 1).astype(jnp.float32)
    gate_cols = lax.dynamic_slice_in_dim(modulation[2], offset, columns, 0)
    return input_cols + gate_cols[None, :] * attn


def solution(mesh):
    placed = (
        P("slot", None),
        P(),
        P(),
        P(),
        P(),
        P(None, None, "head"),
        P("head"),
        P("head"),
        P("slot", None, None, "head"),
        P("head", None),
    )
    return jax.shard_map(
        local, mesh=mesh, in_specs=placed, out_specs=P("slot", "head"), check_vma=False
    )
```

```python
import jax
import jax.numpy as jnp
from jax import lax
from jax.sharding import PartitionSpec as P
from jax.experimental import pallas as pl
from jax.experimental.pallas import tpu as pltpu

HD = 128
BLOCK = 128


def from_behind(shard, axis, by):
    length = lax.axis_size(axis)
    return lax.ppermute(shard, axis, [(i, (i + by) % length) for i in range(length)])


def head_norm(values, gain, heads):
    shaped = values.reshape(values.shape[0], heads, HD)
    scaled = shaped * lax.rsqrt(jnp.mean(shaped * shaped, axis=-1, keepdims=True) + 1e-06)
    return scaled * gain.reshape(heads, HD)


def attend(state, queries, span_kv, visible_blocks):
    highest, totals, accum = state
    heads = queries.shape[1]
    span_keys = span_kv[:, 0].reshape(span_kv.shape[0], heads, HD)
    span_values = span_kv[:, 1].reshape(span_kv.shape[0], heads, HD)
    visible = jnp.repeat(jnp.repeat(visible_blocks, BLOCK, axis=0), BLOCK, axis=1) > 0
    scores = jnp.einsum("qhd,khd->hqk", queries, span_keys, preferred_element_type=jnp.float32) * (
        1.0 / HD**0.5
    )
    scores = jnp.where(visible[None], scores, -1e30)
    new_high = jnp.maximum(highest, jnp.max(scores, axis=-1))
    factor = jnp.exp(highest - new_high)
    weights = jnp.where(visible[None], jnp.exp(scores - new_high[..., None]), 0.0)
    totals = totals * factor + jnp.sum(weights, axis=-1)
    accum = accum * factor[..., None] + jnp.einsum(
        "hqk,khd->hqd",
        weights.astype(jnp.bfloat16),
        span_values,
        preferred_element_type=jnp.float32,
    )
    return (new_high, totals, accum)


def flash_kernel(chosen, q_ref, lk_ref, lv_ref, pk_ref, pv_ref, bias_ref, o_ref, m_sc, l_sc, acc_sc, *, heads, n_local):
    step = pl.program_id(0)
    span = q_ref.shape[0]
    blocks = bias_ref.shape[0]

    @pl.when(step == 0)
    def _():
        m_sc[...] = jnp.full(m_sc.shape, -1e30, jnp.float32)
        l_sc[...] = jnp.zeros(l_sc.shape, jnp.float32)
        acc_sc[...] = jnp.zeros(acc_sc.shape, jnp.float32)

    def body(k_ref, v_ref):
        bias = bias_ref[...][:, None, :]
        for h in range(heads):
            cols = slice(h * HD, (h + 1) * HD)
            q = q_ref[:, cols]
            k = k_ref[:, cols]
            s = lax.dot_general(q, k, (((1,), (1,)), ((), ())), preferred_element_type=jnp.float32)
            s = (s * (1.0 / HD**0.5)).reshape(blocks, span // blocks, s.shape[1]) + bias
            s = s.reshape(span, -1)
            m_prev = m_sc[h]
            m_new = jnp.maximum(m_prev, jnp.max(s, axis=1, keepdims=True))
            factor = jnp.exp(m_prev - m_new)
            p = jnp.exp(s - m_new)
            l_sc[h] = l_sc[h] * factor + jnp.sum(p, axis=1, keepdims=True)
            acc_sc[h] = acc_sc[h] * factor + jnp.dot(
                p.astype(jnp.bfloat16), v_ref[:, cols], preferred_element_type=jnp.float32
            )
            m_sc[h] = m_new

    @pl.when(step < n_local)
    def _():
        body(lk_ref, lv_ref)

    @pl.when(step >= n_local)
    def _():
        body(pk_ref, pv_ref)

    @pl.when(step == pl.num_programs(0) - 1)
    def _():
        for h in range(heads):
            cols = slice(h * HD, (h + 1) * HD)
            o_ref[:, cols] = (acc_sc[h] / l_sc[h]).astype(o_ref.dtype)


def flash(queries, local_stack, piece, bias, chosen, heads):
    span, width = queries.shape
    n_local = local_stack.shape[0]
    steps = n_local + chosen.shape[0]
    blocks = bias.shape[1]

    def local_map(kv):
        return lambda j, c: (jnp.minimum(j, n_local - 1), 0, kv)

    def pool_map(kv):
        return lambda j, c: (c[jnp.maximum(j - n_local, 0)], 0, kv)

    kv_block = (None, span, width)
    grid_spec = pltpu.PrefetchScalarGridSpec(
        num_scalar_prefetch=1,
        grid=(steps,),
        in_specs=[
            pl.BlockSpec((span, width), lambda j, c: (0, 0)),
            pl.BlockSpec(kv_block, local_map(0)),
            pl.BlockSpec(kv_block, local_map(1)),
            pl.BlockSpec(kv_block, pool_map(0)),
            pl.BlockSpec(kv_block, pool_map(1)),
            pl.BlockSpec((None, blocks, span), lambda j, c: (j, 0, 0)),
        ],
        out_specs=pl.BlockSpec((span, width), lambda j, c: (0, 0)),
        scratch_shapes=[
            pltpu.VMEM((heads, span, 1), jnp.float32),
            pltpu.VMEM((heads, span, 1), jnp.float32),
            pltpu.VMEM((heads, span, HD), jnp.float32),
        ],
    )
    kernel = lambda *refs: flash_kernel(*refs, heads=heads, n_local=n_local)
    return pl.pallas_call(
        kernel,
        grid_spec=grid_spec,
        out_shape=jax.ShapeDtypeStruct((span, width), jnp.bfloat16),
        compiler_params=pltpu.CompilerParams(dimension_semantics=("arbitrary",)),
        cost_estimate=pl.CostEstimate(
            flops=4 * steps * heads * span * span * HD,
            transcendentals=steps * heads * span * span,
            bytes_accessed=2 * steps * span * width * 2,
        ),
    )(chosen, queries, local_stack, local_stack, piece, piece, bias)


def fetch_out_weight(w_out, head, core):
    groups = lax.axis_size("head")
    columns = w_out.shape[1] // groups
    half = columns // 2
    mine = []
    for shift in range(groups):
        dest = (head + shift) % groups
        block = lax.dynamic_slice_in_dim(w_out, dest * columns + core * half, half, 1)
        if shift:
            block = lax.ppermute(block, "head", [(i, (i + shift) % groups) for i in range(groups)])
        mine.append(block)
    own_full = lax.dynamic_slice_in_dim(w_out, head * columns, columns, 1)
    return own_full, mine


def local(
    activations,
    mod_table,
    step_index,
    block_mask,
    cache_index,
    w_qkv,
    q_gain,
    k_gain,
    pool_kv,
    w_out,
):
    slot = lax.axis_index("slot")
    head = lax.axis_index("head")
    core = slot % 2
    groups = lax.axis_size("head")
    span = activations.shape[0]
    heads = q_gain.shape[0] // HD
    blocks_q = span // BLOCK
    cache_len = cache_index.shape[1]

    own_full, mine = fetch_out_weight(w_out, head, core)
    piece = lax.all_gather(pool_kv, "slot", axis=0, tiled=True)

    onehot = (jnp.arange(mod_table.shape[0], dtype=jnp.int32) == step_index[slot]).astype(
        jnp.float32
    )
    modulation = jnp.einsum("n,nkd->kd", onehot, mod_table.astype(jnp.float32))
    inputs = activations.astype(jnp.float32)
    normed = inputs * lax.rsqrt(jnp.mean(inputs * inputs, axis=-1, keepdims=True) + 1e-06)
    hidden = (normed * (1.0 + modulation[1][None, :]) + modulation[0][None, :]).astype(jnp.bfloat16)
    qkv = jnp.einsum("td,dkh->tkh", hidden, w_qkv, preferred_element_type=jnp.float32)
    queries = head_norm(qkv[:, 0], q_gain, heads).astype(jnp.bfloat16)
    keys = head_norm(qkv[:, 1], k_gain, heads).astype(jnp.bfloat16)
    values = qkv[:, 2].astype(jnp.bfloat16)
    local_kv = jnp.stack([keys.reshape(span, heads * HD), values], axis=1)
    own_mask = lax.dynamic_index_in_dim(block_mask, slot, 0, keepdims=False)
    own_cache = lax.dynamic_index_in_dim(cache_index, slot, 0, keepdims=False)
    before = from_behind(local_kv, "slot", 1)
    earlier = from_behind(local_kv, "slot", 2)
    width = heads * HD
    local_stack = jnp.stack([local_kv, before, earlier]).reshape(3, span, 2 * width)
    pool_flat = piece.reshape(piece.shape[0], span, 2 * width)
    visible = jnp.concatenate([jnp.ones((blocks_q, blocks_q), jnp.int32), own_mask], axis=1)
    visible = jnp.transpose(visible.reshape(blocks_q, 3 + cache_len, blocks_q), (1, 0, 2))
    visible = jnp.repeat(visible, BLOCK, axis=2)
    bias = jnp.where(visible > 0, 0.0, -1e30).astype(jnp.float32)
    local_stack, mine = lax.optimization_barrier((local_stack, mine))
    mixed = flash(queries.reshape(span, width), local_stack, pool_flat, bias, own_cache, heads)
    slots = lax.axis_size("slot")
    sibling = lax.ppermute(
        jnp.stack(mine[1:]), "slot", [(i, i ^ 1) for i in range(slots)]
    )

    received = [
        lax.ppermute(mixed, "head", [(i, (i + shift) % groups) for i in range(groups)])
        for shift in range(1, groups)
    ]
    columns = own_full.shape[1]
    half = columns // 2
    attn = jnp.dot(mixed, own_full, preferred_element_type=jnp.float32).astype(jnp.bfloat16).astype(jnp.float32)
    attn_mine = None
    attn_sib = None
    for shift in range(1, groups):
        group_o = received[shift - 1]
        part = jnp.dot(group_o, mine[shift], preferred_element_type=jnp.float32)
        part = part.astype(jnp.bfloat16).astype(jnp.float32)
        attn_mine = part if attn_mine is None else attn_mine + part
        part = jnp.dot(group_o, sibling[shift - 1], preferred_element_type=jnp.float32)
        part = part.astype(jnp.bfloat16).astype(jnp.float32)
        attn_sib = part if attn_sib is None else attn_sib + part
    other = jnp.concatenate([attn_mine, attn_sib], axis=1)
    swapped = jnp.concatenate([attn_sib, attn_mine], axis=1)
    attn = attn + jnp.where(core == 0, other, swapped)

    offset = head * columns
    input_cols = lax.dynamic_slice_in_dim(activations, offset, columns, 1).astype(jnp.float32)
    gate_cols = lax.dynamic_slice_in_dim(modulation[2], offset, columns, 0)
    return input_cols + gate_cols[None, :] * attn


def solution(mesh):
    placed = (
        P("slot", None),
        P(),
        P(),
        P(),
        P(),
        P(None, None, "head"),
        P("head"),
        P("head"),
        P("slot", None, None, "head"),
        P("head", None),
    )
    return jax.shard_map(
        local, mesh=mesh, in_specs=placed, out_specs=P("slot", "head"), check_vma=False
    )
```

```python
import jax
import jax.numpy as jnp
from jax import lax
from jax.sharding import PartitionSpec as P
from jax.experimental import pallas as pl
from jax.experimental.pallas import tpu as pltpu

HD = 128
BLOCK = 128


def from_behind(shard, axis, by):
    length = lax.axis_size(axis)
    return lax.ppermute(shard, axis, [(i, (i + by) % length) for i in range(length)])


def head_norm(values, gain, heads):
    shaped = values.reshape(values.shape[0], heads, HD)
    scaled = shaped * lax.rsqrt(jnp.mean(shaped * shaped, axis=-1, keepdims=True) + 1e-06)
    return scaled * gain.reshape(heads, HD)


def attend(state, queries, span_kv, visible_blocks):
    highest, totals, accum = state
    heads = queries.shape[1]
    span_keys = span_kv[:, 0].reshape(span_kv.shape[0], heads, HD)
    span_values = span_kv[:, 1].reshape(span_kv.shape[0], heads, HD)
    visible = jnp.repeat(jnp.repeat(visible_blocks, BLOCK, axis=0), BLOCK, axis=1) > 0
    scores = jnp.einsum("qhd,khd->hqk", queries, span_keys, preferred_element_type=jnp.float32) * (
        1.0 / HD**0.5
    )
    scores = jnp.where(visible[None], scores, -1e30)
    new_high = jnp.maximum(highest, jnp.max(scores, axis=-1))
    factor = jnp.exp(highest - new_high)
    weights = jnp.where(visible[None], jnp.exp(scores - new_high[..., None]), 0.0)
    totals = totals * factor + jnp.sum(weights, axis=-1)
    accum = accum * factor[..., None] + jnp.einsum(
        "hqk,khd->hqd",
        weights.astype(jnp.bfloat16),
        span_values,
        preferred_element_type=jnp.float32,
    )
    return (new_high, totals, accum)


def flash_kernel(chosen, q_ref, lk_ref, lv_ref, pk_ref, pv_ref, bias_ref, o_ref, m_sc, l_sc, acc_sc, *, heads, n_local):
    step = pl.program_id(0)
    span = q_ref.shape[0]
    blocks = bias_ref.shape[0]

    @pl.when(step == 0)
    def _():
        m_sc[...] = jnp.full(m_sc.shape, -1e30, jnp.float32)
        l_sc[...] = jnp.zeros(l_sc.shape, jnp.float32)
        acc_sc[...] = jnp.zeros(acc_sc.shape, jnp.float32)

    def body(k_ref, v_ref):
        bias = bias_ref[...][:, None, :]
        for h in range(heads):
            cols = slice(h * HD, (h + 1) * HD)
            q = q_ref[:, cols]
            k = k_ref[:, cols]
            s = lax.dot_general(q, k, (((1,), (1,)), ((), ())), preferred_element_type=jnp.float32)
            s = (s * (1.0 / HD**0.5)).reshape(blocks, span // blocks, s.shape[1]) + bias
            s = s.reshape(span, -1)
            m_prev = m_sc[h]
            m_new = jnp.maximum(m_prev, jnp.max(s, axis=1, keepdims=True))
            factor = jnp.exp(m_prev - m_new)
            p = jnp.exp(s - m_new)
            l_sc[h] = l_sc[h] * factor + jnp.sum(p, axis=1, keepdims=True)
            acc_sc[h] = acc_sc[h] * factor + jnp.dot(
                p.astype(jnp.bfloat16), v_ref[:, cols], preferred_element_type=jnp.float32
            )
            m_sc[h] = m_new

    @pl.when(step < n_local)
    def _():
        body(lk_ref, lv_ref)

    @pl.when(step >= n_local)
    def _():
        body(pk_ref, pv_ref)

    @pl.when(step == pl.num_programs(0) - 1)
    def _():
        for h in range(heads):
            cols = slice(h * HD, (h + 1) * HD)
            o_ref[:, cols] = (acc_sc[h] / l_sc[h]).astype(o_ref.dtype)


def flash(queries, local_stack, piece, bias, chosen, heads):
    span, width = queries.shape
    n_local = local_stack.shape[0]
    steps = n_local + chosen.shape[0]
    blocks = bias.shape[1]

    def local_map(kv):
        return lambda j, c: (jnp.minimum(j, n_local - 1), 0, kv)

    def pool_map(kv):
        return lambda j, c: (c[jnp.maximum(j - n_local, 0)], 0, kv)

    kv_block = (None, span, width)
    grid_spec = pltpu.PrefetchScalarGridSpec(
        num_scalar_prefetch=1,
        grid=(steps,),
        in_specs=[
            pl.BlockSpec((span, width), lambda j, c: (0, 0)),
            pl.BlockSpec(kv_block, local_map(0)),
            pl.BlockSpec(kv_block, local_map(1)),
            pl.BlockSpec(kv_block, pool_map(0)),
            pl.BlockSpec(kv_block, pool_map(1)),
            pl.BlockSpec((None, blocks, span), lambda j, c: (j, 0, 0)),
        ],
        out_specs=pl.BlockSpec((span, width), lambda j, c: (0, 0)),
        scratch_shapes=[
            pltpu.VMEM((heads, span, 1), jnp.float32),
            pltpu.VMEM((heads, span, 1), jnp.float32),
            pltpu.VMEM((heads, span, HD), jnp.float32),
        ],
    )
    kernel = lambda *refs: flash_kernel(*refs, heads=heads, n_local=n_local)
    return pl.pallas_call(
        kernel,
        grid_spec=grid_spec,
        out_shape=jax.ShapeDtypeStruct((span, width), jnp.bfloat16),
        compiler_params=pltpu.CompilerParams(dimension_semantics=("arbitrary",)),
        cost_estimate=pl.CostEstimate(
            flops=4 * steps * heads * span * span * HD,
            transcendentals=steps * heads * span * span,
            bytes_accessed=2 * steps * span * width * 2,
        ),
    )(chosen, queries, local_stack, local_stack, piece, piece, bias)


def fetch_out_weight(w_out, head, core):
    groups = lax.axis_size("head")
    columns = w_out.shape[1] // groups
    half = columns // 2
    mine = []
    for shift in range(groups):
        dest = (head + shift) % groups
        block = lax.dynamic_slice_in_dim(w_out, dest * columns + core * half, half, 1)
        if shift:
            block = lax.ppermute(block, "head", [(i, (i + shift) % groups) for i in range(groups)])
        mine.append(block)
    own_full = lax.dynamic_slice_in_dim(w_out, head * columns, columns, 1)
    return own_full, mine


def local(
    activations,
    mod_table,
    step_index,
    block_mask,
    cache_index,
    w_qkv,
    q_gain,
    k_gain,
    pool_kv,
    w_out,
):
    slot = lax.axis_index("slot")
    head = lax.axis_index("head")
    core = slot % 2
    groups = lax.axis_size("head")
    span = activations.shape[0]
    heads = q_gain.shape[0] // HD
    blocks_q = span // BLOCK
    cache_len = cache_index.shape[1]

    own_full, mine = fetch_out_weight(w_out, head, core)
    slots = lax.axis_size("slot")
    same_core = [pool_kv] + [from_behind(pool_kv, "slot", 2 * k) for k in range(1, slots // 2)]
    same_core = jnp.concatenate(same_core, axis=0)

    onehot = (jnp.arange(mod_table.shape[0], dtype=jnp.int32) == step_index[slot]).astype(
        jnp.float32
    )
    modulation = jnp.einsum("n,nkd->kd", onehot, mod_table.astype(jnp.float32))
    inputs = activations.astype(jnp.float32)
    normed = inputs * lax.rsqrt(jnp.mean(inputs * inputs, axis=-1, keepdims=True) + 1e-06)
    hidden = (normed * (1.0 + modulation[1][None, :]) + modulation[0][None, :]).astype(jnp.bfloat16)
    qkv = jnp.einsum("td,dkh->tkh", hidden, w_qkv, preferred_element_type=jnp.float32)
    queries = head_norm(qkv[:, 0], q_gain, heads).astype(jnp.bfloat16)
    queries, same_core = lax.optimization_barrier((queries, same_core))
    other_core = lax.ppermute(same_core, "slot", [(i, i ^ 1) for i in range(slots)])
    piece = jnp.concatenate([same_core, other_core], axis=0)
    keys = head_norm(qkv[:, 1], k_gain, heads).astype(jnp.bfloat16)
    values = qkv[:, 2].astype(jnp.bfloat16)
    local_kv = jnp.stack([keys.reshape(span, heads * HD), values], axis=1)
    own_mask = lax.dynamic_index_in_dim(block_mask, slot, 0, keepdims=False)
    own_cache = lax.dynamic_index_in_dim(cache_index, slot, 0, keepdims=False)
    sibling_slot = jnp.bitwise_xor(slot, 1)
    own_cache = jnp.where(
        own_cache % 2 == core,
        ((slot - own_cache) % slots) // 2,
        slots // 2 + ((sibling_slot - own_cache) % slots) // 2,
    ).astype(jnp.int32)
    before = from_behind(local_kv, "slot", 1)
    earlier = from_behind(local_kv, "slot", 2)
    width = heads * HD
    local_stack = jnp.stack([local_kv, before, earlier]).reshape(3, span, 2 * width)
    pool_flat = piece.reshape(piece.shape[0], span, 2 * width)
    visible = jnp.concatenate([jnp.ones((blocks_q, blocks_q), jnp.int32), own_mask], axis=1)
    visible = jnp.transpose(visible.reshape(blocks_q, 3 + cache_len, blocks_q), (1, 0, 2))
    visible = jnp.repeat(visible, BLOCK, axis=2)
    bias = jnp.where(visible > 0, 0.0, -1e30).astype(jnp.float32)
    local_stack, mine = lax.optimization_barrier((local_stack, mine))
    mixed = flash(queries.reshape(span, width), local_stack, pool_flat, bias, own_cache, heads)
    sibling = lax.ppermute(
        jnp.stack(mine[1:]), "slot", [(i, i ^ 1) for i in range(slots)]
    )

    received = [
        lax.ppermute(mixed, "head", [(i, (i + shift) % groups) for i in range(groups)])
        for shift in range(1, groups)
    ]
    columns = own_full.shape[1]
    half = columns // 2
    attn = jnp.dot(mixed, own_full, preferred_element_type=jnp.float32).astype(jnp.bfloat16).astype(jnp.float32)
    attn_mine = None
    attn_sib = None
    for shift in range(1, groups):
        group_o = received[shift - 1]
        part = jnp.dot(group_o, mine[shift], preferred_element_type=jnp.float32)
        part = part.astype(jnp.bfloat16).astype(jnp.float32)
        attn_mine = part if attn_mine is None else attn_mine + part
        part = jnp.dot(group_o, sibling[shift - 1], preferred_element_type=jnp.float32)
        part = part.astype(jnp.bfloat16).astype(jnp.float32)
        attn_sib = part if attn_sib is None else attn_sib + part
    other = jnp.concatenate([attn_mine, attn_sib], axis=1)
    swapped = jnp.concatenate([attn_sib, attn_mine], axis=1)
    attn = attn + jnp.where(core == 0, other, swapped)

    offset = head * columns
    input_cols = lax.dynamic_slice_in_dim(activations, offset, columns, 1).astype(jnp.float32)
    gate_cols = lax.dynamic_slice_in_dim(modulation[2], offset, columns, 0)
    return input_cols + gate_cols[None, :] * attn


def solution(mesh):
    placed = (
        P("slot", None),
        P(),
        P(),
        P(),
        P(),
        P(None, None, "head"),
        P("head"),
        P("head"),
        P("slot", None, None, "head"),
        P("head", None),
    )
    return jax.shard_map(
        local, mesh=mesh, in_specs=placed, out_specs=P("slot", "head"), check_vma=False
    )
```

```python
import jax
import jax.numpy as jnp
from jax import lax
from jax.sharding import PartitionSpec as P
from jax.experimental import pallas as pl
from jax.experimental.pallas import tpu as pltpu

HD = 128
BLOCK = 128


def from_behind(shard, axis, by):
    length = lax.axis_size(axis)
    return lax.ppermute(shard, axis, [(i, (i + by) % length) for i in range(length)])


def head_norm(values, gain, heads):
    shaped = values.reshape(values.shape[0], heads, HD)
    scaled = shaped * lax.rsqrt(jnp.mean(shaped * shaped, axis=-1, keepdims=True) + 1e-06)
    return scaled * gain.reshape(heads, HD)


def attend(state, queries, span_kv, visible_blocks):
    highest, totals, accum = state
    heads = queries.shape[1]
    span_keys = span_kv[:, 0].reshape(span_kv.shape[0], heads, HD)
    span_values = span_kv[:, 1].reshape(span_kv.shape[0], heads, HD)
    visible = jnp.repeat(jnp.repeat(visible_blocks, BLOCK, axis=0), BLOCK, axis=1) > 0
    scores = jnp.einsum("qhd,khd->hqk", queries, span_keys, preferred_element_type=jnp.float32) * (
        1.0 / HD**0.5
    )
    scores = jnp.where(visible[None], scores, -1e30)
    new_high = jnp.maximum(highest, jnp.max(scores, axis=-1))
    factor = jnp.exp(highest - new_high)
    weights = jnp.where(visible[None], jnp.exp(scores - new_high[..., None]), 0.0)
    totals = totals * factor + jnp.sum(weights, axis=-1)
    accum = accum * factor[..., None] + jnp.einsum(
        "hqk,khd->hqd",
        weights.astype(jnp.bfloat16),
        span_values,
        preferred_element_type=jnp.float32,
    )
    return (new_high, totals, accum)


def flash_kernel(chosen, q_ref, lk_ref, lv_ref, ak_ref, av_ref, bk_ref, bv_ref, bias_ref, o_ref, m_sc, l_sc, acc_sc, *, heads, n_local, half):
    step = pl.program_id(0)
    span = q_ref.shape[0]
    blocks = bias_ref.shape[0]

    @pl.when(step == 0)
    def _():
        m_sc[...] = jnp.full(m_sc.shape, -1e30, jnp.float32)
        l_sc[...] = jnp.zeros(l_sc.shape, jnp.float32)
        acc_sc[...] = jnp.zeros(acc_sc.shape, jnp.float32)

    def body(k_ref, v_ref):
        bias = bias_ref[...][:, None, :]
        for h in range(heads):
            cols = slice(h * HD, (h + 1) * HD)
            q = q_ref[:, cols]
            k = k_ref[:, cols]
            s = lax.dot_general(q, k, (((1,), (1,)), ((), ())), preferred_element_type=jnp.float32)
            s = (s * (1.0 / HD**0.5)).reshape(blocks, span // blocks, s.shape[1]) + bias
            s = s.reshape(span, -1)
            m_prev = m_sc[h]
            m_new = jnp.maximum(m_prev, jnp.max(s, axis=1, keepdims=True))
            factor = jnp.exp(m_prev - m_new)
            p = jnp.exp(s - m_new)
            l_sc[h] = l_sc[h] * factor + jnp.sum(p, axis=1, keepdims=True)
            acc_sc[h] = acc_sc[h] * factor + jnp.dot(
                p.astype(jnp.bfloat16), v_ref[:, cols], preferred_element_type=jnp.float32
            )
            m_sc[h] = m_new

    @pl.when(step < n_local)
    def _():
        body(lk_ref, lv_ref)

    pos = chosen[jnp.maximum(step - n_local, 0)]

    @pl.when((step >= n_local) & (pos < half))
    def _():
        body(ak_ref, av_ref)

    @pl.when((step >= n_local) & (pos >= half))
    def _():
        body(bk_ref, bv_ref)

    @pl.when(step == pl.num_programs(0) - 1)
    def _():
        for h in range(heads):
            cols = slice(h * HD, (h + 1) * HD)
            o_ref[:, cols] = (acc_sc[h] / l_sc[h]).astype(o_ref.dtype)


def flash(queries, local_stack, same_core, other_core, bias, chosen, heads):
    span, width = queries.shape
    n_local = local_stack.shape[0]
    half = same_core.shape[0]
    steps = n_local + chosen.shape[0]
    blocks = bias.shape[1]

    def local_map(kv):
        return lambda j, c: (jnp.minimum(j, n_local - 1), 0, kv)

    def pool_map(kv, upper):
        def index(j, c):
            pos = c[jnp.maximum(j - n_local, 0)]
            hit = (j >= n_local) & ((pos >= half) == upper)
            return (jnp.where(hit, pos - upper * half, 0), 0, kv)

        return index

    kv_block = (None, span, width)
    grid_spec = pltpu.PrefetchScalarGridSpec(
        num_scalar_prefetch=1,
        grid=(steps,),
        in_specs=[
            pl.BlockSpec((span, width), lambda j, c: (0, 0)),
            pl.BlockSpec(kv_block, local_map(0)),
            pl.BlockSpec(kv_block, local_map(1)),
            pl.BlockSpec(kv_block, pool_map(0, False)),
            pl.BlockSpec(kv_block, pool_map(1, False)),
            pl.BlockSpec(kv_block, pool_map(0, True)),
            pl.BlockSpec(kv_block, pool_map(1, True)),
            pl.BlockSpec((None, blocks, span), lambda j, c: (j, 0, 0)),
        ],
        out_specs=pl.BlockSpec((span, width), lambda j, c: (0, 0)),
        scratch_shapes=[
            pltpu.VMEM((heads, span, 1), jnp.float32),
            pltpu.VMEM((heads, span, 1), jnp.float32),
            pltpu.VMEM((heads, span, HD), jnp.float32),
        ],
    )
    kernel = lambda *refs: flash_kernel(*refs, heads=heads, n_local=n_local, half=half)
    return pl.pallas_call(
        kernel,
        grid_spec=grid_spec,
        out_shape=jax.ShapeDtypeStruct((span, width), jnp.bfloat16),
        compiler_params=pltpu.CompilerParams(dimension_semantics=("arbitrary",)),
        cost_estimate=pl.CostEstimate(
            flops=4 * steps * heads * span * span * HD,
            transcendentals=steps * heads * span * span,
            bytes_accessed=2 * steps * span * width * 2,
        ),
    )(chosen, queries, local_stack, local_stack, same_core, same_core, other_core, other_core, bias)


def fetch_out_weight(w_out, head, core):
    groups = lax.axis_size("head")
    columns = w_out.shape[1] // groups
    half = columns // 2
    mine = []
    for shift in range(groups):
        dest = (head + shift) % groups
        block = lax.dynamic_slice_in_dim(w_out, dest * columns + core * half, half, 1)
        if shift:
            block = lax.ppermute(block, "head", [(i, (i + shift) % groups) for i in range(groups)])
        mine.append(block)
    own_full = lax.dynamic_slice_in_dim(w_out, head * columns, columns, 1)
    return own_full, mine


def local(
    activations,
    mod_table,
    step_index,
    block_mask,
    cache_index,
    w_qkv,
    q_gain,
    k_gain,
    pool_kv,
    w_out,
):
    slot = lax.axis_index("slot")
    head = lax.axis_index("head")
    core = slot % 2
    groups = lax.axis_size("head")
    span = activations.shape[0]
    heads = q_gain.shape[0] // HD
    blocks_q = span // BLOCK
    cache_len = cache_index.shape[1]

    own_full, mine = fetch_out_weight(w_out, head, core)
    slots = lax.axis_size("slot")
    pool_flat = pool_kv.reshape(1, pool_kv.shape[1], -1)
    same_core = [pool_flat] + [from_behind(pool_flat, "slot", 2 * k) for k in range(1, slots // 2)]
    same_core = jnp.concatenate(same_core, axis=0)

    onehot = (jnp.arange(mod_table.shape[0], dtype=jnp.int32) == step_index[slot]).astype(
        jnp.float32
    )
    modulation = jnp.einsum("n,nkd->kd", onehot, mod_table.astype(jnp.float32))
    inputs = activations.astype(jnp.float32)
    normed = inputs * lax.rsqrt(jnp.mean(inputs * inputs, axis=-1, keepdims=True) + 1e-06)
    hidden = (normed * (1.0 + modulation[1][None, :]) + modulation[0][None, :]).astype(jnp.bfloat16)
    qkv = jnp.einsum("td,dkh->tkh", hidden, w_qkv, preferred_element_type=jnp.float32)
    queries = head_norm(qkv[:, 0], q_gain, heads).astype(jnp.bfloat16)
    queries, same_core = lax.optimization_barrier((queries, same_core))
    other_core = lax.ppermute(same_core, "slot", [(i, i ^ 1) for i in range(slots)])
    keys = head_norm(qkv[:, 1], k_gain, heads).astype(jnp.bfloat16)
    values = qkv[:, 2].astype(jnp.bfloat16)
    local_kv = jnp.concatenate([keys.reshape(span, heads * HD), values], axis=1)
    own_mask = lax.dynamic_index_in_dim(block_mask, slot, 0, keepdims=False)
    own_cache = lax.dynamic_index_in_dim(cache_index, slot, 0, keepdims=False)
    sibling_slot = jnp.bitwise_xor(slot, 1)
    own_cache = jnp.where(
        own_cache % 2 == core,
        ((slot - own_cache) % slots) // 2,
        slots // 2 + ((sibling_slot - own_cache) % slots) // 2,
    ).astype(jnp.int32)
    before = from_behind(local_kv, "slot", 1)
    earlier = from_behind(local_kv, "slot", 2)
    width = heads * HD
    local_stack = jnp.stack([local_kv, before, earlier]).reshape(3, span, 2 * width)
    visible = jnp.concatenate([jnp.ones((blocks_q, blocks_q), jnp.int32), own_mask], axis=1)
    visible = jnp.transpose(visible.reshape(blocks_q, 3 + cache_len, blocks_q), (1, 0, 2))
    visible = jnp.repeat(visible, BLOCK, axis=2)
    bias = jnp.where(visible > 0, 0.0, -1e30).astype(jnp.float32)
    local_stack, mine = lax.optimization_barrier((local_stack, mine))
    mixed = flash(queries.reshape(span, width), local_stack, same_core, other_core, bias, own_cache, heads)
    sibling = lax.ppermute(
        jnp.stack(mine[1:]), "slot", [(i, i ^ 1) for i in range(slots)]
    )

    received = [
        lax.ppermute(mixed, "head", [(i, (i + shift) % groups) for i in range(groups)])
        for shift in range(1, groups)
    ]
    columns = own_full.shape[1]
    half = columns // 2
    attn = jnp.dot(mixed, own_full, preferred_element_type=jnp.float32).astype(jnp.bfloat16).astype(jnp.float32)
    attn_mine = None
    attn_sib = None
    for shift in range(1, groups):
        group_o = received[shift - 1]
        part = jnp.dot(group_o, mine[shift], preferred_element_type=jnp.float32)
        part = part.astype(jnp.bfloat16).astype(jnp.float32)
        attn_mine = part if attn_mine is None else attn_mine + part
        part = jnp.dot(group_o, sibling[shift - 1], preferred_element_type=jnp.float32)
        part = part.astype(jnp.bfloat16).astype(jnp.float32)
        attn_sib = part if attn_sib is None else attn_sib + part
    other = jnp.concatenate([attn_mine, attn_sib], axis=1)
    swapped = jnp.concatenate([attn_sib, attn_mine], axis=1)
    attn = attn + jnp.where(core == 0, other, swapped)

    offset = head * columns
    input_cols = lax.dynamic_slice_in_dim(activations, offset, columns, 1).astype(jnp.float32)
    gate_cols = lax.dynamic_slice_in_dim(modulation[2], offset, columns, 0)
    return input_cols + gate_cols[None, :] * attn


def solution(mesh):
    placed = (
        P("slot", None),
        P(),
        P(),
        P(),
        P(),
        P(None, None, "head"),
        P("head"),
        P("head"),
        P("slot", None, None, "head"),
        P("head", None),
    )
    return jax.shard_map(
        local, mesh=mesh, in_specs=placed, out_specs=P("slot", "head"), check_vma=False
    )
```

```python
import jax
import jax.numpy as jnp
from jax import lax
from jax.sharding import PartitionSpec as P
from jax.experimental import pallas as pl
from jax.experimental.pallas import tpu as pltpu

HD = 128
BLOCK = 128


def from_behind(shard, axis, by):
    length = lax.axis_size(axis)
    return lax.ppermute(shard, axis, [(i, (i + by) % length) for i in range(length)])


def head_norm(values, gain, heads):
    shaped = values.reshape(values.shape[0], heads, HD)
    scaled = shaped * lax.rsqrt(jnp.mean(shaped * shaped, axis=-1, keepdims=True) + 1e-06)
    return scaled * gain.reshape(heads, HD)


def attend(state, queries, span_kv, visible_blocks):
    highest, totals, accum = state
    heads = queries.shape[1]
    span_keys = span_kv[:, 0].reshape(span_kv.shape[0], heads, HD)
    span_values = span_kv[:, 1].reshape(span_kv.shape[0], heads, HD)
    visible = jnp.repeat(jnp.repeat(visible_blocks, BLOCK, axis=0), BLOCK, axis=1) > 0
    scores = jnp.einsum("qhd,khd->hqk", queries, span_keys, preferred_element_type=jnp.float32) * (
        1.0 / HD**0.5
    )
    scores = jnp.where(visible[None], scores, -1e30)
    new_high = jnp.maximum(highest, jnp.max(scores, axis=-1))
    factor = jnp.exp(highest - new_high)
    weights = jnp.where(visible[None], jnp.exp(scores - new_high[..., None]), 0.0)
    totals = totals * factor + jnp.sum(weights, axis=-1)
    accum = accum * factor[..., None] + jnp.einsum(
        "hqk,khd->hqd",
        weights.astype(jnp.bfloat16),
        span_values,
        preferred_element_type=jnp.float32,
    )
    return (new_high, totals, accum)


def flash_kernel(chosen, q_ref, lk_ref, lv_ref, ak_ref, av_ref, bk_ref, bv_ref, bias_ref, o_ref, m_sc, l_sc, acc_sc, *, heads, n_local, half):
    step = pl.program_id(0)
    span = q_ref.shape[0]
    blocks = bias_ref.shape[0]

    @pl.when(step == 0)
    def _():
        m_sc[...] = jnp.full(m_sc.shape, -1e30, jnp.float32)
        l_sc[...] = jnp.zeros(l_sc.shape, jnp.float32)
        acc_sc[...] = jnp.zeros(acc_sc.shape, jnp.float32)

    def body(k_ref, v_ref):
        bias = bias_ref[...][:, None, :]
        for h in range(heads):
            cols = slice(h * HD, (h + 1) * HD)
            q = q_ref[:, cols]
            k = k_ref[:, cols]
            s = lax.dot_general(q, k, (((1,), (1,)), ((), ())), preferred_element_type=jnp.float32)
            s = (s * (1.0 / HD**0.5)).reshape(blocks, span // blocks, s.shape[1]) + bias
            s = s.reshape(span, -1)
            m_prev = m_sc[h]
            m_new = jnp.maximum(m_prev, jnp.max(s, axis=1, keepdims=True))
            factor = jnp.exp(m_prev - m_new)
            p = jnp.exp(s - m_new)
            l_sc[h] = l_sc[h] * factor + jnp.sum(p, axis=1, keepdims=True)
            acc_sc[h] = acc_sc[h] * factor + jnp.dot(
                p.astype(jnp.bfloat16), v_ref[:, cols], preferred_element_type=jnp.float32
            )
            m_sc[h] = m_new

    @pl.when(step < n_local)
    def _():
        body(lk_ref, lv_ref)

    pos = chosen[jnp.maximum(step - n_local, 0)]

    @pl.when((step >= n_local) & (pos < half))
    def _():
        body(ak_ref, av_ref)

    @pl.when((step >= n_local) & (pos >= half))
    def _():
        body(bk_ref, bv_ref)

    @pl.when(step == pl.num_programs(0) - 1)
    def _():
        for h in range(heads):
            cols = slice(h * HD, (h + 1) * HD)
            o_ref[:, cols] = (acc_sc[h] / l_sc[h]).astype(o_ref.dtype)


def flash(queries, local_stack, same_core, other_core, bias, chosen, heads):
    span, width = queries.shape
    n_local = local_stack.shape[0]
    half = same_core.shape[0]
    steps = n_local + chosen.shape[0]
    blocks = bias.shape[1]

    def local_map(kv):
        return lambda j, c: (jnp.minimum(j, n_local - 1), 0, kv)

    def pool_map(kv, upper):
        def index(j, c):
            pos = c[jnp.maximum(j - n_local, 0)]
            hit = (j >= n_local) & ((pos >= half) == upper)
            return (jnp.where(hit, pos - upper * half, 0), 0, kv)

        return index

    kv_block = (None, span, width)
    grid_spec = pltpu.PrefetchScalarGridSpec(
        num_scalar_prefetch=1,
        grid=(steps,),
        in_specs=[
            pl.BlockSpec((span, width), lambda j, c: (0, 0)),
            pl.BlockSpec(kv_block, local_map(0)),
            pl.BlockSpec(kv_block, local_map(1)),
            pl.BlockSpec(kv_block, pool_map(0, False)),
            pl.BlockSpec(kv_block, pool_map(1, False)),
            pl.BlockSpec(kv_block, pool_map(0, True)),
            pl.BlockSpec(kv_block, pool_map(1, True)),
            pl.BlockSpec((None, blocks, span), lambda j, c: (j, 0, 0)),
        ],
        out_specs=pl.BlockSpec((span, width), lambda j, c: (0, 0)),
        scratch_shapes=[
            pltpu.VMEM((heads, span, 1), jnp.float32),
            pltpu.VMEM((heads, span, 1), jnp.float32),
            pltpu.VMEM((heads, span, HD), jnp.float32),
        ],
    )
    kernel = lambda *refs: flash_kernel(*refs, heads=heads, n_local=n_local, half=half)
    return pl.pallas_call(
        kernel,
        grid_spec=grid_spec,
        out_shape=jax.ShapeDtypeStruct((span, width), jnp.bfloat16),
        compiler_params=pltpu.CompilerParams(dimension_semantics=("arbitrary",)),
        cost_estimate=pl.CostEstimate(
            flops=4 * steps * heads * span * span * HD,
            transcendentals=steps * heads * span * span,
            bytes_accessed=2 * steps * span * width * 2,
        ),
    )(chosen, queries, local_stack, local_stack, same_core, same_core, other_core, other_core, bias)


def fetch_out_weight(w_out, head, core):
    groups = lax.axis_size("head")
    columns = w_out.shape[1] // groups
    half = columns // 2
    mine = []
    for shift in range(groups):
        dest = (head + shift) % groups
        block = lax.dynamic_slice_in_dim(w_out, dest * columns + core * half, half, 1)
        if shift:
            block = lax.ppermute(block, "head", [(i, (i + shift) % groups) for i in range(groups)])
        mine.append(block)
    own_full = lax.dynamic_slice_in_dim(w_out, head * columns, columns, 1)
    return own_full, mine


def local(
    activations,
    mod_table,
    step_index,
    block_mask,
    cache_index,
    w_qkv,
    q_gain,
    k_gain,
    pool_kv,
    w_out,
):
    slot = lax.axis_index("slot")
    head = lax.axis_index("head")
    core = slot % 2
    groups = lax.axis_size("head")
    span = activations.shape[0]
    heads = q_gain.shape[0] // HD
    blocks_q = span // BLOCK
    cache_len = cache_index.shape[1]

    own_full, mine = fetch_out_weight(w_out, head, core)
    slots = lax.axis_size("slot")
    pool_flat = pool_kv.reshape(1, pool_kv.shape[1], -1)
    same_core = [pool_flat] + [from_behind(pool_flat, "slot", 2 * k) for k in range(1, slots // 2)]
    same_core = jnp.concatenate(same_core, axis=0)

    onehot = (jnp.arange(mod_table.shape[0], dtype=jnp.int32) == step_index[slot]).astype(
        jnp.float32
    )
    modulation = jnp.einsum("n,nkd->kd", onehot, mod_table.astype(jnp.float32))
    inputs = activations.astype(jnp.float32)
    normed = inputs * lax.rsqrt(jnp.mean(inputs * inputs, axis=-1, keepdims=True) + 1e-06)
    hidden = (normed * (1.0 + modulation[1][None, :]) + modulation[0][None, :]).astype(jnp.bfloat16)
    qkv = jnp.einsum("td,dkh->tkh", hidden, w_qkv, preferred_element_type=jnp.float32)
    qkv, same_core, mine = lax.optimization_barrier((qkv, same_core, mine))
    queries = head_norm(qkv[:, 0], q_gain, heads).astype(jnp.bfloat16)
    other_core = lax.ppermute(same_core, "slot", [(i, i ^ 1) for i in range(slots)])
    keys = head_norm(qkv[:, 1], k_gain, heads).astype(jnp.bfloat16)
    values = qkv[:, 2].astype(jnp.bfloat16)
    local_kv = jnp.concatenate([keys.reshape(span, heads * HD), values], axis=1)
    own_mask = lax.dynamic_index_in_dim(block_mask, slot, 0, keepdims=False)
    own_cache = lax.dynamic_index_in_dim(cache_index, slot, 0, keepdims=False)
    sibling_slot = jnp.bitwise_xor(slot, 1)
    own_cache = jnp.where(
        own_cache % 2 == core,
        ((slot - own_cache) % slots) // 2,
        slots // 2 + ((sibling_slot - own_cache) % slots) // 2,
    ).astype(jnp.int32)
    before = from_behind(local_kv, "slot", 1)
    earlier = from_behind(local_kv, "slot", 2)
    width = heads * HD
    local_stack = jnp.stack([local_kv, before, earlier]).reshape(3, span, 2 * width)
    visible = jnp.concatenate([jnp.ones((blocks_q, blocks_q), jnp.int32), own_mask], axis=1)
    visible = jnp.transpose(visible.reshape(blocks_q, 3 + cache_len, blocks_q), (1, 0, 2))
    visible = jnp.repeat(visible, BLOCK, axis=2)
    bias = jnp.where(visible > 0, 0.0, -1e30).astype(jnp.float32)
    mixed = flash(queries.reshape(span, width), local_stack, same_core, other_core, bias, own_cache, heads)
    sibling = lax.ppermute(
        jnp.stack(mine[1:]), "slot", [(i, i ^ 1) for i in range(slots)]
    )

    received = [
        lax.ppermute(mixed, "head", [(i, (i + shift) % groups) for i in range(groups)])
        for shift in range(1, groups)
    ]
    columns = own_full.shape[1]
    half = columns // 2
    attn = jnp.dot(mixed, own_full, preferred_element_type=jnp.float32).astype(jnp.bfloat16).astype(jnp.float32)
    attn_mine = None
    attn_sib = None
    for shift in range(1, groups):
        group_o = received[shift - 1]
        part = jnp.dot(group_o, mine[shift], preferred_element_type=jnp.float32)
        part = part.astype(jnp.bfloat16).astype(jnp.float32)
        attn_mine = part if attn_mine is None else attn_mine + part
        part = jnp.dot(group_o, sibling[shift - 1], preferred_element_type=jnp.float32)
        part = part.astype(jnp.bfloat16).astype(jnp.float32)
        attn_sib = part if attn_sib is None else attn_sib + part
    other = jnp.concatenate([attn_mine, attn_sib], axis=1)
    swapped = jnp.concatenate([attn_sib, attn_mine], axis=1)
    attn = attn + jnp.where(core == 0, other, swapped)

    offset = head * columns
    input_cols = lax.dynamic_slice_in_dim(activations, offset, columns, 1).astype(jnp.float32)
    gate_cols = lax.dynamic_slice_in_dim(modulation[2], offset, columns, 0)
    return input_cols + gate_cols[None, :] * attn


def solution(mesh):
    placed = (
        P("slot", None),
        P(),
        P(),
        P(),
        P(),
        P(None, None, "head"),
        P("head"),
        P("head"),
        P("slot", None, None, "head"),
        P("head", None),
    )
    return jax.shard_map(
        local, mesh=mesh, in_specs=placed, out_specs=P("slot", "head"), check_vma=False
    )
```

```python
import jax
import jax.numpy as jnp
from jax import lax
from jax.sharding import PartitionSpec as P
from jax.experimental import pallas as pl
from jax.experimental.pallas import tpu as pltpu

HD = 128
BLOCK = 128


def from_behind(shard, axis, by):
    length = lax.axis_size(axis)
    return lax.ppermute(shard, axis, [(i, (i + by) % length) for i in range(length)])


def head_norm(values, gain, heads):
    shaped = values.reshape(values.shape[0], heads, HD)
    scaled = shaped * lax.rsqrt(jnp.mean(shaped * shaped, axis=-1, keepdims=True) + 1e-06)
    return scaled * gain.reshape(heads, HD)


def attend(state, queries, span_kv, visible_blocks):
    highest, totals, accum = state
    heads = queries.shape[1]
    span_keys = span_kv[:, 0].reshape(span_kv.shape[0], heads, HD)
    span_values = span_kv[:, 1].reshape(span_kv.shape[0], heads, HD)
    visible = jnp.repeat(jnp.repeat(visible_blocks, BLOCK, axis=0), BLOCK, axis=1) > 0
    scores = jnp.einsum("qhd,khd->hqk", queries, span_keys, preferred_element_type=jnp.float32) * (
        1.0 / HD**0.5
    )
    scores = jnp.where(visible[None], scores, -1e30)
    new_high = jnp.maximum(highest, jnp.max(scores, axis=-1))
    factor = jnp.exp(highest - new_high)
    weights = jnp.where(visible[None], jnp.exp(scores - new_high[..., None]), 0.0)
    totals = totals * factor + jnp.sum(weights, axis=-1)
    accum = accum * factor[..., None] + jnp.einsum(
        "hqk,khd->hqd",
        weights.astype(jnp.bfloat16),
        span_values,
        preferred_element_type=jnp.float32,
    )
    return (new_high, totals, accum)


def flash_kernel(chosen, q_ref, lk_ref, lv_ref, ak_ref, av_ref, bk_ref, bv_ref, bias_ref, o_ref, m_sc, l_sc, acc_sc, *, heads, n_local, half):
    step = pl.program_id(0)
    span = q_ref.shape[0]
    blocks = bias_ref.shape[0]

    @pl.when(step == 0)
    def _():
        m_sc[...] = jnp.full(m_sc.shape, -1e30, jnp.float32)
        l_sc[...] = jnp.zeros(l_sc.shape, jnp.float32)
        acc_sc[...] = jnp.zeros(acc_sc.shape, jnp.float32)

    def body(k_ref, v_ref):
        bias = bias_ref[...][:, None, :]
        for h in range(heads):
            cols = slice(h * HD, (h + 1) * HD)
            q = q_ref[:, cols]
            k = k_ref[:, cols]
            s = lax.dot_general(q, k, (((1,), (1,)), ((), ())), preferred_element_type=jnp.float32)
            s = (s * (1.0 / HD**0.5)).reshape(blocks, span // blocks, s.shape[1]) + bias
            s = s.reshape(span, -1)
            m_prev = m_sc[h]
            m_new = jnp.maximum(m_prev, jnp.max(s, axis=1, keepdims=True))
            factor = jnp.exp(m_prev - m_new)
            p = jnp.exp(s - m_new)
            l_sc[h] = l_sc[h] * factor + jnp.sum(p, axis=1, keepdims=True)
            acc_sc[h] = acc_sc[h] * factor + jnp.dot(
                p.astype(jnp.bfloat16), v_ref[:, cols], preferred_element_type=jnp.float32
            )
            m_sc[h] = m_new

    @pl.when(step < n_local)
    def _():
        body(lk_ref, lv_ref)

    pos = chosen[jnp.maximum(step - n_local, 0)]

    @pl.when((step >= n_local) & (pos < half))
    def _():
        body(ak_ref, av_ref)

    @pl.when((step >= n_local) & (pos >= half))
    def _():
        body(bk_ref, bv_ref)

    @pl.when(step == pl.num_programs(0) - 1)
    def _():
        for h in range(heads):
            cols = slice(h * HD, (h + 1) * HD)
            o_ref[:, cols] = (acc_sc[h] / l_sc[h]).astype(o_ref.dtype)


def flash(queries, local_stack, same_core, other_core, bias, chosen, heads):
    span, width = queries.shape
    n_local = local_stack.shape[0]
    half = same_core.shape[0]
    steps = n_local + chosen.shape[0]
    blocks = bias.shape[1]

    def local_map(kv):
        return lambda j, c: (jnp.minimum(j, n_local - 1), 0, kv)

    def pool_map(kv, upper):
        def index(j, c):
            pos = c[jnp.maximum(j - n_local, 0)]
            hit = (j >= n_local) & ((pos >= half) == upper)
            return (jnp.where(hit, pos - upper * half, 0), 0, kv)

        return index

    keys_len = local_stack.shape[1]
    kv_block = (None, keys_len, width)
    grid_spec = pltpu.PrefetchScalarGridSpec(
        num_scalar_prefetch=1,
        grid=(steps,),
        in_specs=[
            pl.BlockSpec((span, width), lambda j, c: (0, 0)),
            pl.BlockSpec(kv_block, local_map(0)),
            pl.BlockSpec(kv_block, local_map(1)),
            pl.BlockSpec(kv_block, pool_map(0, False)),
            pl.BlockSpec(kv_block, pool_map(1, False)),
            pl.BlockSpec(kv_block, pool_map(0, True)),
            pl.BlockSpec(kv_block, pool_map(1, True)),
            pl.BlockSpec((None, blocks, keys_len), lambda j, c: (j, 0, 0)),
        ],
        out_specs=pl.BlockSpec((span, width), lambda j, c: (0, 0)),
        scratch_shapes=[
            pltpu.VMEM((heads, span, 1), jnp.float32),
            pltpu.VMEM((heads, span, 1), jnp.float32),
            pltpu.VMEM((heads, span, HD), jnp.float32),
        ],
    )
    kernel = lambda *refs: flash_kernel(*refs, heads=heads, n_local=n_local, half=half)
    return pl.pallas_call(
        kernel,
        grid_spec=grid_spec,
        out_shape=jax.ShapeDtypeStruct((span, width), jnp.bfloat16),
        compiler_params=pltpu.CompilerParams(dimension_semantics=("arbitrary",)),
        cost_estimate=pl.CostEstimate(
            flops=4 * steps * heads * span * span * HD,
            transcendentals=steps * heads * span * span,
            bytes_accessed=2 * steps * span * width * 2,
        ),
    )(chosen, queries, local_stack, local_stack, same_core, same_core, other_core, other_core, bias)


def fetch_out_weight(w_out, head, core):
    groups = lax.axis_size("head")
    columns = w_out.shape[1] // groups
    half = columns // 2
    mine = []
    for shift in range(groups):
        dest = (head + shift) % groups
        block = lax.dynamic_slice_in_dim(w_out, dest * columns + core * half, half, 1)
        if shift:
            block = lax.ppermute(block, "head", [(i, (i + shift) % groups) for i in range(groups)])
        mine.append(block)
    own_full = lax.dynamic_slice_in_dim(w_out, head * columns, columns, 1)
    return own_full, mine


def local(
    activations,
    mod_table,
    step_index,
    block_mask,
    cache_index,
    w_qkv,
    q_gain,
    k_gain,
    pool_kv,
    w_out,
):
    slot = lax.axis_index("slot")
    head = lax.axis_index("head")
    core = slot % 2
    groups = lax.axis_size("head")
    span = activations.shape[0]
    heads = q_gain.shape[0] // HD
    blocks_q = span // BLOCK
    cache_len = cache_index.shape[1]

    own_full, mine = fetch_out_weight(w_out, head, core)
    slots = lax.axis_size("slot")
    pool_flat = pool_kv.reshape(1, pool_kv.shape[1], -1)
    same_core = [pool_flat] + [from_behind(pool_flat, "slot", 2 * k) for k in range(1, slots // 2)]
    same_core = jnp.concatenate(same_core, axis=0)

    onehot = (jnp.arange(mod_table.shape[0], dtype=jnp.int32) == step_index[slot]).astype(
        jnp.float32
    )
    modulation = jnp.einsum("n,nkd->kd", onehot, mod_table.astype(jnp.float32))
    inputs = activations.astype(jnp.float32)
    normed = inputs * lax.rsqrt(jnp.mean(inputs * inputs, axis=-1, keepdims=True) + 1e-06)
    hidden = (normed * (1.0 + modulation[1][None, :]) + modulation[0][None, :]).astype(jnp.bfloat16)
    qkv = jnp.einsum("td,dkh->tkh", hidden, w_qkv, preferred_element_type=jnp.float32)
    queries = head_norm(qkv[:, 0], q_gain, heads).astype(jnp.bfloat16)
    keys = head_norm(qkv[:, 1], k_gain, heads).astype(jnp.bfloat16)
    values = qkv[:, 2].astype(jnp.bfloat16)
    local_kv = jnp.concatenate([keys.reshape(span, heads * HD), values], axis=1)
    queries, local_kv, same_core, mine = lax.optimization_barrier((queries, local_kv, same_core, mine))
    other_core = lax.ppermute(same_core, "slot", [(i, i ^ 1) for i in range(slots)])
    own_mask = lax.dynamic_index_in_dim(block_mask, slot, 0, keepdims=False)
    own_cache = lax.dynamic_index_in_dim(cache_index, slot, 0, keepdims=False)
    sibling_slot = jnp.bitwise_xor(slot, 1)
    own_cache = jnp.where(
        own_cache % 2 == core,
        ((slot - own_cache) % slots) // 2,
        slots // 2 + ((sibling_slot - own_cache) % slots) // 2,
    ).astype(jnp.int32)
    before = from_behind(local_kv, "slot", 1)
    earlier = from_behind(local_kv, "slot", 2)
    width = heads * HD
    local_stack = jnp.stack([local_kv, before, earlier]).reshape(3, span, 2 * width)
    visible = jnp.concatenate([jnp.ones((blocks_q, blocks_q), jnp.int32), own_mask], axis=1)
    visible = jnp.transpose(visible.reshape(blocks_q, 3 + cache_len, blocks_q), (1, 0, 2))
    visible = jnp.repeat(visible, BLOCK, axis=2)
    bias = jnp.where(visible > 0, 0.0, -1e30).astype(jnp.float32)
    rows = span // 2
    parts = rows // BLOCK
    queries = queries.reshape(span, width)
    mixed_parts = [
        flash(queries[p * rows : (p + 1) * rows], local_stack, same_core, other_core,
              bias[:, p * parts : (p + 1) * parts], own_cache, heads)
        for p in range(2)
    ]
    sibling = lax.ppermute(
        jnp.stack(mine[1:]), "slot", [(i, i ^ 1) for i in range(slots)]
    )

    received = [
        jnp.concatenate([
            lax.ppermute(part, "head", [(i, (i + shift) % groups) for i in range(groups)])
            for part in mixed_parts
        ], axis=0)
        for shift in range(1, groups)
    ]
    mixed = jnp.concatenate(mixed_parts, axis=0)
    columns = own_full.shape[1]
    half = columns // 2
    attn = jnp.dot(mixed, own_full, preferred_element_type=jnp.float32).astype(jnp.bfloat16).astype(jnp.float32)
    attn_mine = None
    attn_sib = None
    for shift in range(1, groups):
        group_o = received[shift - 1]
        part = jnp.dot(group_o, mine[shift], preferred_element_type=jnp.float32)
        part = part.astype(jnp.bfloat16).astype(jnp.float32)
        attn_mine = part if attn_mine is None else attn_mine + part
        part = jnp.dot(group_o, sibling[shift - 1], preferred_element_type=jnp.float32)
        part = part.astype(jnp.bfloat16).astype(jnp.float32)
        attn_sib = part if attn_sib is None else attn_sib + part
    other = jnp.concatenate([attn_mine, attn_sib], axis=1)
    swapped = jnp.concatenate([attn_sib, attn_mine], axis=1)
    attn = attn + jnp.where(core == 0, other, swapped)

    offset = head * columns
    input_cols = lax.dynamic_slice_in_dim(activations, offset, columns, 1).astype(jnp.float32)
    gate_cols = lax.dynamic_slice_in_dim(modulation[2], offset, columns, 0)
    return input_cols + gate_cols[None, :] * attn


def solution(mesh):
    placed = (
        P("slot", None),
        P(),
        P(),
        P(),
        P(),
        P(None, None, "head"),
        P("head"),
        P("head"),
        P("slot", None, None, "head"),
        P("head", None),
    )
    return jax.shard_map(
        local, mesh=mesh, in_specs=placed, out_specs=P("slot", "head"), check_vma=False
    )
```

```python
import jax
import jax.numpy as jnp
from jax import lax
from jax.sharding import PartitionSpec as P
from jax.experimental import pallas as pl
from jax.experimental.pallas import tpu as pltpu

HD = 128
BLOCK = 128


def from_behind(shard, axis, by):
    length = lax.axis_size(axis)
    return lax.ppermute(shard, axis, [(i, (i + by) % length) for i in range(length)])


def head_norm(values, gain, heads):
    shaped = values.reshape(values.shape[0], heads, HD)
    scaled = shaped * lax.rsqrt(jnp.mean(shaped * shaped, axis=-1, keepdims=True) + 1e-06)
    return scaled * gain.reshape(heads, HD)


def attend(state, queries, span_kv, visible_blocks):
    highest, totals, accum = state
    heads = queries.shape[1]
    span_keys = span_kv[:, 0].reshape(span_kv.shape[0], heads, HD)
    span_values = span_kv[:, 1].reshape(span_kv.shape[0], heads, HD)
    visible = jnp.repeat(jnp.repeat(visible_blocks, BLOCK, axis=0), BLOCK, axis=1) > 0
    scores = jnp.einsum("qhd,khd->hqk", queries, span_keys, preferred_element_type=jnp.float32) * (
        1.0 / HD**0.5
    )
    scores = jnp.where(visible[None], scores, -1e30)
    new_high = jnp.maximum(highest, jnp.max(scores, axis=-1))
    factor = jnp.exp(highest - new_high)
    weights = jnp.where(visible[None], jnp.exp(scores - new_high[..., None]), 0.0)
    totals = totals * factor + jnp.sum(weights, axis=-1)
    accum = accum * factor[..., None] + jnp.einsum(
        "hqk,khd->hqd",
        weights.astype(jnp.bfloat16),
        span_values,
        preferred_element_type=jnp.float32,
    )
    return (new_high, totals, accum)


def flash_kernel(chosen, q_ref, lk_ref, lv_ref, ak_ref, av_ref, bk_ref, bv_ref, bias_ref, o_ref, m_sc, l_sc, acc_sc, *, heads, n_local, half):
    step = pl.program_id(0)
    span = q_ref.shape[0]
    blocks = bias_ref.shape[0]

    @pl.when(step == 0)
    def _():
        m_sc[...] = jnp.full(m_sc.shape, -1e30, jnp.float32)
        l_sc[...] = jnp.zeros(l_sc.shape, jnp.float32)
        acc_sc[...] = jnp.zeros(acc_sc.shape, jnp.float32)

    def body(k_ref, v_ref):
        bias = bias_ref[...][:, None, :]
        for h in range(heads):
            cols = slice(h * HD, (h + 1) * HD)
            q = q_ref[:, cols]
            k = k_ref[:, cols]
            s = lax.dot_general(q, k, (((1,), (1,)), ((), ())), preferred_element_type=jnp.float32)
            s = (s * (1.0 / HD**0.5)).reshape(blocks, span // blocks, s.shape[1]) + bias
            s = s.reshape(span, -1)
            m_prev = m_sc[h]
            m_new = jnp.maximum(m_prev, jnp.max(s, axis=1, keepdims=True))
            factor = jnp.exp(m_prev - m_new)
            p = jnp.exp(s - m_new)
            l_sc[h] = l_sc[h] * factor + jnp.sum(p, axis=1, keepdims=True)
            acc_sc[h] = acc_sc[h] * factor + jnp.dot(
                p.astype(jnp.bfloat16), v_ref[:, cols], preferred_element_type=jnp.float32
            )
            m_sc[h] = m_new

    @pl.when(step < n_local)
    def _():
        body(lk_ref, lv_ref)

    pos = chosen[jnp.maximum(step - n_local, 0)]

    @pl.when((step >= n_local) & (pos < half))
    def _():
        body(ak_ref, av_ref)

    @pl.when((step >= n_local) & (pos >= half))
    def _():
        body(bk_ref, bv_ref)

    @pl.when(step == pl.num_programs(0) - 1)
    def _():
        for h in range(heads):
            cols = slice(h * HD, (h + 1) * HD)
            o_ref[:, cols] = (acc_sc[h] / l_sc[h]).astype(o_ref.dtype)


def flash(queries, local_stack, same_core, other_core, bias, chosen, heads):
    span, width = queries.shape
    n_local = local_stack.shape[0]
    half = same_core.shape[0]
    steps = n_local + chosen.shape[0]
    blocks = bias.shape[1]

    def local_map(kv):
        return lambda j, c: (jnp.minimum(j, n_local - 1), 0, kv)

    def pool_map(kv, upper):
        def index(j, c):
            pos = c[jnp.maximum(j - n_local, 0)]
            hit = (j >= n_local) & ((pos >= half) == upper)
            return (jnp.where(hit, pos - upper * half, 0), 0, kv)

        return index

    keys_len = local_stack.shape[1]
    kv_block = (None, keys_len, width)
    grid_spec = pltpu.PrefetchScalarGridSpec(
        num_scalar_prefetch=1,
        grid=(steps,),
        in_specs=[
            pl.BlockSpec((span, width), lambda j, c: (0, 0)),
            pl.BlockSpec(kv_block, local_map(0)),
            pl.BlockSpec(kv_block, local_map(1)),
            pl.BlockSpec(kv_block, pool_map(0, False)),
            pl.BlockSpec(kv_block, pool_map(1, False)),
            pl.BlockSpec(kv_block, pool_map(0, True)),
            pl.BlockSpec(kv_block, pool_map(1, True)),
            pl.BlockSpec((None, blocks, keys_len), lambda j, c: (j, 0, 0)),
        ],
        out_specs=pl.BlockSpec((span, width), lambda j, c: (0, 0)),
        scratch_shapes=[
            pltpu.VMEM((heads, span, 1), jnp.float32),
            pltpu.VMEM((heads, span, 1), jnp.float32),
            pltpu.VMEM((heads, span, HD), jnp.float32),
        ],
    )
    kernel = lambda *refs: flash_kernel(*refs, heads=heads, n_local=n_local, half=half)
    return pl.pallas_call(
        kernel,
        grid_spec=grid_spec,
        out_shape=jax.ShapeDtypeStruct((span, width), jnp.bfloat16),
        compiler_params=pltpu.CompilerParams(dimension_semantics=("arbitrary",)),
        cost_estimate=pl.CostEstimate(
            flops=4 * steps * heads * span * span * HD,
            transcendentals=steps * heads * span * span,
            bytes_accessed=2 * steps * span * width * 2,
        ),
    )(chosen, queries, local_stack, local_stack, same_core, same_core, other_core, other_core, bias)


def fetch_out_weight(w_out, head, core):
    groups = lax.axis_size("head")
    columns = w_out.shape[1] // groups
    half = columns // 2
    blocks = lax.dynamic_slice_in_dim(
        w_out.reshape(w_out.shape[0], groups, columns), core * half, half, 2
    )
    exchanged = lax.all_to_all(blocks, "head", 1, 1)
    mine = [
        lax.dynamic_index_in_dim(exchanged, (head - shift) % groups, 1, keepdims=False)
        for shift in range(groups)
    ]
    own_full = lax.dynamic_slice_in_dim(w_out, head * columns, columns, 1)
    return own_full, mine


def local(
    activations,
    mod_table,
    step_index,
    block_mask,
    cache_index,
    w_qkv,
    q_gain,
    k_gain,
    pool_kv,
    w_out,
):
    slot = lax.axis_index("slot")
    head = lax.axis_index("head")
    core = slot % 2
    groups = lax.axis_size("head")
    span = activations.shape[0]
    heads = q_gain.shape[0] // HD
    blocks_q = span // BLOCK
    cache_len = cache_index.shape[1]

    own_full, mine = fetch_out_weight(w_out, head, core)
    slots = lax.axis_size("slot")
    pool_flat = pool_kv.reshape(1, pool_kv.shape[1], -1)
    same_core = [pool_flat] + [from_behind(pool_flat, "slot", 2 * k) for k in range(1, slots // 2)]
    same_core = jnp.concatenate(same_core, axis=0)

    onehot = (jnp.arange(mod_table.shape[0], dtype=jnp.int32) == step_index[slot]).astype(
        jnp.float32
    )
    modulation = jnp.einsum("n,nkd->kd", onehot, mod_table.astype(jnp.float32))
    inputs = activations.astype(jnp.float32)
    normed = inputs * lax.rsqrt(jnp.mean(inputs * inputs, axis=-1, keepdims=True) + 1e-06)
    hidden = (normed * (1.0 + modulation[1][None, :]) + modulation[0][None, :]).astype(jnp.bfloat16)
    qkv = jnp.einsum("td,dkh->tkh", hidden, w_qkv, preferred_element_type=jnp.float32)
    queries = head_norm(qkv[:, 0], q_gain, heads).astype(jnp.bfloat16)
    keys = head_norm(qkv[:, 1], k_gain, heads).astype(jnp.bfloat16)
    values = qkv[:, 2].astype(jnp.bfloat16)
    local_kv = jnp.concatenate([keys.reshape(span, heads * HD), values], axis=1)
    before = from_behind(local_kv, "slot", 1)
    earlier = from_behind(local_kv, "slot", 2)
    queries, before, earlier, same_core, mine = lax.optimization_barrier(
        (queries, before, earlier, same_core, mine)
    )
    other_core = lax.ppermute(same_core, "slot", [(i, i ^ 1) for i in range(slots)])
    own_mask = lax.dynamic_index_in_dim(block_mask, slot, 0, keepdims=False)
    own_cache = lax.dynamic_index_in_dim(cache_index, slot, 0, keepdims=False)
    sibling_slot = jnp.bitwise_xor(slot, 1)
    own_cache = jnp.where(
        own_cache % 2 == core,
        ((slot - own_cache) % slots) // 2,
        slots // 2 + ((sibling_slot - own_cache) % slots) // 2,
    ).astype(jnp.int32)
    width = heads * HD
    local_stack = jnp.stack([local_kv, before, earlier]).reshape(3, span, 2 * width)
    visible = jnp.concatenate([jnp.ones((blocks_q, blocks_q), jnp.int32), own_mask], axis=1)
    visible = jnp.transpose(visible.reshape(blocks_q, 3 + cache_len, blocks_q), (1, 0, 2))
    visible = jnp.repeat(visible, BLOCK, axis=2)
    bias = jnp.where(visible > 0, 0.0, -1e30).astype(jnp.float32)
    rows = span // 2
    parts = rows // BLOCK
    queries = queries.reshape(span, width)
    mixed_parts = [
        flash(queries[p * rows : (p + 1) * rows], local_stack, same_core, other_core,
              bias[:, p * parts : (p + 1) * parts], own_cache, heads)
        for p in range(2)
    ]
    sibling = lax.ppermute(
        jnp.stack(mine[1:]), "slot", [(i, i ^ 1) for i in range(slots)]
    )

    received = [
        jnp.concatenate([
            lax.ppermute(part, "head", [(i, (i + shift) % groups) for i in range(groups)])
            for part in mixed_parts
        ], axis=0)
        for shift in range(1, groups)
    ]
    mixed = jnp.concatenate(mixed_parts, axis=0)
    columns = own_full.shape[1]
    half = columns // 2
    attn = jnp.dot(mixed, own_full, preferred_element_type=jnp.float32).astype(jnp.bfloat16).astype(jnp.float32)
    attn_mine = None
    attn_sib = None
    for shift in range(1, groups):
        group_o = received[shift - 1]
        part = jnp.dot(group_o, mine[shift], preferred_element_type=jnp.float32)
        part = part.astype(jnp.bfloat16).astype(jnp.float32)
        attn_mine = part if attn_mine is None else attn_mine + part
        part = jnp.dot(group_o, sibling[shift - 1], preferred_element_type=jnp.float32)
        part = part.astype(jnp.bfloat16).astype(jnp.float32)
        attn_sib = part if attn_sib is None else attn_sib + part
    other = jnp.concatenate([attn_mine, attn_sib], axis=1)
    swapped = jnp.concatenate([attn_sib, attn_mine], axis=1)
    attn = attn + jnp.where(core == 0, other, swapped)

    offset = head * columns
    input_cols = lax.dynamic_slice_in_dim(activations, offset, columns, 1).astype(jnp.float32)
    gate_cols = lax.dynamic_slice_in_dim(modulation[2], offset, columns, 0)
    return input_cols + gate_cols[None, :] * attn


def solution(mesh):
    placed = (
        P("slot", None),
        P(),
        P(),
        P(),
        P(),
        P(None, None, "head"),
        P("head"),
        P("head"),
        P("slot", None, None, "head"),
        P("head", None),
    )
    return jax.shard_map(
        local, mesh=mesh, in_specs=placed, out_specs=P("slot", "head"), check_vma=False
    )
```

```python
import jax
import jax.numpy as jnp
from jax import lax
from jax.sharding import PartitionSpec as P
from jax.experimental import pallas as pl
from jax.experimental.pallas import tpu as pltpu

HD = 128
BLOCK = 128


def from_behind(shard, axis, by):
    length = lax.axis_size(axis)
    return lax.ppermute(shard, axis, [(i, (i + by) % length) for i in range(length)])


def head_norm(values, gain, heads):
    shaped = values.reshape(values.shape[0], heads, HD)
    scaled = shaped * lax.rsqrt(jnp.mean(shaped * shaped, axis=-1, keepdims=True) + 1e-06)
    return scaled * gain.reshape(heads, HD)


def attend(state, queries, span_kv, visible_blocks):
    highest, totals, accum = state
    heads = queries.shape[1]
    span_keys = span_kv[:, 0].reshape(span_kv.shape[0], heads, HD)
    span_values = span_kv[:, 1].reshape(span_kv.shape[0], heads, HD)
    visible = jnp.repeat(jnp.repeat(visible_blocks, BLOCK, axis=0), BLOCK, axis=1) > 0
    scores = jnp.einsum("qhd,khd->hqk", queries, span_keys, preferred_element_type=jnp.float32) * (
        1.0 / HD**0.5
    )
    scores = jnp.where(visible[None], scores, -1e30)
    new_high = jnp.maximum(highest, jnp.max(scores, axis=-1))
    factor = jnp.exp(highest - new_high)
    weights = jnp.where(visible[None], jnp.exp(scores - new_high[..., None]), 0.0)
    totals = totals * factor + jnp.sum(weights, axis=-1)
    accum = accum * factor[..., None] + jnp.einsum(
        "hqk,khd->hqd",
        weights.astype(jnp.bfloat16),
        span_values,
        preferred_element_type=jnp.float32,
    )
    return (new_high, totals, accum)


def flash_kernel(chosen, q_ref, lk_ref, lv_ref, ak_ref, av_ref, bk_ref, bv_ref, bias_ref, o_ref, m_sc, l_sc, acc_sc, *, heads, n_local, half):
    step = pl.program_id(0)
    span = q_ref.shape[0]
    blocks = bias_ref.shape[0]

    @pl.when(step == 0)
    def _():
        m_sc[...] = jnp.full(m_sc.shape, -1e30, jnp.float32)
        l_sc[...] = jnp.zeros(l_sc.shape, jnp.float32)
        acc_sc[...] = jnp.zeros(acc_sc.shape, jnp.float32)

    def body(k_ref, v_ref):
        bias = bias_ref[...][:, None, :]
        for h in range(heads):
            cols = slice(h * HD, (h + 1) * HD)
            q = q_ref[:, cols]
            k = k_ref[:, cols]
            s = lax.dot_general(q, k, (((1,), (1,)), ((), ())), preferred_element_type=jnp.float32)
            s = (s * (1.0 / HD**0.5)).reshape(blocks, span // blocks, s.shape[1]) + bias
            s = s.reshape(span, -1)
            m_prev = m_sc[h]
            m_new = jnp.maximum(m_prev, jnp.max(s, axis=1, keepdims=True))
            factor = jnp.exp(m_prev - m_new)
            p = jnp.exp(s - m_new)
            l_sc[h] = l_sc[h] * factor + jnp.sum(p, axis=1, keepdims=True)
            acc_sc[h] = acc_sc[h] * factor + jnp.dot(
                p.astype(jnp.bfloat16), v_ref[:, cols], preferred_element_type=jnp.float32
            )
            m_sc[h] = m_new

    @pl.when(step < n_local)
    def _():
        body(lk_ref, lv_ref)

    pos = chosen[jnp.maximum(step - n_local, 0)]

    @pl.when((step >= n_local) & (pos < half))
    def _():
        body(ak_ref, av_ref)

    @pl.when((step >= n_local) & (pos >= half))
    def _():
        body(bk_ref, bv_ref)

    @pl.when(step == pl.num_programs(0) - 1)
    def _():
        for h in range(heads):
            cols = slice(h * HD, (h + 1) * HD)
            o_ref[:, cols] = (acc_sc[h] / l_sc[h]).astype(o_ref.dtype)


def flash(queries, local_stack, same_core, other_core, bias, chosen, heads):
    span, width = queries.shape
    n_local = local_stack.shape[0]
    half = same_core.shape[0]
    steps = n_local + chosen.shape[0]
    blocks = bias.shape[1]

    def local_map(kv):
        return lambda j, c: (jnp.minimum(j, n_local - 1), 0, kv)

    def pool_map(kv, upper):
        def index(j, c):
            pos = c[jnp.maximum(j - n_local, 0)]
            hit = (j >= n_local) & ((pos >= half) == upper)
            return (jnp.where(hit, pos - upper * half, 0), 0, kv)

        return index

    keys_len = local_stack.shape[1]
    kv_block = (None, keys_len, width)
    grid_spec = pltpu.PrefetchScalarGridSpec(
        num_scalar_prefetch=1,
        grid=(steps,),
        in_specs=[
            pl.BlockSpec((span, width), lambda j, c: (0, 0)),
            pl.BlockSpec(kv_block, local_map(0)),
            pl.BlockSpec(kv_block, local_map(1)),
            pl.BlockSpec(kv_block, pool_map(0, False)),
            pl.BlockSpec(kv_block, pool_map(1, False)),
            pl.BlockSpec(kv_block, pool_map(0, True)),
            pl.BlockSpec(kv_block, pool_map(1, True)),
            pl.BlockSpec((None, blocks, keys_len), lambda j, c: (j, 0, 0)),
        ],
        out_specs=pl.BlockSpec((span, width), lambda j, c: (0, 0)),
        scratch_shapes=[
            pltpu.VMEM((heads, span, 1), jnp.float32),
            pltpu.VMEM((heads, span, 1), jnp.float32),
            pltpu.VMEM((heads, span, HD), jnp.float32),
        ],
    )
    kernel = lambda *refs: flash_kernel(*refs, heads=heads, n_local=n_local, half=half)
    return pl.pallas_call(
        kernel,
        grid_spec=grid_spec,
        out_shape=jax.ShapeDtypeStruct((span, width), jnp.bfloat16),
        compiler_params=pltpu.CompilerParams(dimension_semantics=("arbitrary",)),
        cost_estimate=pl.CostEstimate(
            flops=4 * steps * heads * span * span * HD,
            transcendentals=steps * heads * span * span,
            bytes_accessed=2 * steps * span * width * 2,
        ),
    )(chosen, queries, local_stack, local_stack, same_core, same_core, other_core, other_core, bias)


def fetch_out_weight(w_out, head, core):
    groups = lax.axis_size("head")
    columns = w_out.shape[1] // groups
    half = columns // 2
    blocks = jnp.stack([
        lax.dynamic_slice_in_dim(w_out, dest * columns + core * half, half, 1)
        for dest in range(groups)
    ])
    exchanged = lax.all_to_all(blocks, "head", 0, 0)
    mine = [
        lax.dynamic_index_in_dim(exchanged, (head - shift) % groups, 0, keepdims=False)
        for shift in range(groups)
    ]
    own_full = lax.dynamic_slice_in_dim(w_out, head * columns, columns, 1)
    return own_full, mine


def local(
    activations,
    mod_table,
    step_index,
    block_mask,
    cache_index,
    w_qkv,
    q_gain,
    k_gain,
    pool_kv,
    w_out,
):
    slot = lax.axis_index("slot")
    head = lax.axis_index("head")
    core = slot % 2
    groups = lax.axis_size("head")
    span = activations.shape[0]
    heads = q_gain.shape[0] // HD
    blocks_q = span // BLOCK
    cache_len = cache_index.shape[1]

    own_full, mine = fetch_out_weight(w_out, head, core)
    slots = lax.axis_size("slot")
    pool_flat = pool_kv.reshape(1, pool_kv.shape[1], -1)
    same_core = [pool_flat] + [from_behind(pool_flat, "slot", 2 * k) for k in range(1, slots // 2)]
    same_core = jnp.concatenate(same_core, axis=0)

    onehot = (jnp.arange(mod_table.shape[0], dtype=jnp.int32) == step_index[slot]).astype(
        jnp.float32
    )
    modulation = jnp.einsum("n,nkd->kd", onehot, mod_table.astype(jnp.float32))
    inputs = activations.astype(jnp.float32)
    normed = inputs * lax.rsqrt(jnp.mean(inputs * inputs, axis=-1, keepdims=True) + 1e-06)
    hidden = (normed * (1.0 + modulation[1][None, :]) + modulation[0][None, :]).astype(jnp.bfloat16)
    qkv = jnp.einsum("td,dkh->tkh", hidden, w_qkv, preferred_element_type=jnp.float32)
    queries = head_norm(qkv[:, 0], q_gain, heads).astype(jnp.bfloat16)
    keys = head_norm(qkv[:, 1], k_gain, heads).astype(jnp.bfloat16)
    values = qkv[:, 2].astype(jnp.bfloat16)
    local_kv = jnp.concatenate([keys.reshape(span, heads * HD), values], axis=1)
    before = from_behind(local_kv, "slot", 1)
    earlier = from_behind(local_kv, "slot", 2)
    queries, before, earlier, same_core, mine = lax.optimization_barrier(
        (queries, before, earlier, same_core, mine)
    )
    other_core = lax.ppermute(same_core, "slot", [(i, i ^ 1) for i in range(slots)])
    own_mask = lax.dynamic_index_in_dim(block_mask, slot, 0, keepdims=False)
    own_cache = lax.dynamic_index_in_dim(cache_index, slot, 0, keepdims=False)
    sibling_slot = jnp.bitwise_xor(slot, 1)
    own_cache = jnp.where(
        own_cache % 2 == core,
        ((slot - own_cache) % slots) // 2,
        slots // 2 + ((sibling_slot - own_cache) % slots) // 2,
    ).astype(jnp.int32)
    width = heads * HD
    local_stack = jnp.stack([local_kv, before, earlier]).reshape(3, span, 2 * width)
    visible = jnp.concatenate([jnp.ones((blocks_q, blocks_q), jnp.int32), own_mask], axis=1)
    visible = jnp.transpose(visible.reshape(blocks_q, 3 + cache_len, blocks_q), (1, 0, 2))
    visible = jnp.repeat(visible, BLOCK, axis=2)
    bias = jnp.where(visible > 0, 0.0, -1e30).astype(jnp.float32)
    rows = span // 2
    parts = rows // BLOCK
    queries = queries.reshape(span, width)
    mixed_parts = [
        flash(queries[p * rows : (p + 1) * rows], local_stack, same_core, other_core,
              bias[:, p * parts : (p + 1) * parts], own_cache, heads)
        for p in range(2)
    ]
    sibling = lax.ppermute(
        jnp.stack(mine[1:]), "slot", [(i, i ^ 1) for i in range(slots)]
    )

    received = [
        jnp.concatenate([
            lax.ppermute(part, "head", [(i, (i + shift) % groups) for i in range(groups)])
            for part in mixed_parts
        ], axis=0)
        for shift in range(1, groups)
    ]
    mixed = jnp.concatenate(mixed_parts, axis=0)
    columns = own_full.shape[1]
    half = columns // 2
    attn = jnp.dot(mixed, own_full, preferred_element_type=jnp.float32).astype(jnp.bfloat16).astype(jnp.float32)
    attn_mine = None
    attn_sib = None
    for shift in range(1, groups):
        group_o = received[shift - 1]
        part = jnp.dot(group_o, mine[shift], preferred_element_type=jnp.float32)
        part = part.astype(jnp.bfloat16).astype(jnp.float32)
        attn_mine = part if attn_mine is None else attn_mine + part
        part = jnp.dot(group_o, sibling[shift - 1], preferred_element_type=jnp.float32)
        part = part.astype(jnp.bfloat16).astype(jnp.float32)
        attn_sib = part if attn_sib is None else attn_sib + part
    other = jnp.concatenate([attn_mine, attn_sib], axis=1)
    swapped = jnp.concatenate([attn_sib, attn_mine], axis=1)
    attn = attn + jnp.where(core == 0, other, swapped)

    offset = head * columns
    input_cols = lax.dynamic_slice_in_dim(activations, offset, columns, 1).astype(jnp.float32)
    gate_cols = lax.dynamic_slice_in_dim(modulation[2], offset, columns, 0)
    return input_cols + gate_cols[None, :] * attn


def solution(mesh):
    placed = (
        P("slot", None),
        P(),
        P(),
        P(),
        P(),
        P(None, None, "head"),
        P("head"),
        P("head"),
        P("slot", None, None, "head"),
        P("head", None),
    )
    return jax.shard_map(
        local, mesh=mesh, in_specs=placed, out_specs=P("slot", "head"), check_vma=False
    )
```

```python
import jax
import jax.numpy as jnp
from jax import lax
from jax.sharding import PartitionSpec as P
from jax.experimental import pallas as pl
from jax.experimental.pallas import tpu as pltpu

HD = 128
BLOCK = 128


def from_behind(shard, axis, by):
    length = lax.axis_size(axis)
    return lax.ppermute(shard, axis, [(i, (i + by) % length) for i in range(length)])


def head_norm(values, gain, heads):
    shaped = values.reshape(values.shape[0], heads, HD)
    scaled = shaped * lax.rsqrt(jnp.mean(shaped * shaped, axis=-1, keepdims=True) + 1e-06)
    return scaled * gain.reshape(heads, HD)


def attend(state, queries, span_kv, visible_blocks):
    highest, totals, accum = state
    heads = queries.shape[1]
    span_keys = span_kv[:, 0].reshape(span_kv.shape[0], heads, HD)
    span_values = span_kv[:, 1].reshape(span_kv.shape[0], heads, HD)
    visible = jnp.repeat(jnp.repeat(visible_blocks, BLOCK, axis=0), BLOCK, axis=1) > 0
    scores = jnp.einsum("qhd,khd->hqk", queries, span_keys, preferred_element_type=jnp.float32) * (
        1.0 / HD**0.5
    )
    scores = jnp.where(visible[None], scores, -1e30)
    new_high = jnp.maximum(highest, jnp.max(scores, axis=-1))
    factor = jnp.exp(highest - new_high)
    weights = jnp.where(visible[None], jnp.exp(scores - new_high[..., None]), 0.0)
    totals = totals * factor + jnp.sum(weights, axis=-1)
    accum = accum * factor[..., None] + jnp.einsum(
        "hqk,khd->hqd",
        weights.astype(jnp.bfloat16),
        span_values,
        preferred_element_type=jnp.float32,
    )
    return (new_high, totals, accum)


def flash_kernel(chosen, q_ref, lk_ref, lv_ref, ak_ref, av_ref, bk_ref, bv_ref, bias_ref, o_ref, m_sc, l_sc, acc_sc, *, heads, n_local, half):
    step = pl.program_id(0)
    span = q_ref.shape[0]
    blocks = bias_ref.shape[0]

    @pl.when(step == 0)
    def _():
        m_sc[...] = jnp.full(m_sc.shape, -1e30, jnp.float32)
        l_sc[...] = jnp.zeros(l_sc.shape, jnp.float32)
        acc_sc[...] = jnp.zeros(acc_sc.shape, jnp.float32)

    def body(k_ref, v_ref):
        rows = span // blocks
        for h in range(heads):
            cols = slice(h * HD, (h + 1) * HD)
            k = k_ref[:, cols]
            v = v_ref[:, cols]
            for a in range(blocks):
                part = slice(a * rows, (a + 1) * rows)
                q = q_ref[part, cols]
                s = lax.dot_general(q, k, (((1,), (1,)), ((), ())), preferred_element_type=jnp.float32)
                s = s * (1.0 / HD**0.5) + bias_ref[a : a + 1, :]
                m_prev = m_sc[h, part]
                m_new = jnp.maximum(m_prev, jnp.max(s, axis=1, keepdims=True))
                factor = jnp.exp(m_prev - m_new)
                p = jnp.exp(s - m_new)
                l_sc[h, part] = l_sc[h, part] * factor + jnp.sum(p, axis=1, keepdims=True)
                acc_sc[h, part] = acc_sc[h, part] * factor + jnp.dot(
                    p.astype(jnp.bfloat16), v, preferred_element_type=jnp.float32
                )
                m_sc[h, part] = m_new

    @pl.when(step < n_local)
    def _():
        body(lk_ref, lv_ref)

    pos = chosen[jnp.maximum(step - n_local, 0)]

    @pl.when((step >= n_local) & (pos < half))
    def _():
        body(ak_ref, av_ref)

    @pl.when((step >= n_local) & (pos >= half))
    def _():
        body(bk_ref, bv_ref)

    @pl.when(step == pl.num_programs(0) - 1)
    def _():
        for h in range(heads):
            cols = slice(h * HD, (h + 1) * HD)
            o_ref[:, cols] = (acc_sc[h] / l_sc[h]).astype(o_ref.dtype)


def flash(queries, local_stack, same_core, other_core, bias, chosen, heads):
    span, width = queries.shape
    n_local = local_stack.shape[0]
    half = same_core.shape[0]
    steps = n_local + chosen.shape[0]
    blocks = bias.shape[1]

    def local_map(kv):
        return lambda j, c: (jnp.minimum(j, n_local - 1), 0, kv)

    def pool_map(kv, upper):
        def index(j, c):
            pos = c[jnp.maximum(j - n_local, 0)]
            hit = (j >= n_local) & ((pos >= half) == upper)
            return (jnp.where(hit, pos - upper * half, 0), 0, kv)

        return index

    keys_len = local_stack.shape[1]
    kv_block = (None, keys_len, width)
    grid_spec = pltpu.PrefetchScalarGridSpec(
        num_scalar_prefetch=1,
        grid=(steps,),
        in_specs=[
            pl.BlockSpec((span, width), lambda j, c: (0, 0)),
            pl.BlockSpec(kv_block, local_map(0)),
            pl.BlockSpec(kv_block, local_map(1)),
            pl.BlockSpec(kv_block, pool_map(0, False)),
            pl.BlockSpec(kv_block, pool_map(1, False)),
            pl.BlockSpec(kv_block, pool_map(0, True)),
            pl.BlockSpec(kv_block, pool_map(1, True)),
            pl.BlockSpec((None, blocks, keys_len), lambda j, c: (j, 0, 0)),
        ],
        out_specs=pl.BlockSpec((span, width), lambda j, c: (0, 0)),
        scratch_shapes=[
            pltpu.VMEM((heads, span, 1), jnp.float32),
            pltpu.VMEM((heads, span, 1), jnp.float32),
            pltpu.VMEM((heads, span, HD), jnp.float32),
        ],
    )
    kernel = lambda *refs: flash_kernel(*refs, heads=heads, n_local=n_local, half=half)
    return pl.pallas_call(
        kernel,
        grid_spec=grid_spec,
        out_shape=jax.ShapeDtypeStruct((span, width), jnp.bfloat16),
        compiler_params=pltpu.CompilerParams(dimension_semantics=("arbitrary",)),
        cost_estimate=pl.CostEstimate(
            flops=4 * steps * heads * span * span * HD,
            transcendentals=steps * heads * span * span,
            bytes_accessed=2 * steps * span * width * 2,
        ),
    )(chosen, queries, local_stack, local_stack, same_core, same_core, other_core, other_core, bias)


def fetch_out_weight(w_out, head, core):
    groups = lax.axis_size("head")
    columns = w_out.shape[1] // groups
    half = columns // 2
    blocks = jnp.stack([
        lax.dynamic_slice_in_dim(w_out, dest * columns + core * half, half, 1)
        for dest in range(groups)
    ])
    exchanged = lax.all_to_all(blocks, "head", 0, 0)
    mine = [
        lax.dynamic_index_in_dim(exchanged, (head - shift) % groups, 0, keepdims=False)
        for shift in range(groups)
    ]
    own_full = lax.dynamic_slice_in_dim(w_out, head * columns, columns, 1)
    return own_full, mine


def local(
    activations,
    mod_table,
    step_index,
    block_mask,
    cache_index,
    w_qkv,
    q_gain,
    k_gain,
    pool_kv,
    w_out,
):
    slot = lax.axis_index("slot")
    head = lax.axis_index("head")
    core = slot % 2
    groups = lax.axis_size("head")
    span = activations.shape[0]
    heads = q_gain.shape[0] // HD
    blocks_q = span // BLOCK
    cache_len = cache_index.shape[1]

    own_full, mine = fetch_out_weight(w_out, head, core)
    slots = lax.axis_size("slot")
    pool_flat = pool_kv.reshape(1, pool_kv.shape[1], -1)
    same_core = [pool_flat] + [from_behind(pool_flat, "slot", 2 * k) for k in range(1, slots // 2)]
    same_core = jnp.concatenate(same_core, axis=0)

    onehot = (jnp.arange(mod_table.shape[0], dtype=jnp.int32) == step_index[slot]).astype(
        jnp.float32
    )
    modulation = jnp.einsum("n,nkd->kd", onehot, mod_table.astype(jnp.float32))
    inputs = activations.astype(jnp.float32)
    normed = inputs * lax.rsqrt(jnp.mean(inputs * inputs, axis=-1, keepdims=True) + 1e-06)
    hidden = (normed * (1.0 + modulation[1][None, :]) + modulation[0][None, :]).astype(jnp.bfloat16)
    qkv = jnp.einsum("td,dkh->tkh", hidden, w_qkv, preferred_element_type=jnp.float32)
    queries = head_norm(qkv[:, 0], q_gain, heads).astype(jnp.bfloat16)
    keys = head_norm(qkv[:, 1], k_gain, heads).astype(jnp.bfloat16)
    values = qkv[:, 2].astype(jnp.bfloat16)
    local_kv = jnp.concatenate([keys.reshape(span, heads * HD), values], axis=1)
    before = from_behind(local_kv, "slot", 1)
    earlier = from_behind(local_kv, "slot", 2)
    queries, before, earlier, same_core, mine = lax.optimization_barrier(
        (queries, before, earlier, same_core, mine)
    )
    other_core = lax.ppermute(same_core, "slot", [(i, i ^ 1) for i in range(slots)])
    own_mask = lax.dynamic_index_in_dim(block_mask, slot, 0, keepdims=False)
    own_cache = lax.dynamic_index_in_dim(cache_index, slot, 0, keepdims=False)
    sibling_slot = jnp.bitwise_xor(slot, 1)
    own_cache = jnp.where(
        own_cache % 2 == core,
        ((slot - own_cache) % slots) // 2,
        slots // 2 + ((sibling_slot - own_cache) % slots) // 2,
    ).astype(jnp.int32)
    width = heads * HD
    local_stack = jnp.stack([local_kv, before, earlier]).reshape(3, span, 2 * width)
    visible = jnp.concatenate([jnp.ones((blocks_q, blocks_q), jnp.int32), own_mask], axis=1)
    visible = jnp.transpose(visible.reshape(blocks_q, 3 + cache_len, blocks_q), (1, 0, 2))
    visible = jnp.repeat(visible, BLOCK, axis=2)
    bias = jnp.where(visible > 0, 0.0, -1e30).astype(jnp.float32)
    rows = span // 2
    parts = rows // BLOCK
    queries = queries.reshape(span, width)
    mixed_parts = [
        flash(queries[p * rows : (p + 1) * rows], local_stack, same_core, other_core,
              bias[:, p * parts : (p + 1) * parts], own_cache, heads)
        for p in range(2)
    ]
    sibling = lax.ppermute(
        jnp.stack(mine[1:]), "slot", [(i, i ^ 1) for i in range(slots)]
    )

    received = [
        jnp.concatenate([
            lax.ppermute(part, "head", [(i, (i + shift) % groups) for i in range(groups)])
            for part in mixed_parts
        ], axis=0)
        for shift in range(1, groups)
    ]
    mixed = jnp.concatenate(mixed_parts, axis=0)
    columns = own_full.shape[1]
    half = columns // 2
    attn = jnp.dot(mixed, own_full, preferred_element_type=jnp.float32).astype(jnp.bfloat16).astype(jnp.float32)
    attn_mine = None
    attn_sib = None
    for shift in range(1, groups):
        group_o = received[shift - 1]
        part = jnp.dot(group_o, mine[shift], preferred_element_type=jnp.float32)
        part = part.astype(jnp.bfloat16).astype(jnp.float32)
        attn_mine = part if attn_mine is None else attn_mine + part
        part = jnp.dot(group_o, sibling[shift - 1], preferred_element_type=jnp.float32)
        part = part.astype(jnp.bfloat16).astype(jnp.float32)
        attn_sib = part if attn_sib is None else attn_sib + part
    other = jnp.concatenate([attn_mine, attn_sib], axis=1)
    swapped = jnp.concatenate([attn_sib, attn_mine], axis=1)
    attn = attn + jnp.where(core == 0, other, swapped)

    offset = head * columns
    input_cols = lax.dynamic_slice_in_dim(activations, offset, columns, 1).astype(jnp.float32)
    gate_cols = lax.dynamic_slice_in_dim(modulation[2], offset, columns, 0)
    return input_cols + gate_cols[None, :] * attn


def solution(mesh):
    placed = (
        P("slot", None),
        P(),
        P(),
        P(),
        P(),
        P(None, None, "head"),
        P("head"),
        P("head"),
        P("slot", None, None, "head"),
        P("head", None),
    )
    return jax.shard_map(
        local, mesh=mesh, in_specs=placed, out_specs=P("slot", "head"), check_vma=False
    )
```

```python
import jax
import jax.numpy as jnp
from jax import lax
from jax.sharding import PartitionSpec as P
from jax.experimental import pallas as pl
from jax.experimental.pallas import tpu as pltpu

HD = 128
BLOCK = 128


def from_behind(shard, axis, by):
    length = lax.axis_size(axis)
    return lax.ppermute(shard, axis, [(i, (i + by) % length) for i in range(length)])


def head_norm(values, gain, heads):
    shaped = values.reshape(values.shape[0], heads, HD)
    scaled = shaped * lax.rsqrt(jnp.mean(shaped * shaped, axis=-1, keepdims=True) + 1e-06)
    return scaled * gain.reshape(heads, HD)


def attend(state, queries, span_kv, visible_blocks):
    highest, totals, accum = state
    heads = queries.shape[1]
    span_keys = span_kv[:, 0].reshape(span_kv.shape[0], heads, HD)
    span_values = span_kv[:, 1].reshape(span_kv.shape[0], heads, HD)
    visible = jnp.repeat(jnp.repeat(visible_blocks, BLOCK, axis=0), BLOCK, axis=1) > 0
    scores = jnp.einsum("qhd,khd->hqk", queries, span_keys, preferred_element_type=jnp.float32) * (
        1.0 / HD**0.5
    )
    scores = jnp.where(visible[None], scores, -1e30)
    new_high = jnp.maximum(highest, jnp.max(scores, axis=-1))
    factor = jnp.exp(highest - new_high)
    weights = jnp.where(visible[None], jnp.exp(scores - new_high[..., None]), 0.0)
    totals = totals * factor + jnp.sum(weights, axis=-1)
    accum = accum * factor[..., None] + jnp.einsum(
        "hqk,khd->hqd",
        weights.astype(jnp.bfloat16),
        span_values,
        preferred_element_type=jnp.float32,
    )
    return (new_high, totals, accum)


def flash_kernel(chosen, q_ref, lk_ref, lv_ref, ak_ref, av_ref, bk_ref, bv_ref, bias_ref, o_ref, m_sc, l_sc, acc_sc, *, heads, n_local, half):
    step = pl.program_id(0)
    span = q_ref.shape[0]
    blocks = bias_ref.shape[0]

    @pl.when(step == 0)
    def _():
        m_sc[...] = jnp.full(m_sc.shape, -1e30, jnp.float32)
        l_sc[...] = jnp.zeros(l_sc.shape, jnp.float32)
        acc_sc[...] = jnp.zeros(acc_sc.shape, jnp.float32)

    def body(k_ref, v_ref):
        bias = bias_ref[...][:, None, :]
        for h in range(heads):
            cols = slice(h * HD, (h + 1) * HD)
            q = q_ref[:, cols]
            k = k_ref[:, cols]
            s = lax.dot_general(q, k, (((1,), (1,)), ((), ())), preferred_element_type=jnp.float32)
            s = (s * (1.0 / HD**0.5)).reshape(blocks, span // blocks, s.shape[1]) + bias
            s = s.reshape(span, -1)
            m_prev = m_sc[h]
            m_new = jnp.maximum(m_prev, jnp.max(s, axis=1, keepdims=True))
            factor = jnp.exp(m_prev - m_new)
            p = jnp.exp(s - m_new)
            l_sc[h] = l_sc[h] * factor + jnp.sum(p, axis=1, keepdims=True)
            acc_sc[h] = acc_sc[h] * factor + jnp.dot(
                p.astype(jnp.bfloat16), v_ref[:, cols], preferred_element_type=jnp.float32
            )
            m_sc[h] = m_new

    @pl.when(step < n_local)
    def _():
        body(lk_ref, lv_ref)

    pos = chosen[jnp.maximum(step - n_local, 0)]

    @pl.when((step >= n_local) & (pos < half))
    def _():
        body(ak_ref, av_ref)

    @pl.when((step >= n_local) & (pos >= half))
    def _():
        body(bk_ref, bv_ref)

    @pl.when(step == pl.num_programs(0) - 1)
    def _():
        for h in range(heads):
            cols = slice(h * HD, (h + 1) * HD)
            o_ref[:, cols] = (acc_sc[h] / l_sc[h]).astype(o_ref.dtype)


def flash(queries, local_stack, same_core, other_core, bias, chosen, heads):
    span, width = queries.shape
    n_local = local_stack.shape[0]
    half = same_core.shape[0]
    steps = n_local + chosen.shape[0]
    blocks = bias.shape[1]

    def local_map(kv):
        return lambda j, c: (jnp.minimum(j, n_local - 1), 0, kv)

    def pool_map(kv, upper):
        def index(j, c):
            pos = c[jnp.maximum(j - n_local, 0)]
            hit = (j >= n_local) & ((pos >= half) == upper)
            return (jnp.where(hit, pos - upper * half, 0), 0, kv)

        return index

    keys_len = local_stack.shape[1]
    kv_block = (None, keys_len, width)
    grid_spec = pltpu.PrefetchScalarGridSpec(
        num_scalar_prefetch=1,
        grid=(steps,),
        in_specs=[
            pl.BlockSpec((span, width), lambda j, c: (0, 0)),
            pl.BlockSpec(kv_block, local_map(0)),
            pl.BlockSpec(kv_block, local_map(1)),
            pl.BlockSpec(kv_block, pool_map(0, False)),
            pl.BlockSpec(kv_block, pool_map(1, False)),
            pl.BlockSpec(kv_block, pool_map(0, True)),
            pl.BlockSpec(kv_block, pool_map(1, True)),
            pl.BlockSpec((None, blocks, keys_len), lambda j, c: (j, 0, 0)),
        ],
        out_specs=pl.BlockSpec((span, width), lambda j, c: (0, 0)),
        scratch_shapes=[
            pltpu.VMEM((heads, span, 1), jnp.float32),
            pltpu.VMEM((heads, span, 1), jnp.float32),
            pltpu.VMEM((heads, span, HD), jnp.float32),
        ],
    )
    kernel = lambda *refs: flash_kernel(*refs, heads=heads, n_local=n_local, half=half)
    return pl.pallas_call(
        kernel,
        grid_spec=grid_spec,
        out_shape=jax.ShapeDtypeStruct((span, width), jnp.bfloat16),
        compiler_params=pltpu.CompilerParams(dimension_semantics=("arbitrary",)),
        cost_estimate=pl.CostEstimate(
            flops=4 * steps * heads * span * span * HD,
            transcendentals=steps * heads * span * span,
            bytes_accessed=2 * steps * span * width * 2,
        ),
    )(chosen, queries, local_stack, local_stack, same_core, same_core, other_core, other_core, bias)


def fetch_out_weight(w_out, head, core):
    groups = lax.axis_size("head")
    columns = w_out.shape[1] // groups
    half = columns // 2
    blocks = jnp.stack([
        lax.dynamic_slice_in_dim(w_out, dest * columns + core * half, half, 1)
        for dest in range(groups)
    ])
    exchanged = lax.all_to_all(blocks, "head", 0, 0)
    mine = [
        lax.dynamic_index_in_dim(exchanged, (head - shift) % groups, 0, keepdims=False)
        for shift in range(groups)
    ]
    own_full = lax.dynamic_slice_in_dim(w_out, head * columns, columns, 1)
    return own_full, mine


def local(
    activations,
    mod_table,
    step_index,
    block_mask,
    cache_index,
    w_qkv,
    q_gain,
    k_gain,
    pool_kv,
    w_out,
):
    slot = lax.axis_index("slot")
    head = lax.axis_index("head")
    core = slot % 2
    groups = lax.axis_size("head")
    span = activations.shape[0]
    heads = q_gain.shape[0] // HD
    blocks_q = span // BLOCK
    cache_len = cache_index.shape[1]

    own_full, mine = fetch_out_weight(w_out, head, core)
    slots = lax.axis_size("slot")
    pool_flat = pool_kv.reshape(1, pool_kv.shape[1], -1)
    same_core = [pool_flat] + [from_behind(pool_flat, "slot", 2 * k) for k in range(1, slots // 2)]
    same_core = jnp.concatenate(same_core, axis=0)

    onehot = (jnp.arange(mod_table.shape[0], dtype=jnp.int32) == step_index[slot]).astype(
        jnp.float32
    )
    modulation = jnp.einsum("n,nkd->kd", onehot, mod_table.astype(jnp.float32))
    inputs = activations.astype(jnp.float32)
    normed = inputs * lax.rsqrt(jnp.mean(inputs * inputs, axis=-1, keepdims=True) + 1e-06)
    hidden = (normed * (1.0 + modulation[1][None, :]) + modulation[0][None, :]).astype(jnp.bfloat16)
    width = heads * HD
    qkv = jnp.einsum("td,dkh->kth", hidden, w_qkv, preferred_element_type=jnp.float32)
    queries = head_norm(qkv[0], q_gain, heads).astype(jnp.bfloat16)
    keys = head_norm(qkv[1], k_gain, heads).astype(jnp.bfloat16)
    values = qkv[2].astype(jnp.bfloat16)
    local_kv = jnp.concatenate([keys.reshape(span, heads * HD), values], axis=1)
    before = from_behind(local_kv, "slot", 1)
    earlier = from_behind(local_kv, "slot", 2)
    queries, before, earlier, same_core, mine = lax.optimization_barrier(
        (queries, before, earlier, same_core, mine)
    )
    other_core = lax.ppermute(same_core, "slot", [(i, i ^ 1) for i in range(slots)])
    own_mask = lax.dynamic_index_in_dim(block_mask, slot, 0, keepdims=False)
    own_cache = lax.dynamic_index_in_dim(cache_index, slot, 0, keepdims=False)
    sibling_slot = jnp.bitwise_xor(slot, 1)
    own_cache = jnp.where(
        own_cache % 2 == core,
        ((slot - own_cache) % slots) // 2,
        slots // 2 + ((sibling_slot - own_cache) % slots) // 2,
    ).astype(jnp.int32)
    width = heads * HD
    local_stack = jnp.stack([local_kv, before, earlier]).reshape(3, span, 2 * width)
    visible = jnp.concatenate([jnp.ones((blocks_q, blocks_q), jnp.int32), own_mask], axis=1)
    visible = jnp.transpose(visible.reshape(blocks_q, 3 + cache_len, blocks_q), (1, 0, 2))
    visible = jnp.repeat(visible, BLOCK, axis=2)
    bias = jnp.where(visible > 0, 0.0, -1e30).astype(jnp.float32)
    rows = span // 2
    parts = rows // BLOCK
    queries = queries.reshape(span, width)
    mixed_parts = [
        flash(queries[p * rows : (p + 1) * rows], local_stack, same_core, other_core,
              bias[:, p * parts : (p + 1) * parts], own_cache, heads)
        for p in range(2)
    ]
    sibling = lax.ppermute(
        jnp.stack(mine[1:]), "slot", [(i, i ^ 1) for i in range(slots)]
    )

    received = [
        jnp.concatenate([
            lax.ppermute(part, "head", [(i, (i + shift) % groups) for i in range(groups)])
            for part in mixed_parts
        ], axis=0)
        for shift in range(1, groups)
    ]
    mixed = jnp.concatenate(mixed_parts, axis=0)
    columns = own_full.shape[1]
    half = columns // 2
    attn = jnp.dot(mixed, own_full, preferred_element_type=jnp.float32).astype(jnp.bfloat16).astype(jnp.float32)
    attn_mine = None
    attn_sib = None
    for shift in range(1, groups):
        group_o = received[shift - 1]
        part = jnp.dot(group_o, mine[shift], preferred_element_type=jnp.float32)
        part = part.astype(jnp.bfloat16).astype(jnp.float32)
        attn_mine = part if attn_mine is None else attn_mine + part
        part = jnp.dot(group_o, sibling[shift - 1], preferred_element_type=jnp.float32)
        part = part.astype(jnp.bfloat16).astype(jnp.float32)
        attn_sib = part if attn_sib is None else attn_sib + part
    other = jnp.concatenate([attn_mine, attn_sib], axis=1)
    swapped = jnp.concatenate([attn_sib, attn_mine], axis=1)
    attn = attn + jnp.where(core == 0, other, swapped)

    offset = head * columns
    input_cols = lax.dynamic_slice_in_dim(activations, offset, columns, 1).astype(jnp.float32)
    gate_cols = lax.dynamic_slice_in_dim(modulation[2], offset, columns, 0)
    return input_cols + gate_cols[None, :] * attn


def solution(mesh):
    placed = (
        P("slot", None),
        P(),
        P(),
        P(),
        P(),
        P(None, None, "head"),
        P("head"),
        P("head"),
        P("slot", None, None, "head"),
        P("head", None),
    )
    return jax.shard_map(
        local, mesh=mesh, in_specs=placed, out_specs=P("slot", "head"), check_vma=False
    )
```

```python
import jax
import jax.numpy as jnp
from jax import lax
from jax.sharding import PartitionSpec as P
from jax.experimental import pallas as pl
from jax.experimental.pallas import tpu as pltpu

HD = 128
BLOCK = 128


def from_behind(shard, axis, by):
    length = lax.axis_size(axis)
    return lax.ppermute(shard, axis, [(i, (i + by) % length) for i in range(length)])


def head_norm(values, gain, heads):
    shaped = values.reshape(values.shape[0], heads, HD)
    scaled = shaped * lax.rsqrt(jnp.mean(shaped * shaped, axis=-1, keepdims=True) + 1e-06)
    return scaled * gain.reshape(heads, HD)


def attend(state, queries, span_kv, visible_blocks):
    highest, totals, accum = state
    heads = queries.shape[1]
    span_keys = span_kv[:, 0].reshape(span_kv.shape[0], heads, HD)
    span_values = span_kv[:, 1].reshape(span_kv.shape[0], heads, HD)
    visible = jnp.repeat(jnp.repeat(visible_blocks, BLOCK, axis=0), BLOCK, axis=1) > 0
    scores = jnp.einsum("qhd,khd->hqk", queries, span_keys, preferred_element_type=jnp.float32) * (
        1.0 / HD**0.5
    )
    scores = jnp.where(visible[None], scores, -1e30)
    new_high = jnp.maximum(highest, jnp.max(scores, axis=-1))
    factor = jnp.exp(highest - new_high)
    weights = jnp.where(visible[None], jnp.exp(scores - new_high[..., None]), 0.0)
    totals = totals * factor + jnp.sum(weights, axis=-1)
    accum = accum * factor[..., None] + jnp.einsum(
        "hqk,khd->hqd",
        weights.astype(jnp.bfloat16),
        span_values,
        preferred_element_type=jnp.float32,
    )
    return (new_high, totals, accum)


def flash_kernel(chosen, q_ref, lk_ref, lv_ref, ak_ref, av_ref, bk_ref, bv_ref, bias_ref, o_ref, m_sc, l_sc, acc_sc, *, heads, n_local, half):
    step = pl.program_id(0)
    span = q_ref.shape[0]
    blocks = bias_ref.shape[0]

    @pl.when(step == 0)
    def _():
        m_sc[...] = jnp.full(m_sc.shape, -1e30, jnp.float32)
        l_sc[...] = jnp.zeros(l_sc.shape, jnp.float32)
        acc_sc[...] = jnp.zeros(acc_sc.shape, jnp.float32)

    def body(k_ref, v_ref):
        bias = bias_ref[...][:, None, :]
        for h in range(heads):
            cols = slice(h * HD, (h + 1) * HD)
            q = q_ref[:, cols]
            k = k_ref[:, cols]
            s = lax.dot_general(q, k, (((1,), (1,)), ((), ())), preferred_element_type=jnp.float32)
            s = (s * (1.0 / HD**0.5)).reshape(blocks, span // blocks, s.shape[1]) + bias
            s = s.reshape(span, -1)
            m_prev = m_sc[h]
            m_new = jnp.maximum(m_prev, jnp.max(s, axis=1, keepdims=True))
            factor = jnp.exp(m_prev - m_new)
            p = jnp.exp(s - m_new)
            l_sc[h] = l_sc[h] * factor + jnp.sum(p, axis=1, keepdims=True)
            acc_sc[h] = acc_sc[h] * factor + jnp.dot(
                p.astype(jnp.bfloat16), v_ref[:, cols], preferred_element_type=jnp.float32
            )
            m_sc[h] = m_new

    @pl.when(step < n_local)
    def _():
        body(lk_ref, lv_ref)

    pos = chosen[jnp.maximum(step - n_local, 0)]

    @pl.when((step >= n_local) & (pos < half))
    def _():
        body(ak_ref, av_ref)

    @pl.when((step >= n_local) & (pos >= half))
    def _():
        body(bk_ref, bv_ref)

    @pl.when(step == pl.num_programs(0) - 1)
    def _():
        for h in range(heads):
            cols = slice(h * HD, (h + 1) * HD)
            o_ref[:, cols] = (acc_sc[h] / l_sc[h]).astype(o_ref.dtype)


def flash(queries, local_stack, same_core, other_core, bias, chosen, heads):
    span, width = queries.shape
    n_local = local_stack.shape[0]
    half = same_core.shape[0]
    steps = n_local + chosen.shape[0]
    blocks = bias.shape[1]

    def local_map(kv):
        return lambda j, c: (jnp.minimum(j, n_local - 1), 0, kv)

    def pool_map(kv, upper):
        def index(j, c):
            pos = c[jnp.maximum(j - n_local, 0)]
            hit = (j >= n_local) & ((pos >= half) == upper)
            return (jnp.where(hit, pos - upper * half, 0), 0, kv)

        return index

    keys_len = local_stack.shape[1]
    kv_block = (None, keys_len, width)
    grid_spec = pltpu.PrefetchScalarGridSpec(
        num_scalar_prefetch=1,
        grid=(steps,),
        in_specs=[
            pl.BlockSpec((span, width), lambda j, c: (0, 0)),
            pl.BlockSpec(kv_block, local_map(0)),
            pl.BlockSpec(kv_block, local_map(1)),
            pl.BlockSpec(kv_block, pool_map(0, False)),
            pl.BlockSpec(kv_block, pool_map(1, False)),
            pl.BlockSpec(kv_block, pool_map(0, True)),
            pl.BlockSpec(kv_block, pool_map(1, True)),
            pl.BlockSpec((None, blocks, keys_len), lambda j, c: (j, 0, 0)),
        ],
        out_specs=pl.BlockSpec((span, width), lambda j, c: (0, 0)),
        scratch_shapes=[
            pltpu.VMEM((heads, span, 1), jnp.float32),
            pltpu.VMEM((heads, span, 1), jnp.float32),
            pltpu.VMEM((heads, span, HD), jnp.float32),
        ],
    )
    kernel = lambda *refs: flash_kernel(*refs, heads=heads, n_local=n_local, half=half)
    return pl.pallas_call(
        kernel,
        grid_spec=grid_spec,
        out_shape=jax.ShapeDtypeStruct((span, width), jnp.bfloat16),
        compiler_params=pltpu.CompilerParams(dimension_semantics=("arbitrary",)),
        cost_estimate=pl.CostEstimate(
            flops=4 * steps * heads * span * span * HD,
            transcendentals=steps * heads * span * span,
            bytes_accessed=2 * steps * span * width * 2,
        ),
    )(chosen, queries, local_stack, local_stack, same_core, same_core, other_core, other_core, bias)


def fetch_out_weight(w_out, head, core):
    groups = lax.axis_size("head")
    columns = w_out.shape[1] // groups
    half = columns // 2
    blocks = jnp.stack([
        lax.dynamic_slice_in_dim(w_out, dest * columns + core * half, half, 1)
        for dest in range(groups)
    ])
    exchanged = lax.all_to_all(blocks, "head", 0, 0)
    mine = [
        lax.dynamic_index_in_dim(exchanged, (head - shift) % groups, 0, keepdims=False)
        for shift in range(groups)
    ]
    own_full = lax.dynamic_slice_in_dim(w_out, head * columns, columns, 1)
    return own_full, mine


def local(
    activations,
    mod_table,
    step_index,
    block_mask,
    cache_index,
    w_qkv,
    q_gain,
    k_gain,
    pool_kv,
    w_out,
):
    slot = lax.axis_index("slot")
    head = lax.axis_index("head")
    core = slot % 2
    groups = lax.axis_size("head")
    span = activations.shape[0]
    heads = q_gain.shape[0] // HD
    blocks_q = span // BLOCK
    cache_len = cache_index.shape[1]

    own_full, mine = fetch_out_weight(w_out, head, core)
    slots = lax.axis_size("slot")
    pool_flat = pool_kv.reshape(1, pool_kv.shape[1], -1)
    same_core = [pool_flat] + [from_behind(pool_flat, "slot", 2 * k) for k in range(1, slots // 2)]
    same_core = jnp.concatenate(same_core, axis=0)

    onehot = (jnp.arange(mod_table.shape[0], dtype=jnp.int32) == step_index[slot]).astype(
        jnp.float32
    )
    modulation = jnp.einsum("n,nkd->kd", onehot, mod_table.astype(jnp.float32))
    inputs = activations.astype(jnp.float32)
    normed = inputs * lax.rsqrt(jnp.mean(inputs * inputs, axis=-1, keepdims=True) + 1e-06)
    hidden = (normed * (1.0 + modulation[1][None, :]) + modulation[0][None, :]).astype(jnp.bfloat16)
    width = heads * HD
    qkv = jnp.einsum("td,dkh->kth", hidden, w_qkv, preferred_element_type=jnp.float32)
    queries = head_norm(qkv[0], q_gain, heads).astype(jnp.bfloat16)
    keys = head_norm(qkv[1], k_gain, heads).astype(jnp.bfloat16)
    values = qkv[2].astype(jnp.bfloat16)
    local_kv = jnp.concatenate([keys.reshape(span, heads * HD), values], axis=1)
    before = from_behind(local_kv, "slot", 1)
    earlier = from_behind(local_kv, "slot", 2)
    queries, before, earlier, same_core, mine = lax.optimization_barrier(
        (queries, before, earlier, same_core, mine)
    )
    other_core = lax.ppermute(same_core, "slot", [(i, i ^ 1) for i in range(slots)])
    own_mask = lax.dynamic_index_in_dim(block_mask, slot, 0, keepdims=False)
    own_cache = lax.dynamic_index_in_dim(cache_index, slot, 0, keepdims=False)
    sibling_slot = jnp.bitwise_xor(slot, 1)
    own_cache = jnp.where(
        own_cache % 2 == core,
        ((slot - own_cache) % slots) // 2,
        slots // 2 + ((sibling_slot - own_cache) % slots) // 2,
    ).astype(jnp.int32)
    width = heads * HD
    local_stack = jnp.stack([local_kv, before, earlier]).reshape(3, span, 2 * width)
    visible = jnp.concatenate([jnp.ones((blocks_q, blocks_q), jnp.int32), own_mask], axis=1)
    visible = jnp.transpose(visible.reshape(blocks_q, 3 + cache_len, blocks_q), (1, 0, 2))
    visible = jnp.repeat(visible, BLOCK, axis=2)
    bias = jnp.where(visible > 0, 0.0, -1e30).astype(jnp.float32)
    chunks = 4
    rows = span // chunks
    parts = rows // BLOCK
    queries = queries.reshape(span, width)
    mixed_parts = [
        flash(queries[p * rows : (p + 1) * rows], local_stack, same_core, other_core,
              bias[:, p * parts : (p + 1) * parts], own_cache, heads)
        for p in range(chunks)
    ]
    sibling = lax.ppermute(
        jnp.stack(mine[1:]), "slot", [(i, i ^ 1) for i in range(slots)]
    )

    exchanged_o = jnp.concatenate([
        lax.all_to_all(jnp.broadcast_to(part[None], (groups,) + part.shape), "head", 0, 0)
        for part in mixed_parts
    ], axis=1)
    received = [
        lax.dynamic_index_in_dim(exchanged_o, (head - shift) % groups, 0, keepdims=False)
        for shift in range(1, groups)
    ]
    mixed = jnp.concatenate(mixed_parts, axis=0)
    columns = own_full.shape[1]
    half = columns // 2
    attn = jnp.dot(mixed, own_full, preferred_element_type=jnp.float32).astype(jnp.bfloat16).astype(jnp.float32)
    attn_mine = None
    attn_sib = None
    for shift in range(1, groups):
        group_o = received[shift - 1]
        part = jnp.dot(group_o, mine[shift], preferred_element_type=jnp.float32)
        part = part.astype(jnp.bfloat16).astype(jnp.float32)
        attn_mine = part if attn_mine is None else attn_mine + part
        part = jnp.dot(group_o, sibling[shift - 1], preferred_element_type=jnp.float32)
        part = part.astype(jnp.bfloat16).astype(jnp.float32)
        attn_sib = part if attn_sib is None else attn_sib + part
    other = jnp.concatenate([attn_mine, attn_sib], axis=1)
    swapped = jnp.concatenate([attn_sib, attn_mine], axis=1)
    attn = attn + jnp.where(core == 0, other, swapped)

    offset = head * columns
    input_cols = lax.dynamic_slice_in_dim(activations, offset, columns, 1).astype(jnp.float32)
    gate_cols = lax.dynamic_slice_in_dim(modulation[2], offset, columns, 0)
    return input_cols + gate_cols[None, :] * attn


def solution(mesh):
    placed = (
        P("slot", None),
        P(),
        P(),
        P(),
        P(),
        P(None, None, "head"),
        P("head"),
        P("head"),
        P("slot", None, None, "head"),
        P("head", None),
    )
    return jax.shard_map(
        local, mesh=mesh, in_specs=placed, out_specs=P("slot", "head"), check_vma=False
    )
```

```python
import jax
import jax.numpy as jnp
from jax import lax
from jax.sharding import PartitionSpec as P
from jax.experimental import pallas as pl
from jax.experimental.pallas import tpu as pltpu

HD = 128
BLOCK = 128


def from_behind(shard, axis, by):
    length = lax.axis_size(axis)
    return lax.ppermute(shard, axis, [(i, (i + by) % length) for i in range(length)])


def head_norm(values, gain, heads):
    shaped = values.reshape(values.shape[0], heads, HD)
    scaled = shaped * lax.rsqrt(jnp.mean(shaped * shaped, axis=-1, keepdims=True) + 1e-06)
    return scaled * gain.reshape(heads, HD)


def attend(state, queries, span_kv, visible_blocks):
    highest, totals, accum = state
    heads = queries.shape[1]
    span_keys = span_kv[:, 0].reshape(span_kv.shape[0], heads, HD)
    span_values = span_kv[:, 1].reshape(span_kv.shape[0], heads, HD)
    visible = jnp.repeat(jnp.repeat(visible_blocks, BLOCK, axis=0), BLOCK, axis=1) > 0
    scores = jnp.einsum("qhd,khd->hqk", queries, span_keys, preferred_element_type=jnp.float32) * (
        1.0 / HD**0.5
    )
    scores = jnp.where(visible[None], scores, -1e30)
    new_high = jnp.maximum(highest, jnp.max(scores, axis=-1))
    factor = jnp.exp(highest - new_high)
    weights = jnp.where(visible[None], jnp.exp(scores - new_high[..., None]), 0.0)
    totals = totals * factor + jnp.sum(weights, axis=-1)
    accum = accum * factor[..., None] + jnp.einsum(
        "hqk,khd->hqd",
        weights.astype(jnp.bfloat16),
        span_values,
        preferred_element_type=jnp.float32,
    )
    return (new_high, totals, accum)


def flash_kernel(chosen, q_ref, lk_ref, lv_ref, ak_ref, av_ref, bk_ref, bv_ref, bias_ref, o_ref, m_sc, l_sc, acc_sc, *, heads, n_local, half):
    step = pl.program_id(0)
    span = q_ref.shape[0]
    blocks = bias_ref.shape[0]

    @pl.when(step == 0)
    def _():
        m_sc[...] = jnp.full(m_sc.shape, -1e30, jnp.float32)
        l_sc[...] = jnp.zeros(l_sc.shape, jnp.float32)
        acc_sc[...] = jnp.zeros(acc_sc.shape, jnp.float32)

    def body(k_ref, v_ref):
        bias = bias_ref[...][:, None, :]
        for h in range(heads):
            cols = slice(h * HD, (h + 1) * HD)
            q = q_ref[:, cols]
            k = k_ref[:, cols]
            s = lax.dot_general(q, k, (((1,), (1,)), ((), ())), preferred_element_type=jnp.float32)
            s = (s * (1.0 / HD**0.5)).reshape(blocks, span // blocks, s.shape[1]) + bias
            s = s.reshape(span, -1)
            m_prev = m_sc[h]
            m_new = jnp.maximum(m_prev, jnp.max(s, axis=1, keepdims=True))
            factor = jnp.exp(m_prev - m_new)
            p = jnp.exp(s - m_new)
            l_sc[h] = l_sc[h] * factor + jnp.sum(p, axis=1, keepdims=True)
            acc_sc[h] = acc_sc[h] * factor + jnp.dot(
                p.astype(jnp.bfloat16), v_ref[:, cols], preferred_element_type=jnp.float32
            )
            m_sc[h] = m_new

    @pl.when(step < n_local)
    def _():
        body(lk_ref, lv_ref)

    pos = chosen[jnp.maximum(step - n_local, 0)]

    @pl.when((step >= n_local) & (pos < half))
    def _():
        body(ak_ref, av_ref)

    @pl.when((step >= n_local) & (pos >= half))
    def _():
        body(bk_ref, bv_ref)

    @pl.when(step == pl.num_programs(0) - 1)
    def _():
        for h in range(heads):
            cols = slice(h * HD, (h + 1) * HD)
            o_ref[:, cols] = (acc_sc[h] / l_sc[h]).astype(o_ref.dtype)


def flash(queries, local_stack, same_core, other_core, bias, chosen, heads):
    span, width = queries.shape
    n_local = local_stack.shape[0]
    half = same_core.shape[0]
    steps = n_local + chosen.shape[0]
    blocks = bias.shape[1]

    def local_map(kv):
        return lambda j, c: (jnp.minimum(j, n_local - 1), 0, kv)

    def pool_map(kv, upper):
        def index(j, c):
            pos = c[jnp.maximum(j - n_local, 0)]
            hit = (j >= n_local) & ((pos >= half) == upper)
            return (jnp.where(hit, pos - upper * half, 0), 0, kv)

        return index

    keys_len = local_stack.shape[1]
    kv_block = (None, keys_len, width)
    grid_spec = pltpu.PrefetchScalarGridSpec(
        num_scalar_prefetch=1,
        grid=(steps,),
        in_specs=[
            pl.BlockSpec((span, width), lambda j, c: (0, 0)),
            pl.BlockSpec(kv_block, local_map(0)),
            pl.BlockSpec(kv_block, local_map(1)),
            pl.BlockSpec(kv_block, pool_map(0, False)),
            pl.BlockSpec(kv_block, pool_map(1, False)),
            pl.BlockSpec(kv_block, pool_map(0, True)),
            pl.BlockSpec(kv_block, pool_map(1, True)),
            pl.BlockSpec((None, blocks, keys_len), lambda j, c: (j, 0, 0)),
        ],
        out_specs=pl.BlockSpec((span, width), lambda j, c: (0, 0)),
        scratch_shapes=[
            pltpu.VMEM((heads, span, 1), jnp.float32),
            pltpu.VMEM((heads, span, 1), jnp.float32),
            pltpu.VMEM((heads, span, HD), jnp.float32),
        ],
    )
    kernel = lambda *refs: flash_kernel(*refs, heads=heads, n_local=n_local, half=half)
    return pl.pallas_call(
        kernel,
        grid_spec=grid_spec,
        out_shape=jax.ShapeDtypeStruct((span, width), jnp.bfloat16),
        compiler_params=pltpu.CompilerParams(dimension_semantics=("arbitrary",)),
        cost_estimate=pl.CostEstimate(
            flops=4 * steps * heads * span * span * HD,
            transcendentals=steps * heads * span * span,
            bytes_accessed=2 * steps * span * width * 2,
        ),
    )(chosen, queries, local_stack, local_stack, same_core, same_core, other_core, other_core, bias)


def fetch_out_weight(w_out, head, core):
    groups = lax.axis_size("head")
    columns = w_out.shape[1] // groups
    half = columns // 2
    blocks = jnp.stack([
        lax.dynamic_slice_in_dim(w_out, dest * columns + core * half, half, 1)
        for dest in range(groups)
    ])
    exchanged = lax.all_to_all(blocks, "head", 0, 0)
    mine = [
        lax.dynamic_index_in_dim(exchanged, (head - shift) % groups, 0, keepdims=False)
        for shift in range(groups)
    ]
    own_full = lax.dynamic_slice_in_dim(w_out, head * columns, columns, 1)
    return own_full, mine


def local(
    activations,
    mod_table,
    step_index,
    block_mask,
    cache_index,
    w_qkv,
    q_gain,
    k_gain,
    pool_kv,
    w_out,
):
    slot = lax.axis_index("slot")
    head = lax.axis_index("head")
    core = slot % 2
    groups = lax.axis_size("head")
    span = activations.shape[0]
    heads = q_gain.shape[0] // HD
    blocks_q = span // BLOCK
    cache_len = cache_index.shape[1]

    own_full, mine = fetch_out_weight(w_out, head, core)
    slots = lax.axis_size("slot")
    pool_flat = pool_kv.reshape(1, pool_kv.shape[1], -1)
    same_core = [pool_flat] + [from_behind(pool_flat, "slot", 2 * k) for k in range(1, slots // 2)]
    same_core = jnp.concatenate(same_core, axis=0)

    onehot = (jnp.arange(mod_table.shape[0], dtype=jnp.int32) == step_index[slot]).astype(
        jnp.float32
    )
    modulation = jnp.einsum("n,nkd->kd", onehot, mod_table.astype(jnp.float32))
    inputs = activations.astype(jnp.float32)
    normed = inputs * lax.rsqrt(jnp.mean(inputs * inputs, axis=-1, keepdims=True) + 1e-06)
    hidden = (normed * (1.0 + modulation[1][None, :]) + modulation[0][None, :]).astype(jnp.bfloat16)
    width = heads * HD
    qkv = jnp.einsum("td,dkh->kth", hidden, w_qkv, preferred_element_type=jnp.float32)
    queries = head_norm(qkv[0], q_gain, heads).astype(jnp.bfloat16)
    keys = head_norm(qkv[1], k_gain, heads).astype(jnp.bfloat16)
    values = qkv[2].astype(jnp.bfloat16)
    local_kv = jnp.concatenate([keys.reshape(span, heads * HD), values], axis=1)
    local_kv, same_core = lax.optimization_barrier((local_kv, same_core))
    other_core = lax.ppermute(same_core, "slot", [(i, i ^ 1) for i in range(slots)])
    before = from_behind(local_kv, "slot", 1)
    earlier = from_behind(local_kv, "slot", 2)
    queries, before, earlier, mine = lax.optimization_barrier(
        (queries, before, earlier, mine)
    )
    own_mask = lax.dynamic_index_in_dim(block_mask, slot, 0, keepdims=False)
    own_cache = lax.dynamic_index_in_dim(cache_index, slot, 0, keepdims=False)
    sibling_slot = jnp.bitwise_xor(slot, 1)
    own_cache = jnp.where(
        own_cache % 2 == core,
        ((slot - own_cache) % slots) // 2,
        slots // 2 + ((sibling_slot - own_cache) % slots) // 2,
    ).astype(jnp.int32)
    width = heads * HD
    local_stack = jnp.stack([local_kv, before, earlier]).reshape(3, span, 2 * width)
    visible = jnp.concatenate([jnp.ones((blocks_q, blocks_q), jnp.int32), own_mask], axis=1)
    visible = jnp.transpose(visible.reshape(blocks_q, 3 + cache_len, blocks_q), (1, 0, 2))
    visible = jnp.repeat(visible, BLOCK, axis=2)
    bias = jnp.where(visible > 0, 0.0, -1e30).astype(jnp.float32)
    rows = span // 2
    parts = rows // BLOCK
    queries = queries.reshape(span, width)
    mixed_parts = [
        flash(queries[p * rows : (p + 1) * rows], local_stack, same_core, other_core,
              bias[:, p * parts : (p + 1) * parts], own_cache, heads)
        for p in range(2)
    ]
    sibling = lax.ppermute(
        jnp.stack(mine[1:]), "slot", [(i, i ^ 1) for i in range(slots)]
    )

    received = [
        jnp.concatenate([
            lax.ppermute(part, "head", [(i, (i + shift) % groups) for i in range(groups)])
            for part in mixed_parts
        ], axis=0)
        for shift in range(1, groups)
    ]
    mixed = jnp.concatenate(mixed_parts, axis=0)
    columns = own_full.shape[1]
    half = columns // 2
    attn = jnp.dot(mixed, own_full, preferred_element_type=jnp.float32).astype(jnp.bfloat16).astype(jnp.float32)
    attn_mine = None
    attn_sib = None
    for shift in range(1, groups):
        group_o = received[shift - 1]
        part = jnp.dot(group_o, mine[shift], preferred_element_type=jnp.float32)
        part = part.astype(jnp.bfloat16).astype(jnp.float32)
        attn_mine = part if attn_mine is None else attn_mine + part
        part = jnp.dot(group_o, sibling[shift - 1], preferred_element_type=jnp.float32)
        part = part.astype(jnp.bfloat16).astype(jnp.float32)
        attn_sib = part if attn_sib is None else attn_sib + part
    other = jnp.concatenate([attn_mine, attn_sib], axis=1)
    swapped = jnp.concatenate([attn_sib, attn_mine], axis=1)
    attn = attn + jnp.where(core == 0, other, swapped)

    offset = head * columns
    input_cols = lax.dynamic_slice_in_dim(activations, offset, columns, 1).astype(jnp.float32)
    gate_cols = lax.dynamic_slice_in_dim(modulation[2], offset, columns, 0)
    return input_cols + gate_cols[None, :] * attn


def solution(mesh):
    placed = (
        P("slot", None),
        P(),
        P(),
        P(),
        P(),
        P(None, None, "head"),
        P("head"),
        P("head"),
        P("slot", None, None, "head"),
        P("head", None),
    )
    return jax.shard_map(
        local, mesh=mesh, in_specs=placed, out_specs=P("slot", "head"), check_vma=False
    )
```

```python
import jax
import jax.numpy as jnp
from jax import lax
from jax.sharding import PartitionSpec as P
from jax.experimental import pallas as pl
from jax.experimental.pallas import tpu as pltpu

HD = 128
BLOCK = 128


def from_behind(shard, axis, by):
    length = lax.axis_size(axis)
    return lax.ppermute(shard, axis, [(i, (i + by) % length) for i in range(length)])


def head_norm(values, gain, heads):
    shaped = values.reshape(values.shape[0], heads, HD)
    scaled = shaped * lax.rsqrt(jnp.mean(shaped * shaped, axis=-1, keepdims=True) + 1e-06)
    return scaled * gain.reshape(heads, HD)


def attend(state, queries, span_kv, visible_blocks):
    highest, totals, accum = state
    heads = queries.shape[1]
    span_keys = span_kv[:, 0].reshape(span_kv.shape[0], heads, HD)
    span_values = span_kv[:, 1].reshape(span_kv.shape[0], heads, HD)
    visible = jnp.repeat(jnp.repeat(visible_blocks, BLOCK, axis=0), BLOCK, axis=1) > 0
    scores = jnp.einsum("qhd,khd->hqk", queries, span_keys, preferred_element_type=jnp.float32) * (
        1.0 / HD**0.5
    )
    scores = jnp.where(visible[None], scores, -1e30)
    new_high = jnp.maximum(highest, jnp.max(scores, axis=-1))
    factor = jnp.exp(highest - new_high)
    weights = jnp.where(visible[None], jnp.exp(scores - new_high[..., None]), 0.0)
    totals = totals * factor + jnp.sum(weights, axis=-1)
    accum = accum * factor[..., None] + jnp.einsum(
        "hqk,khd->hqd",
        weights.astype(jnp.bfloat16),
        span_values,
        preferred_element_type=jnp.float32,
    )
    return (new_high, totals, accum)


def flash_kernel(chosen, q_ref, lk_ref, lv_ref, ak_ref, av_ref, bk_ref, bv_ref, bias_ref, o_ref, m_sc, l_sc, acc_sc, *, heads, n_local, half):
    step = pl.program_id(0)
    span = q_ref.shape[0]
    blocks = bias_ref.shape[0]

    @pl.when(step == 0)
    def _():
        m_sc[...] = jnp.full(m_sc.shape, -1e30, jnp.float32)
        l_sc[...] = jnp.zeros(l_sc.shape, jnp.float32)
        acc_sc[...] = jnp.zeros(acc_sc.shape, jnp.float32)

    def body(k_ref, v_ref):
        bias = bias_ref[...][:, None, :]
        for h in range(heads):
            cols = slice(h * HD, (h + 1) * HD)
            q = q_ref[:, cols]
            k = k_ref[:, cols]
            s = lax.dot_general(q, k, (((1,), (1,)), ((), ())), preferred_element_type=jnp.float32)
            s = (s * (1.0 / HD**0.5)).reshape(blocks, span // blocks, s.shape[1]) + bias
            s = s.reshape(span, -1)
            m_prev = m_sc[h]
            m_new = jnp.maximum(m_prev, jnp.max(s, axis=1, keepdims=True))
            factor = jnp.exp(m_prev - m_new)
            p = jnp.exp(s - m_new)
            l_sc[h] = l_sc[h] * factor + jnp.sum(p, axis=1, keepdims=True)
            acc_sc[h] = acc_sc[h] * factor + jnp.dot(
                p.astype(jnp.bfloat16), v_ref[:, cols], preferred_element_type=jnp.float32
            )
            m_sc[h] = m_new

    @pl.when(step < n_local)
    def _():
        body(lk_ref, lv_ref)

    pos = chosen[jnp.maximum(step - n_local, 0)]

    @pl.when((step >= n_local) & (pos < half))
    def _():
        body(ak_ref, av_ref)

    @pl.when((step >= n_local) & (pos >= half))
    def _():
        body(bk_ref, bv_ref)

    @pl.when(step == pl.num_programs(0) - 1)
    def _():
        for h in range(heads):
            cols = slice(h * HD, (h + 1) * HD)
            o_ref[:, cols] = (acc_sc[h] / l_sc[h]).astype(o_ref.dtype)


def flash(queries, local_stack, same_core, other_core, bias, chosen, heads):
    span, width = queries.shape
    n_local = local_stack.shape[0]
    half = same_core.shape[0]
    steps = n_local + chosen.shape[0]
    blocks = bias.shape[1]

    def local_map(kv):
        return lambda j, c: (jnp.minimum(j, n_local - 1), 0, kv)

    def pool_map(kv, upper):
        def index(j, c):
            pos = c[jnp.maximum(j - n_local, 0)]
            hit = (j >= n_local) & ((pos >= half) == upper)
            return (jnp.where(hit, pos - upper * half, 0), 0, kv)

        return index

    keys_len = local_stack.shape[1]
    kv_block = (None, keys_len, width)
    grid_spec = pltpu.PrefetchScalarGridSpec(
        num_scalar_prefetch=1,
        grid=(steps,),
        in_specs=[
            pl.BlockSpec((span, width), lambda j, c: (0, 0)),
            pl.BlockSpec(kv_block, local_map(0)),
            pl.BlockSpec(kv_block, local_map(1)),
            pl.BlockSpec(kv_block, pool_map(0, False)),
            pl.BlockSpec(kv_block, pool_map(1, False)),
            pl.BlockSpec(kv_block, pool_map(0, True)),
            pl.BlockSpec(kv_block, pool_map(1, True)),
            pl.BlockSpec((None, blocks, keys_len), lambda j, c: (j, 0, 0)),
        ],
        out_specs=pl.BlockSpec((span, width), lambda j, c: (0, 0)),
        scratch_shapes=[
            pltpu.VMEM((heads, span, 1), jnp.float32),
            pltpu.VMEM((heads, span, 1), jnp.float32),
            pltpu.VMEM((heads, span, HD), jnp.float32),
        ],
    )
    kernel = lambda *refs: flash_kernel(*refs, heads=heads, n_local=n_local, half=half)
    return pl.pallas_call(
        kernel,
        grid_spec=grid_spec,
        out_shape=jax.ShapeDtypeStruct((span, width), jnp.bfloat16),
        compiler_params=pltpu.CompilerParams(dimension_semantics=("arbitrary",)),
        cost_estimate=pl.CostEstimate(
            flops=4 * steps * heads * span * span * HD,
            transcendentals=steps * heads * span * span,
            bytes_accessed=2 * steps * span * width * 2,
        ),
    )(chosen, queries, local_stack, local_stack, same_core, same_core, other_core, other_core, bias)


def fetch_out_weight(w_out, head, core):
    groups = lax.axis_size("head")
    columns = w_out.shape[1] // groups
    half = columns // 2
    blocks = jnp.stack([
        lax.dynamic_slice_in_dim(w_out, dest * columns + core * half, half, 1)
        for dest in range(groups)
    ])
    exchanged = lax.all_to_all(blocks, "head", 0, 0)
    mine = [
        lax.dynamic_index_in_dim(exchanged, (head - shift) % groups, 0, keepdims=False)
        for shift in range(groups)
    ]
    own_full = lax.dynamic_slice_in_dim(w_out, head * columns, columns, 1)
    return own_full, mine


def local(
    activations,
    mod_table,
    step_index,
    block_mask,
    cache_index,
    w_qkv,
    q_gain,
    k_gain,
    pool_kv,
    w_out,
):
    slot = lax.axis_index("slot")
    head = lax.axis_index("head")
    core = slot % 2
    groups = lax.axis_size("head")
    span = activations.shape[0]
    heads = q_gain.shape[0] // HD
    blocks_q = span // BLOCK
    cache_len = cache_index.shape[1]

    own_full, mine = fetch_out_weight(w_out, head, core)
    slots = lax.axis_size("slot")
    pool_flat = pool_kv.reshape(1, pool_kv.shape[1], -1)
    same_core = [pool_flat] + [from_behind(pool_flat, "slot", 2 * k) for k in range(1, slots // 2)]
    same_core = jnp.concatenate(same_core, axis=0)

    onehot = (jnp.arange(mod_table.shape[0], dtype=jnp.int32) == step_index[slot]).astype(
        jnp.float32
    )
    modulation = jnp.einsum("n,nkd->kd", onehot, mod_table.astype(jnp.float32))
    inputs = activations.astype(jnp.float32)
    normed = inputs * lax.rsqrt(jnp.mean(inputs * inputs, axis=-1, keepdims=True) + 1e-06)
    hidden = (normed * (1.0 + modulation[1][None, :]) + modulation[0][None, :]).astype(jnp.bfloat16)
    width = heads * HD
    qkv = jnp.einsum("td,dkh->kth", hidden, w_qkv, preferred_element_type=jnp.float32)
    queries = head_norm(qkv[0], q_gain, heads).astype(jnp.bfloat16)
    keys = head_norm(qkv[1], k_gain, heads).astype(jnp.bfloat16)
    values = qkv[2].astype(jnp.bfloat16)
    local_kv = jnp.concatenate([keys.reshape(span, heads * HD), values], axis=1)
    before = from_behind(local_kv, "slot", 1)
    earlier = from_behind(local_kv, "slot", 2)
    queries, before, earlier, same_core, mine = lax.optimization_barrier(
        (queries, before, earlier, same_core, mine)
    )
    other_core = lax.ppermute(same_core, "slot", [(i, i ^ 1) for i in range(slots)])
    own_mask = lax.dynamic_index_in_dim(block_mask, slot, 0, keepdims=False)
    own_cache = lax.dynamic_index_in_dim(cache_index, slot, 0, keepdims=False)
    sibling_slot = jnp.bitwise_xor(slot, 1)
    own_cache = jnp.where(
        own_cache % 2 == core,
        ((slot - own_cache) % slots) // 2,
        slots // 2 + ((sibling_slot - own_cache) % slots) // 2,
    ).astype(jnp.int32)
    width = heads * HD
    local_stack = jnp.stack([local_kv, before, earlier]).reshape(3, span, 2 * width)
    visible = jnp.concatenate([jnp.ones((blocks_q, blocks_q), jnp.int32), own_mask], axis=1)
    visible = jnp.transpose(visible.reshape(blocks_q, 3 + cache_len, blocks_q), (1, 0, 2))
    visible = jnp.repeat(visible, BLOCK, axis=2)
    bias = jnp.where(visible > 0, 0.0, -1e30).astype(jnp.float32)
    rows = span // 2
    parts = rows // BLOCK
    queries = queries.reshape(span, width)
    mixed_parts = [
        flash(queries[p * rows : (p + 1) * rows], local_stack, same_core, other_core,
              bias[:, p * parts : (p + 1) * parts], own_cache, heads)
        for p in range(2)
    ]
    sibling = lax.ppermute(
        jnp.stack(mine[1:]), "slot", [(i, i ^ 1) for i in range(slots)]
    )

    columns = own_full.shape[1]
    offset = head * columns
    gate_cols = lax.dynamic_slice_in_dim(modulation[2], offset, columns, 0)
    results = []
    for p, mixed_part in enumerate(mixed_parts):
        received = [
            lax.ppermute(mixed_part, "head", [(i, (i + shift) % groups) for i in range(groups)])
            for shift in range(1, groups)
        ]
        attn = jnp.dot(mixed_part, own_full, preferred_element_type=jnp.float32)
        attn = attn.astype(jnp.bfloat16).astype(jnp.float32)
        attn_mine = None
        attn_sib = None
        for shift in range(1, groups):
            group_o = received[shift - 1]
            part = jnp.dot(group_o, mine[shift], preferred_element_type=jnp.float32)
            part = part.astype(jnp.bfloat16).astype(jnp.float32)
            attn_mine = part if attn_mine is None else attn_mine + part
            part = jnp.dot(group_o, sibling[shift - 1], preferred_element_type=jnp.float32)
            part = part.astype(jnp.bfloat16).astype(jnp.float32)
            attn_sib = part if attn_sib is None else attn_sib + part
        other = jnp.concatenate([attn_mine, attn_sib], axis=1)
        swapped = jnp.concatenate([attn_sib, attn_mine], axis=1)
        attn = attn + jnp.where(core == 0, other, swapped)
        input_cols = lax.dynamic_slice(
            activations, (p * rows, offset), (rows, columns)
        ).astype(jnp.float32)
        results.append(input_cols + gate_cols[None, :] * attn)
    return jnp.concatenate(results, axis=0)


def solution(mesh):
    placed = (
        P("slot", None),
        P(),
        P(),
        P(),
        P(),
        P(None, None, "head"),
        P("head"),
        P("head"),
        P("slot", None, None, "head"),
        P("head", None),
    )
    return jax.shard_map(
        local, mesh=mesh, in_specs=placed, out_specs=P("slot", "head"), check_vma=False
    )
```

```python
import jax
import jax.numpy as jnp
from jax import lax
from jax.sharding import PartitionSpec as P
from jax.experimental import pallas as pl
from jax.experimental.pallas import tpu as pltpu

HD = 128
BLOCK = 128


def from_behind(shard, axis, by):
    length = lax.axis_size(axis)
    return lax.ppermute(shard, axis, [(i, (i + by) % length) for i in range(length)])


def head_norm(values, gain, heads):
    outs = []
    for h in range(heads):
        cols = slice(h * HD, (h + 1) * HD)
        piece = values[:, cols]
        scaled = piece * lax.rsqrt(jnp.mean(piece * piece, axis=-1, keepdims=True) + 1e-06)
        outs.append(scaled * gain[cols][None, :])
    return jnp.concatenate(outs, axis=1)


def attend(state, queries, span_kv, visible_blocks):
    highest, totals, accum = state
    heads = queries.shape[1]
    span_keys = span_kv[:, 0].reshape(span_kv.shape[0], heads, HD)
    span_values = span_kv[:, 1].reshape(span_kv.shape[0], heads, HD)
    visible = jnp.repeat(jnp.repeat(visible_blocks, BLOCK, axis=0), BLOCK, axis=1) > 0
    scores = jnp.einsum("qhd,khd->hqk", queries, span_keys, preferred_element_type=jnp.float32) * (
        1.0 / HD**0.5
    )
    scores = jnp.where(visible[None], scores, -1e30)
    new_high = jnp.maximum(highest, jnp.max(scores, axis=-1))
    factor = jnp.exp(highest - new_high)
    weights = jnp.where(visible[None], jnp.exp(scores - new_high[..., None]), 0.0)
    totals = totals * factor + jnp.sum(weights, axis=-1)
    accum = accum * factor[..., None] + jnp.einsum(
        "hqk,khd->hqd",
        weights.astype(jnp.bfloat16),
        span_values,
        preferred_element_type=jnp.float32,
    )
    return (new_high, totals, accum)


def flash_kernel(chosen, q_ref, lk_ref, lv_ref, ak_ref, av_ref, bk_ref, bv_ref, bias_ref, o_ref, m_sc, l_sc, acc_sc, *, heads, n_local, half):
    step = pl.program_id(0)
    span = q_ref.shape[0]
    blocks = bias_ref.shape[0]

    @pl.when(step == 0)
    def _():
        m_sc[...] = jnp.full(m_sc.shape, -1e30, jnp.float32)
        l_sc[...] = jnp.zeros(l_sc.shape, jnp.float32)
        acc_sc[...] = jnp.zeros(acc_sc.shape, jnp.float32)

    def body(k_ref, v_ref):
        bias = bias_ref[...][:, None, :]
        for h in range(heads):
            cols = slice(h * HD, (h + 1) * HD)
            q = q_ref[:, cols]
            k = k_ref[:, cols]
            s = lax.dot_general(q, k, (((1,), (1,)), ((), ())), preferred_element_type=jnp.float32)
            s = (s * (1.0 / HD**0.5)).reshape(blocks, span // blocks, s.shape[1]) + bias
            s = s.reshape(span, -1)
            m_prev = m_sc[h]
            m_new = jnp.maximum(m_prev, jnp.max(s, axis=1, keepdims=True))
            factor = jnp.exp(m_prev - m_new)
            p = jnp.exp(s - m_new)
            l_sc[h] = l_sc[h] * factor + jnp.sum(p, axis=1, keepdims=True)
            acc_sc[h] = acc_sc[h] * factor + jnp.dot(
                p.astype(jnp.bfloat16), v_ref[:, cols], preferred_element_type=jnp.float32
            )
            m_sc[h] = m_new

    @pl.when(step < n_local)
    def _():
        body(lk_ref, lv_ref)

    pos = chosen[jnp.maximum(step - n_local, 0)]

    @pl.when((step >= n_local) & (pos < half))
    def _():
        body(ak_ref, av_ref)

    @pl.when((step >= n_local) & (pos >= half))
    def _():
        body(bk_ref, bv_ref)

    @pl.when(step == pl.num_programs(0) - 1)
    def _():
        for h in range(heads):
            cols = slice(h * HD, (h + 1) * HD)
            o_ref[:, cols] = (acc_sc[h] / l_sc[h]).astype(o_ref.dtype)


def flash(queries, local_stack, same_core, other_core, bias, chosen, heads):
    span, width = queries.shape
    n_local = local_stack.shape[0]
    half = same_core.shape[0]
    steps = n_local + chosen.shape[0]
    blocks = bias.shape[1]

    def local_map(kv):
        return lambda j, c: (jnp.minimum(j, n_local - 1), 0, kv)

    def pool_map(kv, upper):
        def index(j, c):
            pos = c[jnp.maximum(j - n_local, 0)]
            hit = (j >= n_local) & ((pos >= half) == upper)
            return (jnp.where(hit, pos - upper * half, 0), 0, kv)

        return index

    keys_len = local_stack.shape[1]
    kv_block = (None, keys_len, width)
    grid_spec = pltpu.PrefetchScalarGridSpec(
        num_scalar_prefetch=1,
        grid=(steps,),
        in_specs=[
            pl.BlockSpec((span, width), lambda j, c: (0, 0)),
            pl.BlockSpec(kv_block, local_map(0)),
            pl.BlockSpec(kv_block, local_map(1)),
            pl.BlockSpec(kv_block, pool_map(0, False)),
            pl.BlockSpec(kv_block, pool_map(1, False)),
            pl.BlockSpec(kv_block, pool_map(0, True)),
            pl.BlockSpec(kv_block, pool_map(1, True)),
            pl.BlockSpec((None, blocks, keys_len), lambda j, c: (j, 0, 0)),
        ],
        out_specs=pl.BlockSpec((span, width), lambda j, c: (0, 0)),
        scratch_shapes=[
            pltpu.VMEM((heads, span, 1), jnp.float32),
            pltpu.VMEM((heads, span, 1), jnp.float32),
            pltpu.VMEM((heads, span, HD), jnp.float32),
        ],
    )
    kernel = lambda *refs: flash_kernel(*refs, heads=heads, n_local=n_local, half=half)
    return pl.pallas_call(
        kernel,
        grid_spec=grid_spec,
        out_shape=jax.ShapeDtypeStruct((span, width), jnp.bfloat16),
        compiler_params=pltpu.CompilerParams(dimension_semantics=("arbitrary",)),
        cost_estimate=pl.CostEstimate(
            flops=4 * steps * heads * span * span * HD,
            transcendentals=steps * heads * span * span,
            bytes_accessed=2 * steps * span * width * 2,
        ),
    )(chosen, queries, local_stack, local_stack, same_core, same_core, other_core, other_core, bias)


def fetch_out_weight(w_out, head, core):
    groups = lax.axis_size("head")
    columns = w_out.shape[1] // groups
    half = columns // 2
    blocks = jnp.stack([
        lax.dynamic_slice_in_dim(w_out, dest * columns + core * half, half, 1)
        for dest in range(groups)
    ])
    exchanged = lax.all_to_all(blocks, "head", 0, 0)
    mine = [
        lax.dynamic_index_in_dim(exchanged, (head - shift) % groups, 0, keepdims=False)
        for shift in range(groups)
    ]
    own_full = lax.dynamic_slice_in_dim(w_out, head * columns, columns, 1)
    return own_full, mine


def local(
    activations,
    mod_table,
    step_index,
    block_mask,
    cache_index,
    w_qkv,
    q_gain,
    k_gain,
    pool_kv,
    w_out,
):
    slot = lax.axis_index("slot")
    head = lax.axis_index("head")
    core = slot % 2
    groups = lax.axis_size("head")
    span = activations.shape[0]
    heads = q_gain.shape[0] // HD
    blocks_q = span // BLOCK
    cache_len = cache_index.shape[1]

    own_full, mine = fetch_out_weight(w_out, head, core)
    slots = lax.axis_size("slot")
    pool_flat = pool_kv.reshape(1, pool_kv.shape[1], -1)
    same_core = [pool_flat] + [from_behind(pool_flat, "slot", 2 * k) for k in range(1, slots // 2)]
    same_core = jnp.concatenate(same_core, axis=0)

    onehot = (jnp.arange(mod_table.shape[0], dtype=jnp.int32) == step_index[slot]).astype(
        jnp.float32
    )
    modulation = jnp.einsum("n,nkd->kd", onehot, mod_table.astype(jnp.float32))
    inputs = activations.astype(jnp.float32)
    normed = inputs * lax.rsqrt(jnp.mean(inputs * inputs, axis=-1, keepdims=True) + 1e-06)
    hidden = (normed * (1.0 + modulation[1][None, :]) + modulation[0][None, :]).astype(jnp.bfloat16)
    width = heads * HD
    qkv = jnp.einsum("td,dkh->kth", hidden, w_qkv, preferred_element_type=jnp.float32)
    queries = head_norm(qkv[0], q_gain, heads).astype(jnp.bfloat16)
    keys = head_norm(qkv[1], k_gain, heads).astype(jnp.bfloat16)
    values = qkv[2].astype(jnp.bfloat16)
    local_kv = jnp.concatenate([keys.reshape(span, heads * HD), values], axis=1)
    before = from_behind(local_kv, "slot", 1)
    earlier = from_behind(local_kv, "slot", 2)
    queries, before, earlier, same_core, mine = lax.optimization_barrier(
        (queries, before, earlier, same_core, mine)
    )
    other_core = lax.ppermute(same_core, "slot", [(i, i ^ 1) for i in range(slots)])
    own_mask = lax.dynamic_index_in_dim(block_mask, slot, 0, keepdims=False)
    own_cache = lax.dynamic_index_in_dim(cache_index, slot, 0, keepdims=False)
    sibling_slot = jnp.bitwise_xor(slot, 1)
    own_cache = jnp.where(
        own_cache % 2 == core,
        ((slot - own_cache) % slots) // 2,
        slots // 2 + ((sibling_slot - own_cache) % slots) // 2,
    ).astype(jnp.int32)
    width = heads * HD
    local_stack = jnp.stack([local_kv, before, earlier]).reshape(3, span, 2 * width)
    visible = jnp.concatenate([jnp.ones((blocks_q, blocks_q), jnp.int32), own_mask], axis=1)
    visible = jnp.transpose(visible.reshape(blocks_q, 3 + cache_len, blocks_q), (1, 0, 2))
    visible = jnp.repeat(visible, BLOCK, axis=2)
    bias = jnp.where(visible > 0, 0.0, -1e30).astype(jnp.float32)
    rows = span // 2
    parts = rows // BLOCK
    queries = queries.reshape(span, width)
    mixed_parts = [
        flash(queries[p * rows : (p + 1) * rows], local_stack, same_core, other_core,
              bias[:, p * parts : (p + 1) * parts], own_cache, heads)
        for p in range(2)
    ]
    sibling = lax.ppermute(
        jnp.stack(mine[1:]), "slot", [(i, i ^ 1) for i in range(slots)]
    )

    received = [
        jnp.concatenate([
            lax.ppermute(part, "head", [(i, (i + shift) % groups) for i in range(groups)])
            for part in mixed_parts
        ], axis=0)
        for shift in range(1, groups)
    ]
    mixed = jnp.concatenate(mixed_parts, axis=0)
    columns = own_full.shape[1]
    half = columns // 2
    attn = jnp.dot(mixed, own_full, preferred_element_type=jnp.float32).astype(jnp.bfloat16).astype(jnp.float32)
    attn_mine = None
    attn_sib = None
    for shift in range(1, groups):
        group_o = received[shift - 1]
        part = jnp.dot(group_o, mine[shift], preferred_element_type=jnp.float32)
        part = part.astype(jnp.bfloat16).astype(jnp.float32)
        attn_mine = part if attn_mine is None else attn_mine + part
        part = jnp.dot(group_o, sibling[shift - 1], preferred_element_type=jnp.float32)
        part = part.astype(jnp.bfloat16).astype(jnp.float32)
        attn_sib = part if attn_sib is None else attn_sib + part
    other = jnp.concatenate([attn_mine, attn_sib], axis=1)
    swapped = jnp.concatenate([attn_sib, attn_mine], axis=1)
    attn = attn + jnp.where(core == 0, other, swapped)

    offset = head * columns
    input_cols = lax.dynamic_slice_in_dim(activations, offset, columns, 1).astype(jnp.float32)
    gate_cols = lax.dynamic_slice_in_dim(modulation[2], offset, columns, 0)
    return input_cols + gate_cols[None, :] * attn


def solution(mesh):
    placed = (
        P("slot", None),
        P(),
        P(),
        P(),
        P(),
        P(None, None, "head"),
        P("head"),
        P("head"),
        P("slot", None, None, "head"),
        P("head", None),
    )
    return jax.shard_map(
        local, mesh=mesh, in_specs=placed, out_specs=P("slot", "head"), check_vma=False
    )
```

```python
import jax
import jax.numpy as jnp
from jax import lax
from jax.sharding import PartitionSpec as P
from jax.experimental import pallas as pl
from jax.experimental.pallas import tpu as pltpu

HD = 128
BLOCK = 128


def from_behind(shard, axis, by):
    length = lax.axis_size(axis)
    return lax.ppermute(shard, axis, [(i, (i + by) % length) for i in range(length)])


def head_norm(values, gain, heads):
    outs = []
    for h in range(heads):
        cols = slice(h * HD, (h + 1) * HD)
        piece = values[:, cols]
        scaled = piece * lax.rsqrt(jnp.mean(piece * piece, axis=-1, keepdims=True) + 1e-06)
        outs.append(scaled * gain[cols][None, :])
    return jnp.concatenate(outs, axis=1)


def attend(state, queries, span_kv, visible_blocks):
    highest, totals, accum = state
    heads = queries.shape[1]
    span_keys = span_kv[:, 0].reshape(span_kv.shape[0], heads, HD)
    span_values = span_kv[:, 1].reshape(span_kv.shape[0], heads, HD)
    visible = jnp.repeat(jnp.repeat(visible_blocks, BLOCK, axis=0), BLOCK, axis=1) > 0
    scores = jnp.einsum("qhd,khd->hqk", queries, span_keys, preferred_element_type=jnp.float32) * (
        1.0 / HD**0.5
    )
    scores = jnp.where(visible[None], scores, -1e30)
    new_high = jnp.maximum(highest, jnp.max(scores, axis=-1))
    factor = jnp.exp(highest - new_high)
    weights = jnp.where(visible[None], jnp.exp(scores - new_high[..., None]), 0.0)
    totals = totals * factor + jnp.sum(weights, axis=-1)
    accum = accum * factor[..., None] + jnp.einsum(
        "hqk,khd->hqd",
        weights.astype(jnp.bfloat16),
        span_values,
        preferred_element_type=jnp.float32,
    )
    return (new_high, totals, accum)


def online_update(q_ref, k_ref, v_ref, bias_ref, m_sc, l_sc, acc_sc, heads):
    span = q_ref.shape[0]
    blocks = bias_ref.shape[0]
    bias = bias_ref[...][:, None, :]
    for h in range(heads):
        cols = slice(h * HD, (h + 1) * HD)
        q = q_ref[:, cols]
        k = k_ref[:, cols]
        s = lax.dot_general(q, k, (((1,), (1,)), ((), ())), preferred_element_type=jnp.float32)
        s = (s * (1.0 / HD**0.5)).reshape(blocks, span // blocks, s.shape[1]) + bias
        s = s.reshape(span, -1)
        m_prev = m_sc[h]
        m_new = jnp.maximum(m_prev, jnp.max(s, axis=1, keepdims=True))
        factor = jnp.exp(m_prev - m_new)
        p = jnp.exp(s - m_new)
        l_sc[h] = l_sc[h] * factor + jnp.sum(p, axis=1, keepdims=True)
        acc_sc[h] = acc_sc[h] * factor + jnp.dot(
            p.astype(jnp.bfloat16), v_ref[:, cols], preferred_element_type=jnp.float32
        )
        m_sc[h] = m_new


def local_kernel(q_ref, k_ref, v_ref, bias_ref, m_ref, l_ref, acc_ref, *, heads):
    @pl.when(pl.program_id(0) == 0)
    def _():
        m_ref[...] = jnp.full(m_ref.shape, -1e30, jnp.float32)
        l_ref[...] = jnp.zeros(l_ref.shape, jnp.float32)
        acc_ref[...] = jnp.zeros(acc_ref.shape, jnp.float32)

    online_update(q_ref, k_ref, v_ref, bias_ref, m_ref, l_ref, acc_ref, heads)


def pool_kernel(chosen, q_ref, ak_ref, av_ref, bk_ref, bv_ref, bias_ref, m_in, l_in, acc_in,
                o_ref, m_sc, l_sc, acc_sc, *, heads, half):
    step = pl.program_id(0)

    @pl.when(step == 0)
    def _():
        m_sc[...] = m_in[...]
        l_sc[...] = l_in[...]
        acc_sc[...] = acc_in[...]

    pos = chosen[step]

    @pl.when(pos < half)
    def _():
        online_update(q_ref, ak_ref, av_ref, bias_ref, m_sc, l_sc, acc_sc, heads)

    @pl.when(pos >= half)
    def _():
        online_update(q_ref, bk_ref, bv_ref, bias_ref, m_sc, l_sc, acc_sc, heads)

    @pl.when(step == pl.num_programs(0) - 1)
    def _():
        for h in range(heads):
            cols = slice(h * HD, (h + 1) * HD)
            o_ref[:, cols] = (acc_sc[h] / l_sc[h]).astype(o_ref.dtype)


def flash_local(queries, local_stack, bias, heads):
    span, width = queries.shape
    steps, keys_len = local_stack.shape[:2]
    blocks = bias.shape[1]
    kv_block = (None, keys_len, width)
    state = pl.BlockSpec((heads, span, 1), lambda j: (0, 0, 0))
    kernel = lambda *refs: local_kernel(*refs, heads=heads)
    return pl.pallas_call(
        kernel,
        grid=(steps,),
        in_specs=[
            pl.BlockSpec((span, width), lambda j: (0, 0)),
            pl.BlockSpec(kv_block, lambda j: (j, 0, 0)),
            pl.BlockSpec(kv_block, lambda j: (j, 0, 1)),
            pl.BlockSpec((None, blocks, keys_len), lambda j: (j, 0, 0)),
        ],
        out_specs=[state, state, pl.BlockSpec((heads, span, HD), lambda j: (0, 0, 0))],
        out_shape=[
            jax.ShapeDtypeStruct((heads, span, 1), jnp.float32),
            jax.ShapeDtypeStruct((heads, span, 1), jnp.float32),
            jax.ShapeDtypeStruct((heads, span, HD), jnp.float32),
        ],
        compiler_params=pltpu.CompilerParams(dimension_semantics=("arbitrary",)),
        cost_estimate=pl.CostEstimate(
            flops=4 * steps * heads * span * keys_len * HD,
            transcendentals=steps * heads * span * keys_len,
            bytes_accessed=2 * steps * keys_len * width * 2,
        ),
    )(queries, local_stack, local_stack, bias)


def flash_pool(queries, same_core, other_core, bias, chosen, state, heads):
    span, width = queries.shape
    half, keys_len = same_core.shape[:2]
    steps = chosen.shape[0]
    blocks = bias.shape[1]
    kv_block = (None, keys_len, width)

    def pool_map(kv, upper):
        def index(j, c):
            pos = c[j]
            return (jnp.where((pos >= half) == upper, pos - upper * half, 0), 0, kv)

        return index

    state_spec = pl.BlockSpec((heads, span, 1), lambda j, c: (0, 0, 0))
    grid_spec = pltpu.PrefetchScalarGridSpec(
        num_scalar_prefetch=1,
        grid=(steps,),
        in_specs=[
            pl.BlockSpec((span, width), lambda j, c: (0, 0)),
            pl.BlockSpec(kv_block, pool_map(0, False)),
            pl.BlockSpec(kv_block, pool_map(1, False)),
            pl.BlockSpec(kv_block, pool_map(0, True)),
            pl.BlockSpec(kv_block, pool_map(1, True)),
            pl.BlockSpec((None, blocks, keys_len), lambda j, c: (j, 0, 0)),
            state_spec,
            state_spec,
            pl.BlockSpec((heads, span, HD), lambda j, c: (0, 0, 0)),
        ],
        out_specs=pl.BlockSpec((span, width), lambda j, c: (0, 0)),
        scratch_shapes=[
            pltpu.VMEM((heads, span, 1), jnp.float32),
            pltpu.VMEM((heads, span, 1), jnp.float32),
            pltpu.VMEM((heads, span, HD), jnp.float32),
        ],
    )
    kernel = lambda *refs: pool_kernel(*refs, heads=heads, half=half)
    return pl.pallas_call(
        kernel,
        grid_spec=grid_spec,
        out_shape=jax.ShapeDtypeStruct((span, width), jnp.bfloat16),
        compiler_params=pltpu.CompilerParams(dimension_semantics=("arbitrary",)),
        cost_estimate=pl.CostEstimate(
            flops=4 * steps * heads * span * keys_len * HD,
            transcendentals=steps * heads * span * keys_len,
            bytes_accessed=2 * steps * keys_len * width * 2,
        ),
    )(chosen, queries, same_core, same_core, other_core, other_core, bias, *state)


def fetch_out_weight(w_out, head, core):
    groups = lax.axis_size("head")
    columns = w_out.shape[1] // groups
    half = columns // 2
    blocks = jnp.stack([
        lax.dynamic_slice_in_dim(w_out, dest * columns + core * half, half, 1)
        for dest in range(groups)
    ])
    exchanged = lax.all_to_all(blocks, "head", 0, 0)
    mine = [
        lax.dynamic_index_in_dim(exchanged, (head - shift) % groups, 0, keepdims=False)
        for shift in range(groups)
    ]
    own_full = lax.dynamic_slice_in_dim(w_out, head * columns, columns, 1)
    return own_full, mine


def local(
    activations,
    mod_table,
    step_index,
    block_mask,
    cache_index,
    w_qkv,
    q_gain,
    k_gain,
    pool_kv,
    w_out,
):
    slot = lax.axis_index("slot")
    head = lax.axis_index("head")
    core = slot % 2
    groups = lax.axis_size("head")
    span = activations.shape[0]
    heads = q_gain.shape[0] // HD
    blocks_q = span // BLOCK
    cache_len = cache_index.shape[1]

    own_full, mine = fetch_out_weight(w_out, head, core)
    slots = lax.axis_size("slot")
    pool_flat = pool_kv.reshape(1, pool_kv.shape[1], -1)
    same_core = [pool_flat] + [from_behind(pool_flat, "slot", 2 * k) for k in range(1, slots // 2)]
    same_core = jnp.concatenate(same_core, axis=0)

    onehot = (jnp.arange(mod_table.shape[0], dtype=jnp.int32) == step_index[slot]).astype(
        jnp.float32
    )
    modulation = jnp.einsum("n,nkd->kd", onehot, mod_table.astype(jnp.float32))
    inputs = activations.astype(jnp.float32)
    normed = inputs * lax.rsqrt(jnp.mean(inputs * inputs, axis=-1, keepdims=True) + 1e-06)
    hidden = (normed * (1.0 + modulation[1][None, :]) + modulation[0][None, :]).astype(jnp.bfloat16)
    width = heads * HD
    qkv = jnp.einsum("td,dkh->kth", hidden, w_qkv, preferred_element_type=jnp.float32)
    queries = head_norm(qkv[0], q_gain, heads).astype(jnp.bfloat16)
    keys = head_norm(qkv[1], k_gain, heads).astype(jnp.bfloat16)
    values = qkv[2].astype(jnp.bfloat16)
    local_kv = jnp.concatenate([keys.reshape(span, heads * HD), values], axis=1)
    before = from_behind(local_kv, "slot", 1)
    earlier = from_behind(local_kv, "slot", 2)
    queries, before, earlier = lax.optimization_barrier((queries, before, earlier))
    own_mask = lax.dynamic_index_in_dim(block_mask, slot, 0, keepdims=False)
    own_cache = lax.dynamic_index_in_dim(cache_index, slot, 0, keepdims=False)
    sibling_slot = jnp.bitwise_xor(slot, 1)
    own_cache = jnp.where(
        own_cache % 2 == core,
        ((slot - own_cache) % slots) // 2,
        slots // 2 + ((sibling_slot - own_cache) % slots) // 2,
    ).astype(jnp.int32)
    width = heads * HD
    local_stack = jnp.stack([local_kv, before, earlier]).reshape(3, span, 2 * width)
    visible = jnp.concatenate([jnp.ones((blocks_q, blocks_q), jnp.int32), own_mask], axis=1)
    visible = jnp.transpose(visible.reshape(blocks_q, 3 + cache_len, blocks_q), (1, 0, 2))
    visible = jnp.repeat(visible, BLOCK, axis=2)
    bias = jnp.where(visible > 0, 0.0, -1e30).astype(jnp.float32)
    rows = span // 2
    parts = rows // BLOCK
    queries = queries.reshape(span, width)
    n_local = local_stack.shape[0]
    states = [
        flash_local(queries[p * rows : (p + 1) * rows], local_stack,
                    bias[:n_local, p * parts : (p + 1) * parts], heads)
        for p in range(2)
    ]
    states, same_core, mine = lax.optimization_barrier((states, same_core, mine))
    other_core = lax.ppermute(same_core, "slot", [(i, i ^ 1) for i in range(slots)])
    mixed_parts = [
        flash_pool(queries[p * rows : (p + 1) * rows], same_core, other_core,
                   bias[n_local:, p * parts : (p + 1) * parts], own_cache, states[p], heads)
        for p in range(2)
    ]
    sibling = lax.ppermute(
        jnp.stack(mine[1:]), "slot", [(i, i ^ 1) for i in range(slots)]
    )

    received = [
        jnp.concatenate([
            lax.ppermute(part, "head", [(i, (i + shift) % groups) for i in range(groups)])
            for part in mixed_parts
        ], axis=0)
        for shift in range(1, groups)
    ]
    mixed = jnp.concatenate(mixed_parts, axis=0)
    columns = own_full.shape[1]
    half = columns // 2
    attn = jnp.dot(mixed, own_full, preferred_element_type=jnp.float32).astype(jnp.bfloat16).astype(jnp.float32)
    attn_mine = None
    attn_sib = None
    for shift in range(1, groups):
        group_o = received[shift - 1]
        part = jnp.dot(group_o, mine[shift], preferred_element_type=jnp.float32)
        part = part.astype(jnp.bfloat16).astype(jnp.float32)
        attn_mine = part if attn_mine is None else attn_mine + part
        part = jnp.dot(group_o, sibling[shift - 1], preferred_element_type=jnp.float32)
        part = part.astype(jnp.bfloat16).astype(jnp.float32)
        attn_sib = part if attn_sib is None else attn_sib + part
    other = jnp.concatenate([attn_mine, attn_sib], axis=1)
    swapped = jnp.concatenate([attn_sib, attn_mine], axis=1)
    attn = attn + jnp.where(core == 0, other, swapped)

    offset = head * columns
    input_cols = lax.dynamic_slice_in_dim(activations, offset, columns, 1).astype(jnp.float32)
    gate_cols = lax.dynamic_slice_in_dim(modulation[2], offset, columns, 0)
    return input_cols + gate_cols[None, :] * attn


def solution(mesh):
    placed = (
        P("slot", None),
        P(),
        P(),
        P(),
        P(),
        P(None, None, "head"),
        P("head"),
        P("head"),
        P("slot", None, None, "head"),
        P("head", None),
    )
    return jax.shard_map(
        local, mesh=mesh, in_specs=placed, out_specs=P("slot", "head"), check_vma=False
    )
```

```python
import jax
import jax.numpy as jnp
from jax import lax
from jax.sharding import PartitionSpec as P
from jax.experimental import pallas as pl
from jax.experimental.pallas import tpu as pltpu

HD = 128
BLOCK = 128


def from_behind(shard, axis, by):
    length = lax.axis_size(axis)
    return lax.ppermute(shard, axis, [(i, (i + by) % length) for i in range(length)])


def head_norm(values, gain, heads):
    outs = []
    for h in range(heads):
        cols = slice(h * HD, (h + 1) * HD)
        piece = values[:, cols]
        scaled = piece * lax.rsqrt(jnp.mean(piece * piece, axis=-1, keepdims=True) + 1e-06)
        outs.append(scaled * gain[cols][None, :])
    return jnp.concatenate(outs, axis=1)


def attend(state, queries, span_kv, visible_blocks):
    highest, totals, accum = state
    heads = queries.shape[1]
    span_keys = span_kv[:, 0].reshape(span_kv.shape[0], heads, HD)
    span_values = span_kv[:, 1].reshape(span_kv.shape[0], heads, HD)
    visible = jnp.repeat(jnp.repeat(visible_blocks, BLOCK, axis=0), BLOCK, axis=1) > 0
    scores = jnp.einsum("qhd,khd->hqk", queries, span_keys, preferred_element_type=jnp.float32) * (
        1.0 / HD**0.5
    )
    scores = jnp.where(visible[None], scores, -1e30)
    new_high = jnp.maximum(highest, jnp.max(scores, axis=-1))
    factor = jnp.exp(highest - new_high)
    weights = jnp.where(visible[None], jnp.exp(scores - new_high[..., None]), 0.0)
    totals = totals * factor + jnp.sum(weights, axis=-1)
    accum = accum * factor[..., None] + jnp.einsum(
        "hqk,khd->hqd",
        weights.astype(jnp.bfloat16),
        span_values,
        preferred_element_type=jnp.float32,
    )
    return (new_high, totals, accum)


def online_update(q_ref, k_ref, v_ref, bias_ref, m_sc, l_sc, acc_sc, heads):
    span = q_ref.shape[0]
    blocks = bias_ref.shape[0]
    bias = bias_ref[...][:, None, :]
    for h in range(heads):
        cols = slice(h * HD, (h + 1) * HD)
        q = q_ref[:, cols]
        k = k_ref[:, cols]
        s = lax.dot_general(q, k, (((1,), (1,)), ((), ())), preferred_element_type=jnp.float32)
        s = (s * (1.0 / HD**0.5)).reshape(blocks, span // blocks, s.shape[1]) + bias
        s = s.reshape(span, -1)
        m_prev = m_sc[h]
        m_new = jnp.maximum(m_prev, jnp.max(s, axis=1, keepdims=True))
        factor = jnp.exp(m_prev - m_new)
        p = jnp.exp(s - m_new)
        l_sc[h] = l_sc[h] * factor + jnp.sum(p, axis=1, keepdims=True)
        acc_sc[h] = acc_sc[h] * factor + jnp.dot(
            p.astype(jnp.bfloat16), v_ref[:, cols], preferred_element_type=jnp.float32
        )
        m_sc[h] = m_new


def local_kernel(q_ref, k_ref, v_ref, bias_ref, m_ref, l_ref, acc_ref, *, heads):
    @pl.when(pl.program_id(0) == 0)
    def _():
        m_ref[...] = jnp.full(m_ref.shape, -1e30, jnp.float32)
        l_ref[...] = jnp.zeros(l_ref.shape, jnp.float32)
        acc_ref[...] = jnp.zeros(acc_ref.shape, jnp.float32)

    online_update(q_ref, k_ref, v_ref, bias_ref, m_ref, l_ref, acc_ref, heads)


def flash_local(queries, local_stack, bias, heads):
    span, width = queries.shape
    steps, keys_len = local_stack.shape[:2]
    blocks = bias.shape[1]
    kv_block = (None, keys_len, width)
    state = pl.BlockSpec((heads, span, 1), lambda j: (0, 0, 0))
    kernel = lambda *refs: local_kernel(*refs, heads=heads)
    return pl.pallas_call(
        kernel,
        grid=(steps,),
        in_specs=[
            pl.BlockSpec((span, width), lambda j: (0, 0)),
            pl.BlockSpec(kv_block, lambda j: (j, 0, 0)),
            pl.BlockSpec(kv_block, lambda j: (j, 0, 1)),
            pl.BlockSpec((None, blocks, keys_len), lambda j: (j, 0, 0)),
        ],
        out_specs=[state, state, pl.BlockSpec((heads, span, HD), lambda j: (0, 0, 0))],
        out_shape=[
            jax.ShapeDtypeStruct((heads, span, 1), jnp.float32),
            jax.ShapeDtypeStruct((heads, span, 1), jnp.float32),
            jax.ShapeDtypeStruct((heads, span, HD), jnp.float32),
        ],
        compiler_params=pltpu.CompilerParams(dimension_semantics=("arbitrary",)),
        cost_estimate=pl.CostEstimate(
            flops=4 * steps * heads * span * keys_len * HD,
            transcendentals=steps * heads * span * keys_len,
            bytes_accessed=2 * steps * keys_len * width * 2,
        ),
    )(queries, local_stack, local_stack, bias)


def flash_kernel(chosen, q_ref, lk_ref, lv_ref, ak_ref, av_ref, bk_ref, bv_ref, bias_ref, m_in, l_in, acc_in, o_ref, m_sc, l_sc, acc_sc, *, heads, n_local, half):
    step = pl.program_id(0)
    span = q_ref.shape[0]
    blocks = bias_ref.shape[0]

    @pl.when(step == 0)
    def _():
        m_sc[...] = m_in[...]
        l_sc[...] = l_in[...]
        acc_sc[...] = acc_in[...]

    def body(k_ref, v_ref):
        bias = bias_ref[...][:, None, :]
        for h in range(heads):
            cols = slice(h * HD, (h + 1) * HD)
            q = q_ref[:, cols]
            k = k_ref[:, cols]
            s = lax.dot_general(q, k, (((1,), (1,)), ((), ())), preferred_element_type=jnp.float32)
            s = (s * (1.0 / HD**0.5)).reshape(blocks, span // blocks, s.shape[1]) + bias
            s = s.reshape(span, -1)
            m_prev = m_sc[h]
            m_new = jnp.maximum(m_prev, jnp.max(s, axis=1, keepdims=True))
            factor = jnp.exp(m_prev - m_new)
            p = jnp.exp(s - m_new)
            l_sc[h] = l_sc[h] * factor + jnp.sum(p, axis=1, keepdims=True)
            acc_sc[h] = acc_sc[h] * factor + jnp.dot(
                p.astype(jnp.bfloat16), v_ref[:, cols], preferred_element_type=jnp.float32
            )
            m_sc[h] = m_new

    @pl.when(step < n_local)
    def _():
        body(lk_ref, lv_ref)

    pos = chosen[jnp.maximum(step - n_local, 0)]

    @pl.when((step >= n_local) & (pos < half))
    def _():
        body(ak_ref, av_ref)

    @pl.when((step >= n_local) & (pos >= half))
    def _():
        body(bk_ref, bv_ref)

    @pl.when(step == pl.num_programs(0) - 1)
    def _():
        for h in range(heads):
            cols = slice(h * HD, (h + 1) * HD)
            o_ref[:, cols] = (acc_sc[h] / l_sc[h]).astype(o_ref.dtype)


def flash(queries, local_stack, same_core, other_core, bias, chosen, state, heads):
    span, width = queries.shape
    n_local = local_stack.shape[0]
    half = same_core.shape[0]
    steps = n_local + chosen.shape[0]
    blocks = bias.shape[1]

    def local_map(kv):
        return lambda j, c: (jnp.minimum(j, n_local - 1), 0, kv)

    def pool_map(kv, upper):
        def index(j, c):
            pos = c[jnp.maximum(j - n_local, 0)]
            hit = (j >= n_local) & ((pos >= half) == upper)
            return (jnp.where(hit, pos - upper * half, 0), 0, kv)

        return index

    keys_len = local_stack.shape[1]
    kv_block = (None, keys_len, width)
    grid_spec = pltpu.PrefetchScalarGridSpec(
        num_scalar_prefetch=1,
        grid=(steps,),
        in_specs=[
            pl.BlockSpec((span, width), lambda j, c: (0, 0)),
            pl.BlockSpec(kv_block, local_map(0)),
            pl.BlockSpec(kv_block, local_map(1)),
            pl.BlockSpec(kv_block, pool_map(0, False)),
            pl.BlockSpec(kv_block, pool_map(1, False)),
            pl.BlockSpec(kv_block, pool_map(0, True)),
            pl.BlockSpec(kv_block, pool_map(1, True)),
            pl.BlockSpec((None, blocks, keys_len), lambda j, c: (j, 0, 0)),
            pl.BlockSpec((heads, span, 1), lambda j, c: (0, 0, 0)),
            pl.BlockSpec((heads, span, 1), lambda j, c: (0, 0, 0)),
            pl.BlockSpec((heads, span, HD), lambda j, c: (0, 0, 0)),
        ],
        out_specs=pl.BlockSpec((span, width), lambda j, c: (0, 0)),
        scratch_shapes=[
            pltpu.VMEM((heads, span, 1), jnp.float32),
            pltpu.VMEM((heads, span, 1), jnp.float32),
            pltpu.VMEM((heads, span, HD), jnp.float32),
        ],
    )
    kernel = lambda *refs: flash_kernel(*refs, heads=heads, n_local=n_local, half=half)
    return pl.pallas_call(
        kernel,
        grid_spec=grid_spec,
        out_shape=jax.ShapeDtypeStruct((span, width), jnp.bfloat16),
        compiler_params=pltpu.CompilerParams(dimension_semantics=("arbitrary",)),
        cost_estimate=pl.CostEstimate(
            flops=4 * steps * heads * span * span * HD,
            transcendentals=steps * heads * span * span,
            bytes_accessed=2 * steps * span * width * 2,
        ),
    )(chosen, queries, local_stack, local_stack, same_core, same_core, other_core, other_core, bias, *state)


def fetch_out_weight(w_out, head, core):
    groups = lax.axis_size("head")
    columns = w_out.shape[1] // groups
    half = columns // 2
    blocks = jnp.stack([
        lax.dynamic_slice_in_dim(w_out, dest * columns + core * half, half, 1)
        for dest in range(groups)
    ])
    exchanged = lax.all_to_all(blocks, "head", 0, 0)
    mine = [
        lax.dynamic_index_in_dim(exchanged, (head - shift) % groups, 0, keepdims=False)
        for shift in range(groups)
    ]
    own_full = lax.dynamic_slice_in_dim(w_out, head * columns, columns, 1)
    return own_full, mine


def local(
    activations,
    mod_table,
    step_index,
    block_mask,
    cache_index,
    w_qkv,
    q_gain,
    k_gain,
    pool_kv,
    w_out,
):
    slot = lax.axis_index("slot")
    head = lax.axis_index("head")
    core = slot % 2
    groups = lax.axis_size("head")
    span = activations.shape[0]
    heads = q_gain.shape[0] // HD
    blocks_q = span // BLOCK
    cache_len = cache_index.shape[1]

    own_full, mine = fetch_out_weight(w_out, head, core)
    slots = lax.axis_size("slot")
    pool_flat = pool_kv.reshape(1, pool_kv.shape[1], -1)
    same_core = [pool_flat] + [from_behind(pool_flat, "slot", 2 * k) for k in range(1, slots // 2)]
    same_core = jnp.concatenate(same_core, axis=0)

    onehot = (jnp.arange(mod_table.shape[0], dtype=jnp.int32) == step_index[slot]).astype(
        jnp.float32
    )
    modulation = jnp.einsum("n,nkd->kd", onehot, mod_table.astype(jnp.float32))
    inputs = activations.astype(jnp.float32)
    normed = inputs * lax.rsqrt(jnp.mean(inputs * inputs, axis=-1, keepdims=True) + 1e-06)
    hidden = (normed * (1.0 + modulation[1][None, :]) + modulation[0][None, :]).astype(jnp.bfloat16)
    width = heads * HD
    qkv = jnp.einsum("td,dkh->kth", hidden, w_qkv, preferred_element_type=jnp.float32)
    queries = head_norm(qkv[0], q_gain, heads).astype(jnp.bfloat16)
    keys = head_norm(qkv[1], k_gain, heads).astype(jnp.bfloat16)
    values = qkv[2].astype(jnp.bfloat16)
    local_kv = jnp.concatenate([keys.reshape(span, heads * HD), values], axis=1)
    before = from_behind(local_kv, "slot", 1)
    earlier = from_behind(local_kv, "slot", 2)
    rows = span // 2
    parts = rows // BLOCK
    width = heads * HD
    own_mask = lax.dynamic_index_in_dim(block_mask, slot, 0, keepdims=False)
    flat_queries = queries.reshape(span, width)
    own_bias = jnp.zeros((1, blocks_q, span), jnp.float32)
    states = [
        flash_local(flat_queries[p * rows : (p + 1) * rows], local_kv.reshape(1, span, 2 * width),
                    own_bias[:, p * parts : (p + 1) * parts], heads)
        for p in range(2)
    ]
    states, queries, before, earlier, same_core, mine = lax.optimization_barrier(
        (states, queries, before, earlier, same_core, mine)
    )
    other_core = lax.ppermute(same_core, "slot", [(i, i ^ 1) for i in range(slots)])
    own_mask = lax.dynamic_index_in_dim(block_mask, slot, 0, keepdims=False)
    own_cache = lax.dynamic_index_in_dim(cache_index, slot, 0, keepdims=False)
    sibling_slot = jnp.bitwise_xor(slot, 1)
    own_cache = jnp.where(
        own_cache % 2 == core,
        ((slot - own_cache) % slots) // 2,
        slots // 2 + ((sibling_slot - own_cache) % slots) // 2,
    ).astype(jnp.int32)
    width = heads * HD
    local_stack = jnp.stack([before, earlier]).reshape(2, span, 2 * width)
    visible = jnp.concatenate([jnp.ones((blocks_q, blocks_q), jnp.int32), own_mask], axis=1)
    visible = jnp.transpose(visible.reshape(blocks_q, 3 + cache_len, blocks_q), (1, 0, 2))
    visible = jnp.repeat(visible, BLOCK, axis=2)
    bias = jnp.where(visible > 0, 0.0, -1e30).astype(jnp.float32)
    rows = span // 2
    parts = rows // BLOCK
    queries = queries.reshape(span, width)
    mixed_parts = [
        flash(queries[p * rows : (p + 1) * rows], local_stack, same_core, other_core,
              bias[1:, p * parts : (p + 1) * parts], own_cache, states[p], heads)
        for p in range(2)
    ]
    sibling = lax.ppermute(
        jnp.stack(mine[1:]), "slot", [(i, i ^ 1) for i in range(slots)]
    )

    received = [
        jnp.concatenate([
            lax.ppermute(part, "head", [(i, (i + shift) % groups) for i in range(groups)])
            for part in mixed_parts
        ], axis=0)
        for shift in range(1, groups)
    ]
    mixed = jnp.concatenate(mixed_parts, axis=0)
    columns = own_full.shape[1]
    half = columns // 2
    attn = jnp.dot(mixed, own_full, preferred_element_type=jnp.float32).astype(jnp.bfloat16).astype(jnp.float32)
    attn_mine = None
    attn_sib = None
    for shift in range(1, groups):
        group_o = received[shift - 1]
        part = jnp.dot(group_o, mine[shift], preferred_element_type=jnp.float32)
        part = part.astype(jnp.bfloat16).astype(jnp.float32)
        attn_mine = part if attn_mine is None else attn_mine + part
        part = jnp.dot(group_o, sibling[shift - 1], preferred_element_type=jnp.float32)
        part = part.astype(jnp.bfloat16).astype(jnp.float32)
        attn_sib = part if attn_sib is None else attn_sib + part
    other = jnp.concatenate([attn_mine, attn_sib], axis=1)
    swapped = jnp.concatenate([attn_sib, attn_mine], axis=1)
    attn = attn + jnp.where(core == 0, other, swapped)

    offset = head * columns
    input_cols = lax.dynamic_slice_in_dim(activations, offset, columns, 1).astype(jnp.float32)
    gate_cols = lax.dynamic_slice_in_dim(modulation[2], offset, columns, 0)
    return input_cols + gate_cols[None, :] * attn


def solution(mesh):
    placed = (
        P("slot", None),
        P(),
        P(),
        P(),
        P(),
        P(None, None, "head"),
        P("head"),
        P("head"),
        P("slot", None, None, "head"),
        P("head", None),
    )
    return jax.shard_map(
        local, mesh=mesh, in_specs=placed, out_specs=P("slot", "head"), check_vma=False
    )
```

```python
import jax
import jax.numpy as jnp
from jax import lax
from jax.sharding import PartitionSpec as P
from jax.experimental import pallas as pl
from jax.experimental.pallas import tpu as pltpu

HD = 128
BLOCK = 128


def from_behind(shard, axis, by):
    length = lax.axis_size(axis)
    return lax.ppermute(shard, axis, [(i, (i + by) % length) for i in range(length)])


def head_norm(values, gain, heads):
    outs = []
    for h in range(heads):
        cols = slice(h * HD, (h + 1) * HD)
        piece = values[:, cols]
        scaled = piece * lax.rsqrt(jnp.mean(piece * piece, axis=-1, keepdims=True) + 1e-06)
        outs.append(scaled * gain[cols][None, :])
    return jnp.concatenate(outs, axis=1)


def attend(state, queries, span_kv, visible_blocks):
    highest, totals, accum = state
    heads = queries.shape[1]
    span_keys = span_kv[:, 0].reshape(span_kv.shape[0], heads, HD)
    span_values = span_kv[:, 1].reshape(span_kv.shape[0], heads, HD)
    visible = jnp.repeat(jnp.repeat(visible_blocks, BLOCK, axis=0), BLOCK, axis=1) > 0
    scores = jnp.einsum("qhd,khd->hqk", queries, span_keys, preferred_element_type=jnp.float32) * (
        1.0 / HD**0.5
    )
    scores = jnp.where(visible[None], scores, -1e30)
    new_high = jnp.maximum(highest, jnp.max(scores, axis=-1))
    factor = jnp.exp(highest - new_high)
    weights = jnp.where(visible[None], jnp.exp(scores - new_high[..., None]), 0.0)
    totals = totals * factor + jnp.sum(weights, axis=-1)
    accum = accum * factor[..., None] + jnp.einsum(
        "hqk,khd->hqd",
        weights.astype(jnp.bfloat16),
        span_values,
        preferred_element_type=jnp.float32,
    )
    return (new_high, totals, accum)


def online_update(q_ref, k_ref, v_ref, bias_ref, m_sc, l_sc, acc_sc, heads):
    span = q_ref.shape[0]
    blocks = bias_ref.shape[0]
    bias = bias_ref[...][:, None, :]
    for h in range(heads):
        cols = slice(h * HD, (h + 1) * HD)
        q = q_ref[:, cols]
        k = k_ref[:, cols]
        s = lax.dot_general(q, k, (((1,), (1,)), ((), ())), preferred_element_type=jnp.float32)
        s = (s * (1.0 / HD**0.5)).reshape(blocks, span // blocks, s.shape[1]) + bias
        s = s.reshape(span, -1)
        m_prev = m_sc[h]
        m_new = jnp.maximum(m_prev, jnp.max(s, axis=1, keepdims=True))
        factor = jnp.exp(m_prev - m_new)
        p = jnp.exp(s - m_new)
        l_sc[h] = l_sc[h] * factor + jnp.sum(p, axis=1, keepdims=True)
        acc_sc[h] = acc_sc[h] * factor + jnp.dot(
            p.astype(jnp.bfloat16), v_ref[:, cols], preferred_element_type=jnp.float32
        )
        m_sc[h] = m_new


def local_kernel(q_ref, k_ref, v_ref, bias_ref, m_ref, l_ref, acc_ref, *, heads):
    @pl.when(pl.program_id(0) == 0)
    def _():
        m_ref[...] = jnp.full(m_ref.shape, -1e30, jnp.float32)
        l_ref[...] = jnp.zeros(l_ref.shape, jnp.float32)
        acc_ref[...] = jnp.zeros(acc_ref.shape, jnp.float32)

    online_update(q_ref, k_ref, v_ref, bias_ref, m_ref, l_ref, acc_ref, heads)


def flash_local(queries, local_stack, bias, heads):
    span, width = queries.shape
    steps, keys_len = local_stack.shape[:2]
    blocks = bias.shape[1]
    kv_block = (None, keys_len, width)
    state = pl.BlockSpec((heads, span, 1), lambda j: (0, 0, 0))
    kernel = lambda *refs: local_kernel(*refs, heads=heads)
    return pl.pallas_call(
        kernel,
        grid=(steps,),
        in_specs=[
            pl.BlockSpec((span, width), lambda j: (0, 0)),
            pl.BlockSpec(kv_block, lambda j: (j, 0, 0)),
            pl.BlockSpec(kv_block, lambda j: (j, 0, 1)),
            pl.BlockSpec((None, blocks, keys_len), lambda j: (j, 0, 0)),
        ],
        out_specs=[state, state, pl.BlockSpec((heads, span, HD), lambda j: (0, 0, 0))],
        out_shape=[
            jax.ShapeDtypeStruct((heads, span, 1), jnp.float32),
            jax.ShapeDtypeStruct((heads, span, 1), jnp.float32),
            jax.ShapeDtypeStruct((heads, span, HD), jnp.float32),
        ],
        compiler_params=pltpu.CompilerParams(dimension_semantics=("arbitrary",)),
        cost_estimate=pl.CostEstimate(
            flops=4 * steps * heads * span * keys_len * HD,
            transcendentals=steps * heads * span * keys_len,
            bytes_accessed=2 * steps * keys_len * width * 2,
        ),
    )(queries, local_stack, local_stack, bias)


def flash_kernel(chosen, q_ref, lk_ref, lv_ref, ak_ref, av_ref, bk_ref, bv_ref, bias_ref, m_in, l_in, acc_in, o_ref, m_sc, l_sc, acc_sc, *, heads, n_local, half):
    step = pl.program_id(0)
    span = q_ref.shape[0]
    blocks = bias_ref.shape[0]

    @pl.when(step == 0)
    def _():
        m_sc[...] = m_in[...]
        l_sc[...] = l_in[...]
        acc_sc[...] = acc_in[...]

    def body(k_ref, v_ref):
        bias = bias_ref[...][:, None, :]
        for h in range(heads):
            cols = slice(h * HD, (h + 1) * HD)
            q = q_ref[:, cols]
            k = k_ref[:, cols]
            s = lax.dot_general(q, k, (((1,), (1,)), ((), ())), preferred_element_type=jnp.float32)
            s = (s * (1.0 / HD**0.5)).reshape(blocks, span // blocks, s.shape[1]) + bias
            s = s.reshape(span, -1)
            m_prev = m_sc[h]
            m_new = jnp.maximum(m_prev, jnp.max(s, axis=1, keepdims=True))
            factor = jnp.exp(m_prev - m_new)
            p = jnp.exp(s - m_new)
            l_sc[h] = l_sc[h] * factor + jnp.sum(p, axis=1, keepdims=True)
            acc_sc[h] = acc_sc[h] * factor + jnp.dot(
                p.astype(jnp.bfloat16), v_ref[:, cols], preferred_element_type=jnp.float32
            )
            m_sc[h] = m_new

    @pl.when(step < n_local)
    def _():
        body(lk_ref, lv_ref)

    pos = chosen[jnp.maximum(step - n_local, 0)]

    @pl.when((step >= n_local) & (pos < half))
    def _():
        body(ak_ref, av_ref)

    @pl.when((step >= n_local) & (pos >= half))
    def _():
        body(bk_ref, bv_ref)

    @pl.when(step == pl.num_programs(0) - 1)
    def _():
        for h in range(heads):
            cols = slice(h * HD, (h + 1) * HD)
            o_ref[:, cols] = (acc_sc[h] / l_sc[h]).astype(o_ref.dtype)


def flash(queries, local_stack, same_core, other_core, bias, chosen, state, heads):
    span, width = queries.shape
    n_local = local_stack.shape[0]
    half = same_core.shape[0]
    steps = n_local + chosen.shape[0]
    blocks = bias.shape[1]

    def local_map(kv):
        return lambda j, c: (jnp.minimum(j, n_local - 1), 0, kv)

    def pool_map(kv, upper):
        def index(j, c):
            pos = c[jnp.maximum(j - n_local, 0)]
            hit = (j >= n_local) & ((pos >= half) == upper)
            return (jnp.where(hit, pos - upper * half, 0), 0, kv)

        return index

    keys_len = local_stack.shape[1]
    kv_block = (None, keys_len, width)
    grid_spec = pltpu.PrefetchScalarGridSpec(
        num_scalar_prefetch=1,
        grid=(steps,),
        in_specs=[
            pl.BlockSpec((span, width), lambda j, c: (0, 0)),
            pl.BlockSpec(kv_block, local_map(0)),
            pl.BlockSpec(kv_block, local_map(1)),
            pl.BlockSpec(kv_block, pool_map(0, False)),
            pl.BlockSpec(kv_block, pool_map(1, False)),
            pl.BlockSpec(kv_block, pool_map(0, True)),
            pl.BlockSpec(kv_block, pool_map(1, True)),
            pl.BlockSpec((None, blocks, keys_len), lambda j, c: (j, 0, 0)),
            pl.BlockSpec((heads, span, 1), lambda j, c: (0, 0, 0)),
            pl.BlockSpec((heads, span, 1), lambda j, c: (0, 0, 0)),
            pl.BlockSpec((heads, span, HD), lambda j, c: (0, 0, 0)),
        ],
        out_specs=pl.BlockSpec((span, width), lambda j, c: (0, 0)),
        scratch_shapes=[
            pltpu.VMEM((heads, span, 1), jnp.float32),
            pltpu.VMEM((heads, span, 1), jnp.float32),
            pltpu.VMEM((heads, span, HD), jnp.float32),
        ],
    )
    kernel = lambda *refs: flash_kernel(*refs, heads=heads, n_local=n_local, half=half)
    return pl.pallas_call(
        kernel,
        grid_spec=grid_spec,
        out_shape=jax.ShapeDtypeStruct((span, width), jnp.bfloat16),
        compiler_params=pltpu.CompilerParams(dimension_semantics=("arbitrary",)),
        cost_estimate=pl.CostEstimate(
            flops=4 * steps * heads * span * span * HD,
            transcendentals=steps * heads * span * span,
            bytes_accessed=2 * steps * span * width * 2,
        ),
    )(chosen, queries, local_stack, local_stack, same_core, same_core, other_core, other_core, bias, *state)


def fetch_out_weight(w_out, head, core):
    groups = lax.axis_size("head")
    columns = w_out.shape[1] // groups
    half = columns // 2
    blocks = jnp.stack([
        lax.dynamic_slice_in_dim(w_out, dest * columns + core * half, half, 1)
        for dest in range(groups)
    ])
    exchanged = lax.all_to_all(blocks, "head", 0, 0)
    mine = [
        lax.dynamic_index_in_dim(exchanged, (head - shift) % groups, 0, keepdims=False)
        for shift in range(groups)
    ]
    own_full = lax.dynamic_slice_in_dim(w_out, head * columns, columns, 1)
    return own_full, mine


def local(
    activations,
    mod_table,
    step_index,
    block_mask,
    cache_index,
    w_qkv,
    q_gain,
    k_gain,
    pool_kv,
    w_out,
):
    slot = lax.axis_index("slot")
    head = lax.axis_index("head")
    core = slot % 2
    groups = lax.axis_size("head")
    span = activations.shape[0]
    heads = q_gain.shape[0] // HD
    blocks_q = span // BLOCK
    cache_len = cache_index.shape[1]

    own_full, mine = fetch_out_weight(w_out, head, core)
    slots = lax.axis_size("slot")
    pool_flat = pool_kv.reshape(1, pool_kv.shape[1], -1)
    same_core = pool_flat
    bit = 2
    while bit < slots:
        partner = lax.ppermute(same_core, "slot", [(i, i ^ bit) for i in range(slots)])
        same_core = jnp.concatenate([same_core, partner], axis=0)
        bit *= 2

    onehot = (jnp.arange(mod_table.shape[0], dtype=jnp.int32) == step_index[slot]).astype(
        jnp.float32
    )
    modulation = jnp.einsum("n,nkd->kd", onehot, mod_table.astype(jnp.float32))
    inputs = activations.astype(jnp.float32)
    normed = inputs * lax.rsqrt(jnp.mean(inputs * inputs, axis=-1, keepdims=True) + 1e-06)
    hidden = (normed * (1.0 + modulation[1][None, :]) + modulation[0][None, :]).astype(jnp.bfloat16)
    width = heads * HD
    qkv = jnp.einsum("td,dkh->kth", hidden, w_qkv, preferred_element_type=jnp.float32)
    queries = head_norm(qkv[0], q_gain, heads).astype(jnp.bfloat16)
    keys = head_norm(qkv[1], k_gain, heads).astype(jnp.bfloat16)
    values = qkv[2].astype(jnp.bfloat16)
    local_kv = jnp.concatenate([keys.reshape(span, heads * HD), values], axis=1)
    before = from_behind(local_kv, "slot", 1)
    earlier = from_behind(local_kv, "slot", 2)
    rows = span // 2
    parts = rows // BLOCK
    width = heads * HD
    own_mask = lax.dynamic_index_in_dim(block_mask, slot, 0, keepdims=False)
    flat_queries = queries.reshape(span, width)
    own_bias = jnp.zeros((1, blocks_q, span), jnp.float32)
    states = [
        flash_local(flat_queries[p * rows : (p + 1) * rows], local_kv.reshape(1, span, 2 * width),
                    own_bias[:, p * parts : (p + 1) * parts], heads)
        for p in range(2)
    ]
    states, queries, before, earlier, same_core, mine = lax.optimization_barrier(
        (states, queries, before, earlier, same_core, mine)
    )
    other_core = lax.ppermute(same_core, "slot", [(i, i ^ 1) for i in range(slots)])
    own_mask = lax.dynamic_index_in_dim(block_mask, slot, 0, keepdims=False)
    own_cache = lax.dynamic_index_in_dim(cache_index, slot, 0, keepdims=False)
    sibling_slot = jnp.bitwise_xor(slot, 1)
    own_cache = jnp.where(
        own_cache % 2 == core,
        jnp.bitwise_xor(own_cache, slot) // 2,
        slots // 2 + jnp.bitwise_xor(own_cache, sibling_slot) // 2,
    ).astype(jnp.int32)
    width = heads * HD
    local_stack = jnp.stack([before, earlier]).reshape(2, span, 2 * width)
    visible = jnp.concatenate([jnp.ones((blocks_q, blocks_q), jnp.int32), own_mask], axis=1)
    visible = jnp.transpose(visible.reshape(blocks_q, 3 + cache_len, blocks_q), (1, 0, 2))
    visible = jnp.repeat(visible, BLOCK, axis=2)
    bias = jnp.where(visible > 0, 0.0, -1e30).astype(jnp.float32)
    rows = span // 2
    parts = rows // BLOCK
    queries = queries.reshape(span, width)
    mixed_parts = [
        flash(queries[p * rows : (p + 1) * rows], local_stack, same_core, other_core,
              bias[1:, p * parts : (p + 1) * parts], own_cache, states[p], heads)
        for p in range(2)
    ]
    sibling = lax.ppermute(
        jnp.stack(mine[1:]), "slot", [(i, i ^ 1) for i in range(slots)]
    )

    received = [
        jnp.concatenate([
            lax.ppermute(part, "head", [(i, (i + shift) % groups) for i in range(groups)])
            for part in mixed_parts
        ], axis=0)
        for shift in range(1, groups)
    ]
    mixed = jnp.concatenate(mixed_parts, axis=0)
    columns = own_full.shape[1]
    half = columns // 2
    attn = jnp.dot(mixed, own_full, preferred_element_type=jnp.float32).astype(jnp.bfloat16).astype(jnp.float32)
    attn_mine = None
    attn_sib = None
    for shift in range(1, groups):
        group_o = received[shift - 1]
        part = jnp.dot(group_o, mine[shift], preferred_element_type=jnp.float32)
        part = part.astype(jnp.bfloat16).astype(jnp.float32)
        attn_mine = part if attn_mine is None else attn_mine + part
        part = jnp.dot(group_o, sibling[shift - 1], preferred_element_type=jnp.float32)
        part = part.astype(jnp.bfloat16).astype(jnp.float32)
        attn_sib = part if attn_sib is None else attn_sib + part
    other = jnp.concatenate([attn_mine, attn_sib], axis=1)
    swapped = jnp.concatenate([attn_sib, attn_mine], axis=1)
    attn = attn + jnp.where(core == 0, other, swapped)

    offset = head * columns
    input_cols = lax.dynamic_slice_in_dim(activations, offset, columns, 1).astype(jnp.float32)
    gate_cols = lax.dynamic_slice_in_dim(modulation[2], offset, columns, 0)
    return input_cols + gate_cols[None, :] * attn


def solution(mesh):
    placed = (
        P("slot", None),
        P(),
        P(),
        P(),
        P(),
        P(None, None, "head"),
        P("head"),
        P("head"),
        P("slot", None, None, "head"),
        P("head", None),
    )
    return jax.shard_map(
        local, mesh=mesh, in_specs=placed, out_specs=P("slot", "head"), check_vma=False
    )
```

```python
import jax
import jax.numpy as jnp
from jax import lax
from jax.sharding import PartitionSpec as P
from jax.experimental import pallas as pl
from jax.experimental.pallas import tpu as pltpu

HD = 128
BLOCK = 128


def from_behind(shard, axis, by):
    length = lax.axis_size(axis)
    return lax.ppermute(shard, axis, [(i, (i + by) % length) for i in range(length)])


def head_norm(values, gain, heads):
    outs = []
    for h in range(heads):
        cols = slice(h * HD, (h + 1) * HD)
        piece = values[:, cols]
        scaled = piece * lax.rsqrt(jnp.mean(piece * piece, axis=-1, keepdims=True) + 1e-06)
        outs.append(scaled * gain[cols][None, :])
    return jnp.concatenate(outs, axis=1)


def attend(state, queries, span_kv, visible_blocks):
    highest, totals, accum = state
    heads = queries.shape[1]
    span_keys = span_kv[:, 0].reshape(span_kv.shape[0], heads, HD)
    span_values = span_kv[:, 1].reshape(span_kv.shape[0], heads, HD)
    visible = jnp.repeat(jnp.repeat(visible_blocks, BLOCK, axis=0), BLOCK, axis=1) > 0
    scores = jnp.einsum("qhd,khd->hqk", queries, span_keys, preferred_element_type=jnp.float32) * (
        1.0 / HD**0.5
    )
    scores = jnp.where(visible[None], scores, -1e30)
    new_high = jnp.maximum(highest, jnp.max(scores, axis=-1))
    factor = jnp.exp(highest - new_high)
    weights = jnp.where(visible[None], jnp.exp(scores - new_high[..., None]), 0.0)
    totals = totals * factor + jnp.sum(weights, axis=-1)
    accum = accum * factor[..., None] + jnp.einsum(
        "hqk,khd->hqd",
        weights.astype(jnp.bfloat16),
        span_values,
        preferred_element_type=jnp.float32,
    )
    return (new_high, totals, accum)


def online_update(q_ref, k_ref, v_ref, bias_ref, m_sc, l_sc, acc_sc, heads):
    span = q_ref.shape[0]
    blocks = bias_ref.shape[0]
    bias = bias_ref[...][:, None, :]
    for h in range(heads):
        cols = slice(h * HD, (h + 1) * HD)
        q = q_ref[:, cols]
        k = k_ref[:, cols]
        s = lax.dot_general(q, k, (((1,), (1,)), ((), ())), preferred_element_type=jnp.float32)
        s = (s * (1.0 / HD**0.5)).reshape(blocks, span // blocks, s.shape[1]) + bias
        s = s.reshape(span, -1)
        m_prev = m_sc[h]
        m_new = jnp.maximum(m_prev, jnp.max(s, axis=1, keepdims=True))
        factor = jnp.exp(m_prev - m_new)
        p = jnp.exp(s - m_new)
        l_sc[h] = l_sc[h] * factor + jnp.sum(p, axis=1, keepdims=True)
        acc_sc[h] = acc_sc[h] * factor + jnp.dot(
            p.astype(jnp.bfloat16), v_ref[:, cols], preferred_element_type=jnp.float32
        )
        m_sc[h] = m_new


def local_kernel(q_ref, k_ref, v_ref, bias_ref, m_ref, l_ref, acc_ref, *, heads):
    @pl.when(pl.program_id(0) == 0)
    def _():
        m_ref[...] = jnp.full(m_ref.shape, -1e30, jnp.float32)
        l_ref[...] = jnp.zeros(l_ref.shape, jnp.float32)
        acc_ref[...] = jnp.zeros(acc_ref.shape, jnp.float32)

    online_update(q_ref, k_ref, v_ref, bias_ref, m_ref, l_ref, acc_ref, heads)


def flash_local(queries, local_stack, bias, heads):
    span, width = queries.shape
    steps, keys_len = local_stack.shape[:2]
    blocks = bias.shape[1]
    kv_block = (None, keys_len, width)
    state = pl.BlockSpec((heads, span, 1), lambda j: (0, 0, 0))
    kernel = lambda *refs: local_kernel(*refs, heads=heads)
    return pl.pallas_call(
        kernel,
        grid=(steps,),
        in_specs=[
            pl.BlockSpec((span, width), lambda j: (0, 0)),
            pl.BlockSpec(kv_block, lambda j: (j, 0, 0)),
            pl.BlockSpec(kv_block, lambda j: (j, 0, 1)),
            pl.BlockSpec((None, blocks, keys_len), lambda j: (j, 0, 0)),
        ],
        out_specs=[state, state, pl.BlockSpec((heads, span, HD), lambda j: (0, 0, 0))],
        out_shape=[
            jax.ShapeDtypeStruct((heads, span, 1), jnp.float32),
            jax.ShapeDtypeStruct((heads, span, 1), jnp.float32),
            jax.ShapeDtypeStruct((heads, span, HD), jnp.float32),
        ],
        compiler_params=pltpu.CompilerParams(dimension_semantics=("arbitrary",)),
        cost_estimate=pl.CostEstimate(
            flops=4 * steps * heads * span * keys_len * HD,
            transcendentals=steps * heads * span * keys_len,
            bytes_accessed=2 * steps * keys_len * width * 2,
        ),
    )(queries, local_stack, local_stack, bias)


def flash_kernel(chosen, q_ref, lk_ref, lv_ref, ak_ref, av_ref, bk_ref, bv_ref, bias_ref, m_in, l_in, acc_in, o_ref, m_sc, l_sc, acc_sc, *, heads, n_local, half):
    step = pl.program_id(0)
    span = q_ref.shape[0]
    blocks = bias_ref.shape[0]

    @pl.when(step == 0)
    def _():
        m_sc[...] = m_in[...]
        l_sc[...] = l_in[...]
        acc_sc[...] = acc_in[...]

    def body(k_ref, v_ref):
        bias = bias_ref[...][:, None, :]
        for h in range(heads):
            cols = slice(h * HD, (h + 1) * HD)
            q = q_ref[:, cols]
            k = k_ref[:, cols]
            s = lax.dot_general(q, k, (((1,), (1,)), ((), ())), preferred_element_type=jnp.float32)
            s = (s * (1.0 / HD**0.5)).reshape(blocks, span // blocks, s.shape[1]) + bias
            s = s.reshape(span, -1)
            m_prev = m_sc[h]
            m_new = jnp.maximum(m_prev, jnp.max(s, axis=1, keepdims=True))
            factor = jnp.exp(m_prev - m_new)
            p = jnp.exp(s - m_new)
            l_sc[h] = l_sc[h] * factor + jnp.sum(p, axis=1, keepdims=True)
            acc_sc[h] = acc_sc[h] * factor + jnp.dot(
                p.astype(jnp.bfloat16), v_ref[:, cols], preferred_element_type=jnp.float32
            )
            m_sc[h] = m_new

    @pl.when(step < n_local)
    def _():
        body(lk_ref, lv_ref)

    pos = chosen[jnp.maximum(step - n_local, 0)]

    @pl.when((step >= n_local) & (pos < half))
    def _():
        body(ak_ref, av_ref)

    @pl.when((step >= n_local) & (pos >= half))
    def _():
        body(bk_ref, bv_ref)

    @pl.when(step == pl.num_programs(0) - 1)
    def _():
        for h in range(heads):
            cols = slice(h * HD, (h + 1) * HD)
            o_ref[:, cols] = (acc_sc[h] / l_sc[h]).astype(o_ref.dtype)


def flash(queries, local_stack, same_core, other_core, bias, chosen, state, heads):
    span, width = queries.shape
    n_local = local_stack.shape[0]
    half = same_core.shape[0]
    steps = n_local + chosen.shape[0]
    blocks = bias.shape[1]

    def local_map(kv):
        return lambda j, c: (jnp.minimum(j, n_local - 1), 0, kv)

    def pool_map(kv, upper):
        def index(j, c):
            pos = c[jnp.maximum(j - n_local, 0)]
            hit = (j >= n_local) & ((pos >= half) == upper)
            return (jnp.where(hit, pos - upper * half, 0), 0, kv)

        return index

    keys_len = local_stack.shape[1]
    kv_block = (None, keys_len, width)
    grid_spec = pltpu.PrefetchScalarGridSpec(
        num_scalar_prefetch=1,
        grid=(steps,),
        in_specs=[
            pl.BlockSpec((span, width), lambda j, c: (0, 0)),
            pl.BlockSpec(kv_block, local_map(0)),
            pl.BlockSpec(kv_block, local_map(1)),
            pl.BlockSpec(kv_block, pool_map(0, False)),
            pl.BlockSpec(kv_block, pool_map(1, False)),
            pl.BlockSpec(kv_block, pool_map(0, True)),
            pl.BlockSpec(kv_block, pool_map(1, True)),
            pl.BlockSpec((None, blocks, keys_len), lambda j, c: (j, 0, 0)),
            pl.BlockSpec((heads, span, 1), lambda j, c: (0, 0, 0)),
            pl.BlockSpec((heads, span, 1), lambda j, c: (0, 0, 0)),
            pl.BlockSpec((heads, span, HD), lambda j, c: (0, 0, 0)),
        ],
        out_specs=pl.BlockSpec((span, width), lambda j, c: (0, 0)),
        scratch_shapes=[
            pltpu.VMEM((heads, span, 1), jnp.float32),
            pltpu.VMEM((heads, span, 1), jnp.float32),
            pltpu.VMEM((heads, span, HD), jnp.float32),
        ],
    )
    kernel = lambda *refs: flash_kernel(*refs, heads=heads, n_local=n_local, half=half)
    return pl.pallas_call(
        kernel,
        grid_spec=grid_spec,
        out_shape=jax.ShapeDtypeStruct((span, width), jnp.bfloat16),
        compiler_params=pltpu.CompilerParams(dimension_semantics=("arbitrary",)),
        cost_estimate=pl.CostEstimate(
            flops=4 * steps * heads * span * span * HD,
            transcendentals=steps * heads * span * span,
            bytes_accessed=2 * steps * span * width * 2,
        ),
    )(chosen, queries, local_stack, local_stack, same_core, same_core, other_core, other_core, bias, *state)


def fetch_out_weight(w_out, head, core):
    groups = lax.axis_size("head")
    columns = w_out.shape[1] // groups
    half = columns // 2
    blocks = jnp.stack([
        lax.dynamic_slice_in_dim(w_out, dest * columns + core * half, half, 1)
        for dest in range(groups)
    ])
    exchanged = lax.all_to_all(blocks, "head", 0, 0)
    mine = exchanged
    own_full = lax.dynamic_slice_in_dim(w_out, head * columns, columns, 1)
    return own_full, mine


def local(
    activations,
    mod_table,
    step_index,
    block_mask,
    cache_index,
    w_qkv,
    q_gain,
    k_gain,
    pool_kv,
    w_out,
):
    slot = lax.axis_index("slot")
    head = lax.axis_index("head")
    core = slot % 2
    groups = lax.axis_size("head")
    span = activations.shape[0]
    heads = q_gain.shape[0] // HD
    blocks_q = span // BLOCK
    cache_len = cache_index.shape[1]

    own_full, mine = fetch_out_weight(w_out, head, core)
    slots = lax.axis_size("slot")
    pool_flat = pool_kv.reshape(1, pool_kv.shape[1], -1)
    same_core = [pool_flat] + [from_behind(pool_flat, "slot", 2 * k) for k in range(1, slots // 2)]
    same_core = jnp.concatenate(same_core, axis=0)

    onehot = (jnp.arange(mod_table.shape[0], dtype=jnp.int32) == step_index[slot]).astype(
        jnp.float32
    )
    modulation = jnp.einsum("n,nkd->kd", onehot, mod_table.astype(jnp.float32))
    inputs = activations.astype(jnp.float32)
    normed = inputs * lax.rsqrt(jnp.mean(inputs * inputs, axis=-1, keepdims=True) + 1e-06)
    hidden = (normed * (1.0 + modulation[1][None, :]) + modulation[0][None, :]).astype(jnp.bfloat16)
    width = heads * HD
    qkv = jnp.einsum("td,dkh->kth", hidden, w_qkv, preferred_element_type=jnp.float32)
    queries = head_norm(qkv[0], q_gain, heads).astype(jnp.bfloat16)
    keys = head_norm(qkv[1], k_gain, heads).astype(jnp.bfloat16)
    values = qkv[2].astype(jnp.bfloat16)
    local_kv = jnp.concatenate([keys.reshape(span, heads * HD), values], axis=1)
    before = from_behind(local_kv, "slot", 1)
    earlier = from_behind(local_kv, "slot", 2)
    rows = span // 2
    parts = rows // BLOCK
    width = heads * HD
    own_mask = lax.dynamic_index_in_dim(block_mask, slot, 0, keepdims=False)
    flat_queries = queries.reshape(span, width)
    own_bias = jnp.zeros((1, blocks_q, span), jnp.float32)
    states = [
        flash_local(flat_queries[p * rows : (p + 1) * rows], local_kv.reshape(1, span, 2 * width),
                    own_bias[:, p * parts : (p + 1) * parts], heads)
        for p in range(2)
    ]
    states, queries, before, earlier, same_core, mine = lax.optimization_barrier(
        (states, queries, before, earlier, same_core, mine)
    )
    other_core = lax.ppermute(same_core, "slot", [(i, i ^ 1) for i in range(slots)])
    own_mask = lax.dynamic_index_in_dim(block_mask, slot, 0, keepdims=False)
    own_cache = lax.dynamic_index_in_dim(cache_index, slot, 0, keepdims=False)
    sibling_slot = jnp.bitwise_xor(slot, 1)
    own_cache = jnp.where(
        own_cache % 2 == core,
        ((slot - own_cache) % slots) // 2,
        slots // 2 + ((sibling_slot - own_cache) % slots) // 2,
    ).astype(jnp.int32)
    width = heads * HD
    local_stack = jnp.stack([before, earlier]).reshape(2, span, 2 * width)
    visible = jnp.concatenate([jnp.ones((blocks_q, blocks_q), jnp.int32), own_mask], axis=1)
    visible = jnp.transpose(visible.reshape(blocks_q, 3 + cache_len, blocks_q), (1, 0, 2))
    visible = jnp.repeat(visible, BLOCK, axis=2)
    bias = jnp.where(visible > 0, 0.0, -1e30).astype(jnp.float32)
    rows = span // 2
    parts = rows // BLOCK
    queries = queries.reshape(span, width)
    mixed_parts = [
        flash(queries[p * rows : (p + 1) * rows], local_stack, same_core, other_core,
              bias[1:, p * parts : (p + 1) * parts], own_cache, states[p], heads)
        for p in range(2)
    ]
    sibling = lax.ppermute(
        mine, "slot", [(i, i ^ 1) for i in range(slots)]
    )

    received = [
        jnp.concatenate([
            lax.ppermute(part, "head", [(i, (i + shift) % groups) for i in range(groups)])
            for part in mixed_parts
        ], axis=0)
        for shift in range(1, groups)
    ]
    mixed = jnp.concatenate(mixed_parts, axis=0)
    columns = own_full.shape[1]
    half = columns // 2
    attn = jnp.dot(mixed, own_full, preferred_element_type=jnp.float32).astype(jnp.bfloat16).astype(jnp.float32)
    attn_mine = None
    attn_sib = None
    for shift in range(1, groups):
        group_o = received[shift - 1]
        group = (head - shift) % groups
        mine_block = lax.dynamic_index_in_dim(mine, group, 0, keepdims=False)
        part = jnp.dot(group_o, mine_block, preferred_element_type=jnp.float32)
        part = part.astype(jnp.bfloat16).astype(jnp.float32)
        attn_mine = part if attn_mine is None else attn_mine + part
        sibling_block = lax.dynamic_index_in_dim(sibling, group, 0, keepdims=False)
        part = jnp.dot(group_o, sibling_block, preferred_element_type=jnp.float32)
        part = part.astype(jnp.bfloat16).astype(jnp.float32)
        attn_sib = part if attn_sib is None else attn_sib + part
    other = jnp.concatenate([attn_mine, attn_sib], axis=1)
    swapped = jnp.concatenate([attn_sib, attn_mine], axis=1)
    attn = attn + jnp.where(core == 0, other, swapped)

    offset = head * columns
    input_cols = lax.dynamic_slice_in_dim(activations, offset, columns, 1).astype(jnp.float32)
    gate_cols = lax.dynamic_slice_in_dim(modulation[2], offset, columns, 0)
    return input_cols + gate_cols[None, :] * attn


def solution(mesh):
    placed = (
        P("slot", None),
        P(),
        P(),
        P(),
        P(),
        P(None, None, "head"),
        P("head"),
        P("head"),
        P("slot", None, None, "head"),
        P("head", None),
    )
    return jax.shard_map(
        local, mesh=mesh, in_specs=placed, out_specs=P("slot", "head"), check_vma=False
    )
```

```python
import jax
import jax.numpy as jnp
from jax import lax
from jax.sharding import PartitionSpec as P
from jax.experimental import pallas as pl
from jax.experimental.pallas import tpu as pltpu

HD = 128
BLOCK = 128


def from_behind(shard, axis, by):
    length = lax.axis_size(axis)
    return lax.ppermute(shard, axis, [(i, (i + by) % length) for i in range(length)])


def head_norm(values, gain, heads):
    outs = []
    for h in range(heads):
        cols = slice(h * HD, (h + 1) * HD)
        piece = values[:, cols]
        scaled = piece * lax.rsqrt(jnp.mean(piece * piece, axis=-1, keepdims=True) + 1e-06)
        outs.append(scaled * gain[cols][None, :])
    return jnp.concatenate(outs, axis=1)


def attend(state, queries, span_kv, visible_blocks):
    highest, totals, accum = state
    heads = queries.shape[1]
    span_keys = span_kv[:, 0].reshape(span_kv.shape[0], heads, HD)
    span_values = span_kv[:, 1].reshape(span_kv.shape[0], heads, HD)
    visible = jnp.repeat(jnp.repeat(visible_blocks, BLOCK, axis=0), BLOCK, axis=1) > 0
    scores = jnp.einsum("qhd,khd->hqk", queries, span_keys, preferred_element_type=jnp.float32) * (
        1.0 / HD**0.5
    )
    scores = jnp.where(visible[None], scores, -1e30)
    new_high = jnp.maximum(highest, jnp.max(scores, axis=-1))
    factor = jnp.exp(highest - new_high)
    weights = jnp.where(visible[None], jnp.exp(scores - new_high[..., None]), 0.0)
    totals = totals * factor + jnp.sum(weights, axis=-1)
    accum = accum * factor[..., None] + jnp.einsum(
        "hqk,khd->hqd",
        weights.astype(jnp.bfloat16),
        span_values,
        preferred_element_type=jnp.float32,
    )
    return (new_high, totals, accum)


def online_update(q_ref, k_ref, v_ref, bias_ref, m_sc, l_sc, acc_sc, heads):
    span = q_ref.shape[0]
    blocks = bias_ref.shape[0]
    bias = bias_ref[...][:, None, :]
    for h in range(heads):
        cols = slice(h * HD, (h + 1) * HD)
        q = q_ref[:, cols]
        k = k_ref[:, cols]
        s = lax.dot_general(q, k, (((1,), (1,)), ((), ())), preferred_element_type=jnp.float32)
        s = (s * (1.0 / HD**0.5)).reshape(blocks, span // blocks, s.shape[1]) + bias
        s = s.reshape(span, -1)
        m_prev = m_sc[h]
        m_new = jnp.maximum(m_prev, jnp.max(s, axis=1, keepdims=True))
        factor = jnp.exp(m_prev - m_new)
        p = jnp.exp(s - m_new)
        l_sc[h] = l_sc[h] * factor + jnp.sum(p, axis=1, keepdims=True)
        acc_sc[h] = acc_sc[h] * factor + jnp.dot(
            p.astype(jnp.bfloat16), v_ref[:, cols], preferred_element_type=jnp.float32
        )
        m_sc[h] = m_new


def local_kernel(q_ref, k_ref, v_ref, bias_ref, m_ref, l_ref, acc_ref, *, heads):
    @pl.when(pl.program_id(0) == 0)
    def _():
        m_ref[...] = jnp.full(m_ref.shape, -1e30, jnp.float32)
        l_ref[...] = jnp.zeros(l_ref.shape, jnp.float32)
        acc_ref[...] = jnp.zeros(acc_ref.shape, jnp.float32)

    online_update(q_ref, k_ref, v_ref, bias_ref, m_ref, l_ref, acc_ref, heads)


def flash_local(queries, local_stack, bias, heads):
    span, width = queries.shape
    steps, keys_len = local_stack.shape[:2]
    blocks = bias.shape[1]
    kv_block = (None, keys_len, width)
    state = pl.BlockSpec((heads, span, 1), lambda j: (0, 0, 0))
    kernel = lambda *refs: local_kernel(*refs, heads=heads)
    return pl.pallas_call(
        kernel,
        grid=(steps,),
        in_specs=[
            pl.BlockSpec((span, width), lambda j: (0, 0)),
            pl.BlockSpec(kv_block, lambda j: (j, 0, 0)),
            pl.BlockSpec(kv_block, lambda j: (j, 0, 1)),
            pl.BlockSpec((None, blocks, keys_len), lambda j: (j, 0, 0)),
        ],
        out_specs=[state, state, pl.BlockSpec((heads, span, HD), lambda j: (0, 0, 0))],
        out_shape=[
            jax.ShapeDtypeStruct((heads, span, 1), jnp.float32),
            jax.ShapeDtypeStruct((heads, span, 1), jnp.float32),
            jax.ShapeDtypeStruct((heads, span, HD), jnp.float32),
        ],
        compiler_params=pltpu.CompilerParams(dimension_semantics=("arbitrary",)),
        cost_estimate=pl.CostEstimate(
            flops=4 * steps * heads * span * keys_len * HD,
            transcendentals=steps * heads * span * keys_len,
            bytes_accessed=2 * steps * keys_len * width * 2,
        ),
    )(queries, local_stack, local_stack, bias)


def flash_kernel(chosen, q_ref, k1_ref, v1_ref, k2_ref, v2_ref, ak_ref, av_ref, bk_ref, bv_ref, bias_ref, m_in, l_in, acc_in, o_ref, m_sc, l_sc, acc_sc, *, heads, n_local, half):
    step = pl.program_id(0)
    span = q_ref.shape[0]
    blocks = bias_ref.shape[0]

    @pl.when(step == 0)
    def _():
        m_sc[...] = m_in[...]
        l_sc[...] = l_in[...]
        acc_sc[...] = acc_in[...]

    def body(k_ref, v_ref):
        bias = bias_ref[...][:, None, :]
        for h in range(heads):
            cols = slice(h * HD, (h + 1) * HD)
            q = q_ref[:, cols]
            k = k_ref[:, cols]
            s = lax.dot_general(q, k, (((1,), (1,)), ((), ())), preferred_element_type=jnp.float32)
            s = (s * (1.0 / HD**0.5)).reshape(blocks, span // blocks, s.shape[1]) + bias
            s = s.reshape(span, -1)
            m_prev = m_sc[h]
            m_new = jnp.maximum(m_prev, jnp.max(s, axis=1, keepdims=True))
            factor = jnp.exp(m_prev - m_new)
            p = jnp.exp(s - m_new)
            l_sc[h] = l_sc[h] * factor + jnp.sum(p, axis=1, keepdims=True)
            acc_sc[h] = acc_sc[h] * factor + jnp.dot(
                p.astype(jnp.bfloat16), v_ref[:, cols], preferred_element_type=jnp.float32
            )
            m_sc[h] = m_new

    @pl.when(step == 0)
    def _():
        body(k1_ref, v1_ref)

    @pl.when(step == 1)
    def _():
        body(k2_ref, v2_ref)

    pos = chosen[jnp.maximum(step - n_local, 0)]

    @pl.when((step >= n_local) & (pos < half))
    def _():
        body(ak_ref, av_ref)

    @pl.when((step >= n_local) & (pos >= half))
    def _():
        body(bk_ref, bv_ref)

    @pl.when(step == pl.num_programs(0) - 1)
    def _():
        for h in range(heads):
            cols = slice(h * HD, (h + 1) * HD)
            o_ref[:, cols] = (acc_sc[h] / l_sc[h]).astype(o_ref.dtype)


def flash(queries, before, earlier, same_core, other_core, bias, chosen, state, heads):
    span, width = queries.shape
    n_local = 2
    half = same_core.shape[0]
    steps = n_local + chosen.shape[0]
    blocks = bias.shape[1]

    def local_map(kv):
        return lambda j, c: (jnp.minimum(j, n_local - 1), 0, kv)

    def pool_map(kv, upper):
        def index(j, c):
            pos = c[jnp.maximum(j - n_local, 0)]
            hit = (j >= n_local) & ((pos >= half) == upper)
            return (jnp.where(hit, pos - upper * half, 0), 0, kv)

        return index

    keys_len = before.shape[0]
    kv_block = (None, keys_len, width)
    grid_spec = pltpu.PrefetchScalarGridSpec(
        num_scalar_prefetch=1,
        grid=(steps,),
        in_specs=[
            pl.BlockSpec((span, width), lambda j, c: (0, 0)),
            pl.BlockSpec((keys_len, width), lambda j, c: (0, 0)),
            pl.BlockSpec((keys_len, width), lambda j, c: (0, 1)),
            pl.BlockSpec((keys_len, width), lambda j, c: (0, 0)),
            pl.BlockSpec((keys_len, width), lambda j, c: (0, 1)),
            pl.BlockSpec(kv_block, pool_map(0, False)),
            pl.BlockSpec(kv_block, pool_map(1, False)),
            pl.BlockSpec(kv_block, pool_map(0, True)),
            pl.BlockSpec(kv_block, pool_map(1, True)),
            pl.BlockSpec((None, blocks, keys_len), lambda j, c: (j, 0, 0)),
            pl.BlockSpec((heads, span, 1), lambda j, c: (0, 0, 0)),
            pl.BlockSpec((heads, span, 1), lambda j, c: (0, 0, 0)),
            pl.BlockSpec((heads, span, HD), lambda j, c: (0, 0, 0)),
        ],
        out_specs=pl.BlockSpec((span, width), lambda j, c: (0, 0)),
        scratch_shapes=[
            pltpu.VMEM((heads, span, 1), jnp.float32),
            pltpu.VMEM((heads, span, 1), jnp.float32),
            pltpu.VMEM((heads, span, HD), jnp.float32),
        ],
    )
    kernel = lambda *refs: flash_kernel(*refs, heads=heads, n_local=n_local, half=half)
    return pl.pallas_call(
        kernel,
        grid_spec=grid_spec,
        out_shape=jax.ShapeDtypeStruct((span, width), jnp.bfloat16),
        compiler_params=pltpu.CompilerParams(dimension_semantics=("arbitrary",)),
        cost_estimate=pl.CostEstimate(
            flops=4 * steps * heads * span * span * HD,
            transcendentals=steps * heads * span * span,
            bytes_accessed=2 * steps * span * width * 2,
        ),
    )(chosen, queries, before, before, earlier, earlier, same_core, same_core, other_core, other_core, bias, *state)


def fetch_out_weight(w_out, head, core):
    groups = lax.axis_size("head")
    columns = w_out.shape[1] // groups
    half = columns // 2
    blocks = jnp.stack([
        lax.dynamic_slice_in_dim(w_out, dest * columns + core * half, half, 1)
        for dest in range(groups)
    ])
    exchanged = lax.all_to_all(blocks, "head", 0, 0)
    mine = exchanged
    own_full = lax.dynamic_slice_in_dim(w_out, head * columns, columns, 1)
    return own_full, mine


def local(
    activations,
    mod_table,
    step_index,
    block_mask,
    cache_index,
    w_qkv,
    q_gain,
    k_gain,
    pool_kv,
    w_out,
):
    slot = lax.axis_index("slot")
    head = lax.axis_index("head")
    core = slot % 2
    groups = lax.axis_size("head")
    span = activations.shape[0]
    heads = q_gain.shape[0] // HD
    blocks_q = span // BLOCK
    cache_len = cache_index.shape[1]

    own_full, mine = fetch_out_weight(w_out, head, core)
    slots = lax.axis_size("slot")
    pool_flat = pool_kv.reshape(1, pool_kv.shape[1], -1)
    same_core = [pool_flat] + [from_behind(pool_flat, "slot", 2 * k) for k in range(1, slots // 2)]
    same_core = jnp.concatenate(same_core, axis=0)

    onehot = (jnp.arange(mod_table.shape[0], dtype=jnp.int32) == step_index[slot]).astype(
        jnp.float32
    )
    modulation = jnp.einsum("n,nkd->kd", onehot, mod_table.astype(jnp.float32))
    inputs = activations.astype(jnp.float32)
    normed = inputs * lax.rsqrt(jnp.mean(inputs * inputs, axis=-1, keepdims=True) + 1e-06)
    hidden = (normed * (1.0 + modulation[1][None, :]) + modulation[0][None, :]).astype(jnp.bfloat16)
    width = heads * HD
    qkv = jnp.einsum("td,dkh->kth", hidden, w_qkv, preferred_element_type=jnp.float32)
    queries = head_norm(qkv[0], q_gain, heads).astype(jnp.bfloat16)
    keys = head_norm(qkv[1], k_gain, heads).astype(jnp.bfloat16)
    values = qkv[2].astype(jnp.bfloat16)
    local_kv = jnp.concatenate([keys.reshape(span, heads * HD), values], axis=1)
    before = from_behind(local_kv, "slot", 1)
    earlier = from_behind(local_kv, "slot", 2)
    rows = span // 2
    parts = rows // BLOCK
    width = heads * HD
    own_mask = lax.dynamic_index_in_dim(block_mask, slot, 0, keepdims=False)
    flat_queries = queries.reshape(span, width)
    own_bias = jnp.zeros((1, blocks_q, span), jnp.float32)
    states = [
        flash_local(flat_queries[p * rows : (p + 1) * rows], local_kv.reshape(1, span, 2 * width),
                    own_bias[:, p * parts : (p + 1) * parts], heads)
        for p in range(2)
    ]
    states, queries, before, earlier, same_core, mine = lax.optimization_barrier(
        (states, queries, before, earlier, same_core, mine)
    )
    other_core = lax.ppermute(same_core, "slot", [(i, i ^ 1) for i in range(slots)])
    own_mask = lax.dynamic_index_in_dim(block_mask, slot, 0, keepdims=False)
    own_cache = lax.dynamic_index_in_dim(cache_index, slot, 0, keepdims=False)
    sibling_slot = jnp.bitwise_xor(slot, 1)
    own_cache = jnp.where(
        own_cache % 2 == core,
        ((slot - own_cache) % slots) // 2,
        slots // 2 + ((sibling_slot - own_cache) % slots) // 2,
    ).astype(jnp.int32)
    width = heads * HD
    visible = jnp.concatenate([jnp.ones((blocks_q, blocks_q), jnp.int32), own_mask], axis=1)
    visible = jnp.transpose(visible.reshape(blocks_q, 3 + cache_len, blocks_q), (1, 0, 2))
    visible = jnp.repeat(visible, BLOCK, axis=2)
    bias = jnp.where(visible > 0, 0.0, -1e30).astype(jnp.float32)
    rows = span // 2
    parts = rows // BLOCK
    queries = queries.reshape(span, width)
    mixed_parts = [
        flash(queries[p * rows : (p + 1) * rows], before, earlier, same_core, other_core,
              bias[1:, p * parts : (p + 1) * parts], own_cache, states[p], heads)
        for p in range(2)
    ]
    sibling = lax.ppermute(
        mine, "slot", [(i, i ^ 1) for i in range(slots)]
    )

    received = [
        jnp.concatenate([
            lax.ppermute(part, "head", [(i, (i + shift) % groups) for i in range(groups)])
            for part in mixed_parts
        ], axis=0)
        for shift in range(1, groups)
    ]
    mixed = jnp.concatenate(mixed_parts, axis=0)
    columns = own_full.shape[1]
    half = columns // 2
    attn = jnp.dot(mixed, own_full, preferred_element_type=jnp.float32).astype(jnp.bfloat16).astype(jnp.float32)
    attn_mine = None
    attn_sib = None
    for shift in range(1, groups):
        group_o = received[shift - 1]
        group = (head - shift) % groups
        mine_block = lax.dynamic_index_in_dim(mine, group, 0, keepdims=False)
        part = jnp.dot(group_o, mine_block, preferred_element_type=jnp.float32)
        part = part.astype(jnp.bfloat16).astype(jnp.float32)
        attn_mine = part if attn_mine is None else attn_mine + part
        sibling_block = lax.dynamic_index_in_dim(sibling, group, 0, keepdims=False)
        part = jnp.dot(group_o, sibling_block, preferred_element_type=jnp.float32)
        part = part.astype(jnp.bfloat16).astype(jnp.float32)
        attn_sib = part if attn_sib is None else attn_sib + part
    other = jnp.concatenate([attn_mine, attn_sib], axis=1)
    swapped = jnp.concatenate([attn_sib, attn_mine], axis=1)
    attn = attn + jnp.where(core == 0, other, swapped)

    offset = head * columns
    input_cols = lax.dynamic_slice_in_dim(activations, offset, columns, 1).astype(jnp.float32)
    gate_cols = lax.dynamic_slice_in_dim(modulation[2], offset, columns, 0)
    return input_cols + gate_cols[None, :] * attn


def solution(mesh):
    placed = (
        P("slot", None),
        P(),
        P(),
        P(),
        P(),
        P(None, None, "head"),
        P("head"),
        P("head"),
        P("slot", None, None, "head"),
        P("head", None),
    )
    return jax.shard_map(
        local, mesh=mesh, in_specs=placed, out_specs=P("slot", "head"), check_vma=False
    )
```

```python
import jax
import jax.numpy as jnp
from jax import lax
from jax.sharding import PartitionSpec as P
from jax.experimental import pallas as pl
from jax.experimental.pallas import tpu as pltpu

HD = 128
BLOCK = 128


def from_behind(shard, axis, by):
    length = lax.axis_size(axis)
    return lax.ppermute(shard, axis, [(i, (i + by) % length) for i in range(length)])


def head_norm(values, gain, heads):
    outs = []
    for h in range(heads):
        cols = slice(h * HD, (h + 1) * HD)
        piece = values[:, cols]
        scaled = piece * lax.rsqrt(jnp.mean(piece * piece, axis=-1, keepdims=True) + 1e-06)
        outs.append(scaled * gain[cols][None, :])
    return jnp.concatenate(outs, axis=1)


def attend(state, queries, span_kv, visible_blocks):
    highest, totals, accum = state
    heads = queries.shape[1]
    span_keys = span_kv[:, 0].reshape(span_kv.shape[0], heads, HD)
    span_values = span_kv[:, 1].reshape(span_kv.shape[0], heads, HD)
    visible = jnp.repeat(jnp.repeat(visible_blocks, BLOCK, axis=0), BLOCK, axis=1) > 0
    scores = jnp.einsum("qhd,khd->hqk", queries, span_keys, preferred_element_type=jnp.float32) * (
        1.0 / HD**0.5
    )
    scores = jnp.where(visible[None], scores, -1e30)
    new_high = jnp.maximum(highest, jnp.max(scores, axis=-1))
    factor = jnp.exp(highest - new_high)
    weights = jnp.where(visible[None], jnp.exp(scores - new_high[..., None]), 0.0)
    totals = totals * factor + jnp.sum(weights, axis=-1)
    accum = accum * factor[..., None] + jnp.einsum(
        "hqk,khd->hqd",
        weights.astype(jnp.bfloat16),
        span_values,
        preferred_element_type=jnp.float32,
    )
    return (new_high, totals, accum)


def online_update(q_ref, k_ref, v_ref, bias_ref, m_sc, l_sc, acc_sc, heads):
    span = q_ref.shape[0]
    blocks = bias_ref.shape[0]
    bias = bias_ref[...][:, None, :]
    for h in range(heads):
        cols = slice(h * HD, (h + 1) * HD)
        q = q_ref[:, cols]
        k = k_ref[:, cols]
        s = lax.dot_general(q, k, (((1,), (1,)), ((), ())), preferred_element_type=jnp.float32)
        s = (s * (1.0 / HD**0.5)).reshape(blocks, span // blocks, s.shape[1]) + bias
        s = s.reshape(span, -1)
        m_prev = m_sc[h]
        m_new = jnp.maximum(m_prev, jnp.max(s, axis=1, keepdims=True))
        factor = jnp.exp(m_prev - m_new)
        p = jnp.exp(s - m_new)
        l_sc[h] = l_sc[h] * factor + jnp.sum(p, axis=1, keepdims=True)
        acc_sc[h] = acc_sc[h] * factor + jnp.dot(
            p.astype(jnp.bfloat16), v_ref[:, cols], preferred_element_type=jnp.float32
        )
        m_sc[h] = m_new


def local_kernel(q_ref, k_ref, v_ref, bias_ref, m_ref, l_ref, acc_ref, *, heads):
    @pl.when(pl.program_id(0) == 0)
    def _():
        m_ref[...] = jnp.full(m_ref.shape, -1e30, jnp.float32)
        l_ref[...] = jnp.zeros(l_ref.shape, jnp.float32)
        acc_ref[...] = jnp.zeros(acc_ref.shape, jnp.float32)

    online_update(q_ref, k_ref, v_ref, bias_ref, m_ref, l_ref, acc_ref, heads)


def flash_local(queries, local_stack, bias, heads):
    span, width = queries.shape
    steps, keys_len = local_stack.shape[:2]
    blocks = bias.shape[1]
    kv_block = (None, keys_len, width)
    state = pl.BlockSpec((heads, span, 1), lambda j: (0, 0, 0))
    kernel = lambda *refs: local_kernel(*refs, heads=heads)
    return pl.pallas_call(
        kernel,
        grid=(steps,),
        in_specs=[
            pl.BlockSpec((span, width), lambda j: (0, 0)),
            pl.BlockSpec(kv_block, lambda j: (j, 0, 0)),
            pl.BlockSpec(kv_block, lambda j: (j, 0, 1)),
            pl.BlockSpec((None, blocks, keys_len), lambda j: (j, 0, 0)),
        ],
        out_specs=[state, state, pl.BlockSpec((heads, span, HD), lambda j: (0, 0, 0))],
        out_shape=[
            jax.ShapeDtypeStruct((heads, span, 1), jnp.float32),
            jax.ShapeDtypeStruct((heads, span, 1), jnp.float32),
            jax.ShapeDtypeStruct((heads, span, HD), jnp.float32),
        ],
        compiler_params=pltpu.CompilerParams(dimension_semantics=("arbitrary",)),
        cost_estimate=pl.CostEstimate(
            flops=4 * steps * heads * span * keys_len * HD,
            transcendentals=steps * heads * span * keys_len,
            bytes_accessed=2 * steps * keys_len * width * 2,
        ),
    )(queries, local_stack, local_stack, bias)


def flash_kernel(chosen, q_ref, k1_ref, v1_ref, k2_ref, v2_ref, ak_ref, av_ref, ck_ref, cv_ref, bk_ref, bv_ref, bias_ref, m_in, l_in, acc_in, o_ref, m_sc, l_sc, acc_sc, *, heads, n_local, half):
    step = pl.program_id(0)
    span = q_ref.shape[0]
    blocks = bias_ref.shape[0]

    @pl.when(step == 0)
    def _():
        m_sc[...] = m_in[...]
        l_sc[...] = l_in[...]
        acc_sc[...] = acc_in[...]

    def body(k_ref, v_ref):
        bias = bias_ref[...][:, None, :]
        for h in range(heads):
            cols = slice(h * HD, (h + 1) * HD)
            q = q_ref[:, cols]
            k = k_ref[:, cols]
            s = lax.dot_general(q, k, (((1,), (1,)), ((), ())), preferred_element_type=jnp.float32)
            s = (s * (1.0 / HD**0.5)).reshape(blocks, span // blocks, s.shape[1]) + bias
            s = s.reshape(span, -1)
            m_prev = m_sc[h]
            m_new = jnp.maximum(m_prev, jnp.max(s, axis=1, keepdims=True))
            factor = jnp.exp(m_prev - m_new)
            p = jnp.exp(s - m_new)
            l_sc[h] = l_sc[h] * factor + jnp.sum(p, axis=1, keepdims=True)
            acc_sc[h] = acc_sc[h] * factor + jnp.dot(
                p.astype(jnp.bfloat16), v_ref[:, cols], preferred_element_type=jnp.float32
            )
            m_sc[h] = m_new

    @pl.when(step == 0)
    def _():
        body(k1_ref, v1_ref)

    @pl.when(step == 1)
    def _():
        body(k2_ref, v2_ref)

    pos = chosen[jnp.maximum(step - n_local, 0)]

    @pl.when((step >= n_local) & (pos < half))
    def _():
        body(ak_ref, av_ref)

    @pl.when((step >= n_local) & (pos == half))
    def _():
        body(ck_ref, cv_ref)

    @pl.when((step >= n_local) & (pos > half))
    def _():
        body(bk_ref, bv_ref)

    @pl.when(step == pl.num_programs(0) - 1)
    def _():
        for h in range(heads):
            cols = slice(h * HD, (h + 1) * HD)
            o_ref[:, cols] = (acc_sc[h] / l_sc[h]).astype(o_ref.dtype)


def flash(queries, before, earlier, same_core, sibling_own, other_core, bias, chosen, state, heads):
    span, width = queries.shape
    n_local = 2
    half = same_core.shape[0]
    steps = n_local + chosen.shape[0]
    blocks = bias.shape[1]

    def local_map(kv):
        return lambda j, c: (jnp.minimum(j, n_local - 1), 0, kv)

    def pool_map(kv, upper):
        def index(j, c):
            pos = c[jnp.maximum(j - n_local, 0)]
            if upper:
                hit = (j >= n_local) & (pos > half)
                return (jnp.where(hit, pos - half - 1, 0), 0, kv)
            hit = (j >= n_local) & (pos < half)
            return (jnp.where(hit, pos, 0), 0, kv)

        return index

    keys_len = before.shape[0]
    kv_block = (None, keys_len, width)
    grid_spec = pltpu.PrefetchScalarGridSpec(
        num_scalar_prefetch=1,
        grid=(steps,),
        in_specs=[
            pl.BlockSpec((span, width), lambda j, c: (0, 0)),
            pl.BlockSpec((keys_len, width), lambda j, c: (0, 0)),
            pl.BlockSpec((keys_len, width), lambda j, c: (0, 1)),
            pl.BlockSpec((keys_len, width), lambda j, c: (0, 0)),
            pl.BlockSpec((keys_len, width), lambda j, c: (0, 1)),
            pl.BlockSpec(kv_block, pool_map(0, False)),
            pl.BlockSpec(kv_block, pool_map(1, False)),
            pl.BlockSpec(kv_block, lambda j, c: (0, 0, 0)),
            pl.BlockSpec(kv_block, lambda j, c: (0, 0, 1)),
            pl.BlockSpec(kv_block, pool_map(0, True)),
            pl.BlockSpec(kv_block, pool_map(1, True)),
            pl.BlockSpec((None, blocks, keys_len), lambda j, c: (j, 0, 0)),
            pl.BlockSpec((heads, span, 1), lambda j, c: (0, 0, 0)),
            pl.BlockSpec((heads, span, 1), lambda j, c: (0, 0, 0)),
            pl.BlockSpec((heads, span, HD), lambda j, c: (0, 0, 0)),
        ],
        out_specs=pl.BlockSpec((span, width), lambda j, c: (0, 0)),
        scratch_shapes=[
            pltpu.VMEM((heads, span, 1), jnp.float32),
            pltpu.VMEM((heads, span, 1), jnp.float32),
            pltpu.VMEM((heads, span, HD), jnp.float32),
        ],
    )
    kernel = lambda *refs: flash_kernel(*refs, heads=heads, n_local=n_local, half=half)
    return pl.pallas_call(
        kernel,
        grid_spec=grid_spec,
        out_shape=jax.ShapeDtypeStruct((span, width), jnp.bfloat16),
        compiler_params=pltpu.CompilerParams(dimension_semantics=("arbitrary",)),
        cost_estimate=pl.CostEstimate(
            flops=4 * steps * heads * span * span * HD,
            transcendentals=steps * heads * span * span,
            bytes_accessed=2 * steps * span * width * 2,
        ),
    )(chosen, queries, before, before, earlier, earlier, same_core, same_core, sibling_own, sibling_own, other_core, other_core, bias, *state)


def fetch_out_weight(w_out, head, core):
    groups = lax.axis_size("head")
    columns = w_out.shape[1] // groups
    half = columns // 2
    blocks = jnp.stack([
        lax.dynamic_slice_in_dim(w_out, dest * columns + core * half, half, 1)
        for dest in range(groups)
    ])
    exchanged = lax.all_to_all(blocks, "head", 0, 0)
    mine = exchanged
    own_full = lax.dynamic_slice_in_dim(w_out, head * columns, columns, 1)
    return own_full, mine


def local(
    activations,
    mod_table,
    step_index,
    block_mask,
    cache_index,
    w_qkv,
    q_gain,
    k_gain,
    pool_kv,
    w_out,
):
    slot = lax.axis_index("slot")
    head = lax.axis_index("head")
    core = slot % 2
    groups = lax.axis_size("head")
    span = activations.shape[0]
    heads = q_gain.shape[0] // HD
    blocks_q = span // BLOCK
    cache_len = cache_index.shape[1]

    own_full, mine = fetch_out_weight(w_out, head, core)
    slots = lax.axis_size("slot")
    pool_flat = pool_kv.reshape(1, pool_kv.shape[1], -1)
    same_core = [pool_flat] + [from_behind(pool_flat, "slot", 2 * k) for k in range(1, slots // 2)]
    same_core = jnp.concatenate(same_core, axis=0)

    onehot = (jnp.arange(mod_table.shape[0], dtype=jnp.int32) == step_index[slot]).astype(
        jnp.float32
    )
    modulation = jnp.einsum("n,nkd->kd", onehot, mod_table.astype(jnp.float32))
    inputs = activations.astype(jnp.float32)
    normed = inputs * lax.rsqrt(jnp.mean(inputs * inputs, axis=-1, keepdims=True) + 1e-06)
    hidden = (normed * (1.0 + modulation[1][None, :]) + modulation[0][None, :]).astype(jnp.bfloat16)
    width = heads * HD
    qkv = jnp.einsum("td,dkh->kth", hidden, w_qkv, preferred_element_type=jnp.float32)
    queries = head_norm(qkv[0], q_gain, heads).astype(jnp.bfloat16)
    keys = head_norm(qkv[1], k_gain, heads).astype(jnp.bfloat16)
    values = qkv[2].astype(jnp.bfloat16)
    local_kv = jnp.concatenate([keys.reshape(span, heads * HD), values], axis=1)
    before = from_behind(local_kv, "slot", 1)
    earlier = from_behind(local_kv, "slot", 2)
    rows = span // 2
    parts = rows // BLOCK
    width = heads * HD
    own_mask = lax.dynamic_index_in_dim(block_mask, slot, 0, keepdims=False)
    flat_queries = queries.reshape(span, width)
    own_bias = jnp.zeros((1, blocks_q, span), jnp.float32)
    states = [
        flash_local(flat_queries[p * rows : (p + 1) * rows], local_kv.reshape(1, span, 2 * width),
                    own_bias[:, p * parts : (p + 1) * parts], heads)
        for p in range(2)
    ]
    sibling_own = lax.ppermute(pool_flat, "slot", [(i, i ^ 1) for i in range(slots)])
    states, queries, before, earlier, same_core, sibling_own, mine = lax.optimization_barrier(
        (states, queries, before, earlier, same_core, sibling_own, mine)
    )
    other_core = lax.ppermute(same_core[1:], "slot", [(i, i ^ 1) for i in range(slots)])
    own_mask = lax.dynamic_index_in_dim(block_mask, slot, 0, keepdims=False)
    own_cache = lax.dynamic_index_in_dim(cache_index, slot, 0, keepdims=False)
    sibling_slot = jnp.bitwise_xor(slot, 1)
    own_cache = jnp.where(
        own_cache % 2 == core,
        ((slot - own_cache) % slots) // 2,
        slots // 2 + ((sibling_slot - own_cache) % slots) // 2,
    ).astype(jnp.int32)
    width = heads * HD
    visible = jnp.concatenate([jnp.ones((blocks_q, blocks_q), jnp.int32), own_mask], axis=1)
    visible = jnp.transpose(visible.reshape(blocks_q, 3 + cache_len, blocks_q), (1, 0, 2))
    visible = jnp.repeat(visible, BLOCK, axis=2)
    bias = jnp.where(visible > 0, 0.0, -1e30).astype(jnp.float32)
    rows = span // 2
    parts = rows // BLOCK
    queries = queries.reshape(span, width)
    mixed_parts = [
        flash(queries[p * rows : (p + 1) * rows], before, earlier, same_core, sibling_own, other_core,
              bias[1:, p * parts : (p + 1) * parts], own_cache, states[p], heads)
        for p in range(2)
    ]
    sibling = lax.ppermute(
        mine, "slot", [(i, i ^ 1) for i in range(slots)]
    )

    received = [
        jnp.concatenate([
            lax.ppermute(part, "head", [(i, (i + shift) % groups) for i in range(groups)])
            for part in mixed_parts
        ], axis=0)
        for shift in range(1, groups)
    ]
    mixed = jnp.concatenate(mixed_parts, axis=0)
    columns = own_full.shape[1]
    half = columns // 2
    attn = jnp.dot(mixed, own_full, preferred_element_type=jnp.float32).astype(jnp.bfloat16).astype(jnp.float32)
    attn_mine = None
    attn_sib = None
    for shift in range(1, groups):
        group_o = received[shift - 1]
        group = (head - shift) % groups
        mine_block = lax.dynamic_index_in_dim(mine, group, 0, keepdims=False)
        part = jnp.dot(group_o, mine_block, preferred_element_type=jnp.float32)
        part = part.astype(jnp.bfloat16).astype(jnp.float32)
        attn_mine = part if attn_mine is None else attn_mine + part
        sibling_block = lax.dynamic_index_in_dim(sibling, group, 0, keepdims=False)
        part = jnp.dot(group_o, sibling_block, preferred_element_type=jnp.float32)
        part = part.astype(jnp.bfloat16).astype(jnp.float32)
        attn_sib = part if attn_sib is None else attn_sib + part
    other = jnp.concatenate([attn_mine, attn_sib], axis=1)
    swapped = jnp.concatenate([attn_sib, attn_mine], axis=1)
    attn = attn + jnp.where(core == 0, other, swapped)

    offset = head * columns
    input_cols = lax.dynamic_slice_in_dim(activations, offset, columns, 1).astype(jnp.float32)
    gate_cols = lax.dynamic_slice_in_dim(modulation[2], offset, columns, 0)
    return input_cols + gate_cols[None, :] * attn


def solution(mesh):
    placed = (
        P("slot", None),
        P(),
        P(),
        P(),
        P(),
        P(None, None, "head"),
        P("head"),
        P("head"),
        P("slot", None, None, "head"),
        P("head", None),
    )
    return jax.shard_map(
        local, mesh=mesh, in_specs=placed, out_specs=P("slot", "head"), check_vma=False
    )
```

```python
import jax
import jax.numpy as jnp
from jax import lax
from jax.sharding import PartitionSpec as P
from jax.experimental import pallas as pl
from jax.experimental.pallas import tpu as pltpu

HD = 128
BLOCK = 128


def from_behind(shard, axis, by):
    length = lax.axis_size(axis)
    return lax.ppermute(shard, axis, [(i, (i + by) % length) for i in range(length)])


def head_norm(values, gain, heads):
    outs = []
    for h in range(heads):
        cols = slice(h * HD, (h + 1) * HD)
        piece = values[:, cols]
        scaled = piece * lax.rsqrt(jnp.mean(piece * piece, axis=-1, keepdims=True) + 1e-06)
        outs.append(scaled * gain[cols][None, :])
    return jnp.concatenate(outs, axis=1)


def attend(state, queries, span_kv, visible_blocks):
    highest, totals, accum = state
    heads = queries.shape[1]
    span_keys = span_kv[:, 0].reshape(span_kv.shape[0], heads, HD)
    span_values = span_kv[:, 1].reshape(span_kv.shape[0], heads, HD)
    visible = jnp.repeat(jnp.repeat(visible_blocks, BLOCK, axis=0), BLOCK, axis=1) > 0
    scores = jnp.einsum("qhd,khd->hqk", queries, span_keys, preferred_element_type=jnp.float32) * (
        1.0 / HD**0.5
    )
    scores = jnp.where(visible[None], scores, -1e30)
    new_high = jnp.maximum(highest, jnp.max(scores, axis=-1))
    factor = jnp.exp(highest - new_high)
    weights = jnp.where(visible[None], jnp.exp(scores - new_high[..., None]), 0.0)
    totals = totals * factor + jnp.sum(weights, axis=-1)
    accum = accum * factor[..., None] + jnp.einsum(
        "hqk,khd->hqd",
        weights.astype(jnp.bfloat16),
        span_values,
        preferred_element_type=jnp.float32,
    )
    return (new_high, totals, accum)


def online_update(q_ref, k_ref, v_ref, bias_ref, m_sc, l_sc, acc_sc, heads):
    span = q_ref.shape[0]
    blocks = bias_ref.shape[0]
    bias = bias_ref[...][:, None, :]
    for h in range(heads):
        cols = slice(h * HD, (h + 1) * HD)
        q = q_ref[:, cols]
        k = k_ref[:, cols]
        s = lax.dot_general(q, k, (((1,), (1,)), ((), ())), preferred_element_type=jnp.float32)
        s = (s * (1.0 / HD**0.5)).reshape(blocks, span // blocks, s.shape[1]) + bias
        s = s.reshape(span, -1)
        m_prev = m_sc[h]
        m_new = jnp.maximum(m_prev, jnp.max(s, axis=1, keepdims=True))
        factor = jnp.exp(m_prev - m_new)
        p = jnp.exp(s - m_new)
        l_sc[h] = l_sc[h] * factor + jnp.sum(p, axis=1, keepdims=True)
        acc_sc[h] = acc_sc[h] * factor + jnp.dot(
            p.astype(jnp.bfloat16), v_ref[:, cols], preferred_element_type=jnp.float32
        )
        m_sc[h] = m_new


def local_kernel(q_ref, k_ref, v_ref, bias_ref, m_ref, l_ref, acc_ref, *, heads):
    @pl.when(pl.program_id(0) == 0)
    def _():
        m_ref[...] = jnp.full(m_ref.shape, -1e30, jnp.float32)
        l_ref[...] = jnp.zeros(l_ref.shape, jnp.float32)
        acc_ref[...] = jnp.zeros(acc_ref.shape, jnp.float32)

    online_update(q_ref, k_ref, v_ref, bias_ref, m_ref, l_ref, acc_ref, heads)


def flash_local(queries, local_stack, bias, heads):
    span, width = queries.shape
    steps, keys_len = local_stack.shape[:2]
    blocks = bias.shape[1]
    kv_block = (None, keys_len, width)
    state = pl.BlockSpec((heads, span, 1), lambda j: (0, 0, 0))
    kernel = lambda *refs: local_kernel(*refs, heads=heads)
    return pl.pallas_call(
        kernel,
        grid=(steps,),
        in_specs=[
            pl.BlockSpec((span, width), lambda j: (0, 0)),
            pl.BlockSpec(kv_block, lambda j: (j, 0, 0)),
            pl.BlockSpec(kv_block, lambda j: (j, 0, 1)),
            pl.BlockSpec((None, blocks, keys_len), lambda j: (j, 0, 0)),
        ],
        out_specs=[state, state, pl.BlockSpec((heads, span, HD), lambda j: (0, 0, 0))],
        out_shape=[
            jax.ShapeDtypeStruct((heads, span, 1), jnp.float32),
            jax.ShapeDtypeStruct((heads, span, 1), jnp.float32),
            jax.ShapeDtypeStruct((heads, span, HD), jnp.float32),
        ],
        compiler_params=pltpu.CompilerParams(dimension_semantics=("arbitrary",)),
        cost_estimate=pl.CostEstimate(
            flops=4 * steps * heads * span * keys_len * HD,
            transcendentals=steps * heads * span * keys_len,
            bytes_accessed=2 * steps * keys_len * width * 2,
        ),
    )(queries, local_stack, local_stack, bias)


def flash_kernel(chosen, q_ref, k1_ref, v1_ref, k2_ref, v2_ref, ak_ref, av_ref, ck_ref, cv_ref, bk_ref, bv_ref, bias_ref, m_in, l_in, acc_in, o_ref, m_sc, l_sc, acc_sc, *, heads, n_local, half):
    step = pl.program_id(0)
    span = q_ref.shape[0]
    blocks = bias_ref.shape[0]

    @pl.when(step == 0)
    def _():
        m_sc[...] = m_in[...]
        l_sc[...] = l_in[...]
        acc_sc[...] = acc_in[...]

    def body(k_ref, v_ref):
        bias = bias_ref[...][:, None, :]
        for h in range(heads):
            cols = slice(h * HD, (h + 1) * HD)
            q = q_ref[:, cols]
            k = k_ref[:, cols]
            s = lax.dot_general(q, k, (((1,), (1,)), ((), ())), preferred_element_type=jnp.float32)
            s = (s * (1.0 / HD**0.5)).reshape(blocks, span // blocks, s.shape[1]) + bias
            s = s.reshape(span, -1)
            m_prev = m_sc[h]
            m_new = jnp.maximum(m_prev, jnp.max(s, axis=1, keepdims=True))
            factor = jnp.exp(m_prev - m_new)
            p = jnp.exp(s - m_new)
            l_sc[h] = l_sc[h] * factor + jnp.sum(p, axis=1, keepdims=True)
            acc_sc[h] = acc_sc[h] * factor + jnp.dot(
                p.astype(jnp.bfloat16), v_ref[:, cols], preferred_element_type=jnp.float32
            )
            m_sc[h] = m_new

    @pl.when(step == 0)
    def _():
        body(k1_ref, v1_ref)

    @pl.when(step == 1)
    def _():
        body(k2_ref, v2_ref)

    pos = chosen[jnp.maximum(step - n_local, 0)]

    @pl.when((step >= n_local) & (pos < half))
    def _():
        body(ak_ref, av_ref)

    @pl.when((step >= n_local) & (pos == half))
    def _():
        body(ck_ref, cv_ref)

    @pl.when((step >= n_local) & (pos > half))
    def _():
        body(bk_ref, bv_ref)

    @pl.when(step == pl.num_programs(0) - 1)
    def _():
        for h in range(heads):
            cols = slice(h * HD, (h + 1) * HD)
            o_ref[:, cols] = (acc_sc[h] / l_sc[h]).astype(o_ref.dtype)


def flash(queries, before, earlier, same_core, sibling_own, other_core, bias, chosen, state, heads):
    span, width = queries.shape
    n_local = 2
    half = same_core.shape[0]
    steps = n_local + chosen.shape[0]
    blocks = bias.shape[1]

    def local_map(kv):
        return lambda j, c: (jnp.minimum(j, n_local - 1), 0, kv)

    def pool_map(kv, upper):
        def index(j, c):
            pos = c[jnp.maximum(j - n_local, 0)]
            if upper:
                hit = (j >= n_local) & (pos > half)
                return (jnp.where(hit, pos - half - 1, 0), 0, kv)
            hit = (j >= n_local) & (pos < half)
            return (jnp.where(hit, pos, 0), 0, kv)

        return index

    keys_len = before.shape[0]
    kv_block = (None, keys_len, width)
    grid_spec = pltpu.PrefetchScalarGridSpec(
        num_scalar_prefetch=1,
        grid=(steps,),
        in_specs=[
            pl.BlockSpec((span, width), lambda j, c: (0, 0)),
            pl.BlockSpec((keys_len, width), lambda j, c: (0, 0)),
            pl.BlockSpec((keys_len, width), lambda j, c: (0, 1)),
            pl.BlockSpec((keys_len, width), lambda j, c: (0, 0)),
            pl.BlockSpec((keys_len, width), lambda j, c: (0, 1)),
            pl.BlockSpec(kv_block, pool_map(0, False)),
            pl.BlockSpec(kv_block, pool_map(1, False)),
            pl.BlockSpec(kv_block, lambda j, c: (0, 0, 0)),
            pl.BlockSpec(kv_block, lambda j, c: (0, 0, 1)),
            pl.BlockSpec(kv_block, pool_map(0, True)),
            pl.BlockSpec(kv_block, pool_map(1, True)),
            pl.BlockSpec((None, blocks, keys_len), lambda j, c: (j, 0, 0)),
            pl.BlockSpec((heads, span, 1), lambda j, c: (0, 0, 0)),
            pl.BlockSpec((heads, span, 1), lambda j, c: (0, 0, 0)),
            pl.BlockSpec((heads, span, HD), lambda j, c: (0, 0, 0)),
        ],
        out_specs=pl.BlockSpec((span, width), lambda j, c: (0, 0)),
        scratch_shapes=[
            pltpu.VMEM((heads, span, 1), jnp.float32),
            pltpu.VMEM((heads, span, 1), jnp.float32),
            pltpu.VMEM((heads, span, HD), jnp.float32),
        ],
    )
    kernel = lambda *refs: flash_kernel(*refs, heads=heads, n_local=n_local, half=half)
    return pl.pallas_call(
        kernel,
        grid_spec=grid_spec,
        out_shape=jax.ShapeDtypeStruct((span, width), jnp.bfloat16),
        compiler_params=pltpu.CompilerParams(dimension_semantics=("arbitrary",)),
        cost_estimate=pl.CostEstimate(
            flops=4 * steps * heads * span * span * HD,
            transcendentals=steps * heads * span * span,
            bytes_accessed=2 * steps * span * width * 2,
        ),
    )(chosen, queries, before, before, earlier, earlier, same_core, same_core, sibling_own, sibling_own, other_core, other_core, bias, *state)


def fetch_out_weight(w_out, head, core):
    groups = lax.axis_size("head")
    columns = w_out.shape[1] // groups
    half = columns // 2
    blocks = jnp.stack([
        lax.dynamic_slice_in_dim(w_out, dest * columns + core * half, half, 1)
        for dest in range(groups)
    ])
    exchanged = lax.all_to_all(blocks, "head", 0, 0)
    mine = exchanged
    own_full = lax.dynamic_slice_in_dim(w_out, head * columns, columns, 1)
    return own_full, mine


def local(
    activations,
    mod_table,
    step_index,
    block_mask,
    cache_index,
    w_qkv,
    q_gain,
    k_gain,
    pool_kv,
    w_out,
):
    slot = lax.axis_index("slot")
    head = lax.axis_index("head")
    core = slot % 2
    groups = lax.axis_size("head")
    span = activations.shape[0]
    heads = q_gain.shape[0] // HD
    blocks_q = span // BLOCK
    cache_len = cache_index.shape[1]

    own_full, mine = fetch_out_weight(w_out, head, core)
    slots = lax.axis_size("slot")
    pool_flat = pool_kv.reshape(1, pool_kv.shape[1], -1)
    same_core = [pool_flat] + [from_behind(pool_flat, "slot", 2 * k) for k in range(1, slots // 2)]
    same_core = jnp.concatenate(same_core, axis=0)

    onehot = (jnp.arange(mod_table.shape[0], dtype=jnp.int32) == step_index[slot]).astype(
        jnp.float32
    )
    modulation = jnp.einsum("n,nkd->kd", onehot, mod_table.astype(jnp.float32))
    inputs = activations.astype(jnp.float32)
    normed = inputs * lax.rsqrt(jnp.mean(inputs * inputs, axis=-1, keepdims=True) + 1e-06)
    hidden = (normed * (1.0 + modulation[1][None, :]) + modulation[0][None, :]).astype(jnp.bfloat16)
    width = heads * HD
    qkv = jnp.einsum("td,dkh->kth", hidden, w_qkv, preferred_element_type=jnp.float32)
    queries = head_norm(qkv[0], q_gain, heads).astype(jnp.bfloat16)
    keys = head_norm(qkv[1], k_gain, heads).astype(jnp.bfloat16)
    values = qkv[2].astype(jnp.bfloat16)
    local_kv = jnp.concatenate([keys.reshape(span, heads * HD), values], axis=1)
    before = from_behind(local_kv, "slot", 1)
    earlier = from_behind(local_kv, "slot", 2)
    cuts = [(0, span - BLOCK), (span - BLOCK, span)]
    width = heads * HD
    own_mask = lax.dynamic_index_in_dim(block_mask, slot, 0, keepdims=False)
    flat_queries = queries.reshape(span, width)
    own_bias = jnp.zeros((1, blocks_q, span), jnp.float32)
    states = [
        flash_local(flat_queries[a:b], local_kv.reshape(1, span, 2 * width),
                    own_bias[:, a // BLOCK : b // BLOCK], heads)
        for a, b in cuts
    ]
    sibling_own = lax.ppermute(pool_flat, "slot", [(i, i ^ 1) for i in range(slots)])
    states, queries, before, earlier, same_core, sibling_own, mine = lax.optimization_barrier(
        (states, queries, before, earlier, same_core, sibling_own, mine)
    )
    other_core = lax.ppermute(same_core[1:], "slot", [(i, i ^ 1) for i in range(slots)])
    own_mask = lax.dynamic_index_in_dim(block_mask, slot, 0, keepdims=False)
    own_cache = lax.dynamic_index_in_dim(cache_index, slot, 0, keepdims=False)
    sibling_slot = jnp.bitwise_xor(slot, 1)
    own_cache = jnp.where(
        own_cache % 2 == core,
        ((slot - own_cache) % slots) // 2,
        slots // 2 + ((sibling_slot - own_cache) % slots) // 2,
    ).astype(jnp.int32)
    width = heads * HD
    visible = jnp.concatenate([jnp.ones((blocks_q, blocks_q), jnp.int32), own_mask], axis=1)
    visible = jnp.transpose(visible.reshape(blocks_q, 3 + cache_len, blocks_q), (1, 0, 2))
    visible = jnp.repeat(visible, BLOCK, axis=2)
    bias = jnp.where(visible > 0, 0.0, -1e30).astype(jnp.float32)
    cuts = [(0, span - BLOCK), (span - BLOCK, span)]
    queries = queries.reshape(span, width)
    mixed_parts = [
        flash(queries[a:b], before, earlier, same_core, sibling_own, other_core,
              bias[1:, a // BLOCK : b // BLOCK], own_cache, states[p], heads)
        for p, (a, b) in enumerate(cuts)
    ]
    sibling = lax.ppermute(
        mine, "slot", [(i, i ^ 1) for i in range(slots)]
    )

    received = [
        jnp.concatenate([
            lax.ppermute(part, "head", [(i, (i + shift) % groups) for i in range(groups)])
            for part in mixed_parts
        ], axis=0)
        for shift in range(1, groups)
    ]
    mixed = jnp.concatenate(mixed_parts, axis=0)
    columns = own_full.shape[1]
    half = columns // 2
    attn = jnp.dot(mixed, own_full, preferred_element_type=jnp.float32).astype(jnp.bfloat16).astype(jnp.float32)
    attn_mine = None
    attn_sib = None
    for shift in range(1, groups):
        group_o = received[shift - 1]
        group = (head - shift) % groups
        mine_block = lax.dynamic_index_in_dim(mine, group, 0, keepdims=False)
        part = jnp.dot(group_o, mine_block, preferred_element_type=jnp.float32)
        part = part.astype(jnp.bfloat16).astype(jnp.float32)
        attn_mine = part if attn_mine is None else attn_mine + part
        sibling_block = lax.dynamic_index_in_dim(sibling, group, 0, keepdims=False)
        part = jnp.dot(group_o, sibling_block, preferred_element_type=jnp.float32)
        part = part.astype(jnp.bfloat16).astype(jnp.float32)
        attn_sib = part if attn_sib is None else attn_sib + part
    other = jnp.concatenate([attn_mine, attn_sib], axis=1)
    swapped = jnp.concatenate([attn_sib, attn_mine], axis=1)
    attn = attn + jnp.where(core == 0, other, swapped)

    offset = head * columns
    input_cols = lax.dynamic_slice_in_dim(activations, offset, columns, 1).astype(jnp.float32)
    gate_cols = lax.dynamic_slice_in_dim(modulation[2], offset, columns, 0)
    return input_cols + gate_cols[None, :] * attn


def solution(mesh):
    placed = (
        P("slot", None),
        P(),
        P(),
        P(),
        P(),
        P(None, None, "head"),
        P("head"),
        P("head"),
        P("slot", None, None, "head"),
        P("head", None),
    )
    return jax.shard_map(
        local, mesh=mesh, in_specs=placed, out_specs=P("slot", "head"), check_vma=False
    )
```

```python
import jax
import jax.numpy as jnp
from jax import lax
from jax.sharding import PartitionSpec as P
from jax.experimental import pallas as pl
from jax.experimental.pallas import tpu as pltpu

HD = 128
BLOCK = 128


def from_behind(shard, axis, by):
    length = lax.axis_size(axis)
    return lax.ppermute(shard, axis, [(i, (i + by) % length) for i in range(length)])


def head_norm(values, gain, heads):
    outs = []
    for h in range(heads):
        cols = slice(h * HD, (h + 1) * HD)
        piece = values[:, cols]
        scaled = piece * lax.rsqrt(jnp.mean(piece * piece, axis=-1, keepdims=True) + 1e-06)
        outs.append(scaled * gain[cols][None, :])
    return jnp.concatenate(outs, axis=1)


def attend(state, queries, span_kv, visible_blocks):
    highest, totals, accum = state
    heads = queries.shape[1]
    span_keys = span_kv[:, 0].reshape(span_kv.shape[0], heads, HD)
    span_values = span_kv[:, 1].reshape(span_kv.shape[0], heads, HD)
    visible = jnp.repeat(jnp.repeat(visible_blocks, BLOCK, axis=0), BLOCK, axis=1) > 0
    scores = jnp.einsum("qhd,khd->hqk", queries, span_keys, preferred_element_type=jnp.float32) * (
        1.0 / HD**0.5
    )
    scores = jnp.where(visible[None], scores, -1e30)
    new_high = jnp.maximum(highest, jnp.max(scores, axis=-1))
    factor = jnp.exp(highest - new_high)
    weights = jnp.where(visible[None], jnp.exp(scores - new_high[..., None]), 0.0)
    totals = totals * factor + jnp.sum(weights, axis=-1)
    accum = accum * factor[..., None] + jnp.einsum(
        "hqk,khd->hqd",
        weights.astype(jnp.bfloat16),
        span_values,
        preferred_element_type=jnp.float32,
    )
    return (new_high, totals, accum)


def online_update(q_ref, k_ref, v_ref, bias_ref, m_sc, l_sc, acc_sc, heads):
    span = q_ref.shape[0]
    blocks = bias_ref.shape[0]
    bias = bias_ref[...][:, None, :]
    for h in range(heads):
        cols = slice(h * HD, (h + 1) * HD)
        q = q_ref[:, cols]
        k = k_ref[:, cols]
        s = lax.dot_general(q, k, (((1,), (1,)), ((), ())), preferred_element_type=jnp.float32)
        s = (s * (1.0 / HD**0.5)).reshape(blocks, span // blocks, s.shape[1]) + bias
        s = s.reshape(span, -1)
        m_prev = m_sc[h]
        m_new = jnp.maximum(m_prev, jnp.max(s, axis=1, keepdims=True))
        factor = jnp.exp(m_prev - m_new)
        p = jnp.exp(s - m_new)
        l_sc[h] = l_sc[h] * factor + jnp.sum(p, axis=1, keepdims=True)
        acc_sc[h] = acc_sc[h] * factor + jnp.dot(
            p.astype(jnp.bfloat16), v_ref[:, cols], preferred_element_type=jnp.float32
        )
        m_sc[h] = m_new


def local_kernel(q_ref, k_ref, v_ref, bias_ref, m_ref, l_ref, acc_ref, *, heads):
    @pl.when(pl.program_id(0) == 0)
    def _():
        m_ref[...] = jnp.full(m_ref.shape, -1e30, jnp.float32)
        l_ref[...] = jnp.zeros(l_ref.shape, jnp.float32)
        acc_ref[...] = jnp.zeros(acc_ref.shape, jnp.float32)

    online_update(q_ref, k_ref, v_ref, bias_ref, m_ref, l_ref, acc_ref, heads)


def flash_local(queries, local_stack, bias, heads):
    span, width = queries.shape
    steps, keys_len = local_stack.shape[:2]
    blocks = bias.shape[1]
    kv_block = (None, keys_len, width)
    state = pl.BlockSpec((heads, span, 1), lambda j: (0, 0, 0))
    kernel = lambda *refs: local_kernel(*refs, heads=heads)
    return pl.pallas_call(
        kernel,
        grid=(steps,),
        in_specs=[
            pl.BlockSpec((span, width), lambda j: (0, 0)),
            pl.BlockSpec(kv_block, lambda j: (j, 0, 0)),
            pl.BlockSpec(kv_block, lambda j: (j, 0, 1)),
            pl.BlockSpec((None, blocks, keys_len), lambda j: (j, 0, 0)),
        ],
        out_specs=[state, state, pl.BlockSpec((heads, span, HD), lambda j: (0, 0, 0))],
        out_shape=[
            jax.ShapeDtypeStruct((heads, span, 1), jnp.float32),
            jax.ShapeDtypeStruct((heads, span, 1), jnp.float32),
            jax.ShapeDtypeStruct((heads, span, HD), jnp.float32),
        ],
        compiler_params=pltpu.CompilerParams(dimension_semantics=("arbitrary",)),
        cost_estimate=pl.CostEstimate(
            flops=4 * steps * heads * span * keys_len * HD,
            transcendentals=steps * heads * span * keys_len,
            bytes_accessed=2 * steps * keys_len * width * 2,
        ),
    )(queries, local_stack, local_stack, bias)


def flash_kernel(chosen, q_ref, k1_ref, v1_ref, k2_ref, v2_ref, dk_ref, dv_ref, ak_ref, av_ref, ck_ref, cv_ref, bk_ref, bv_ref, bias_ref, m_in, l_in, acc_in, o_ref, m_sc, l_sc, acc_sc, *, heads, n_local, half):
    step = pl.program_id(0)
    span = q_ref.shape[0]
    blocks = bias_ref.shape[0]

    @pl.when(step == 0)
    def _():
        m_sc[...] = m_in[...]
        l_sc[...] = l_in[...]
        acc_sc[...] = acc_in[...]

    def body(k_ref, v_ref):
        bias = bias_ref[...][:, None, :]
        for h in range(heads):
            cols = slice(h * HD, (h + 1) * HD)
            q = q_ref[:, cols]
            k = k_ref[:, cols]
            s = lax.dot_general(q, k, (((1,), (1,)), ((), ())), preferred_element_type=jnp.float32)
            s = (s * (1.0 / HD**0.5)).reshape(blocks, span // blocks, s.shape[1]) + bias
            s = s.reshape(span, -1)
            m_prev = m_sc[h]
            m_new = jnp.maximum(m_prev, jnp.max(s, axis=1, keepdims=True))
            factor = jnp.exp(m_prev - m_new)
            p = jnp.exp(s - m_new)
            l_sc[h] = l_sc[h] * factor + jnp.sum(p, axis=1, keepdims=True)
            acc_sc[h] = acc_sc[h] * factor + jnp.dot(
                p.astype(jnp.bfloat16), v_ref[:, cols], preferred_element_type=jnp.float32
            )
            m_sc[h] = m_new

    @pl.when(step == 0)
    def _():
        body(k1_ref, v1_ref)

    @pl.when(step == 1)
    def _():
        body(k2_ref, v2_ref)

    pos = chosen[jnp.maximum(step - n_local, 0)]

    @pl.when((step >= n_local) & (pos == 0))
    def _():
        body(dk_ref, dv_ref)

    @pl.when((step >= n_local) & (pos > 0) & (pos < half))
    def _():
        body(ak_ref, av_ref)

    @pl.when((step >= n_local) & (pos == half))
    def _():
        body(ck_ref, cv_ref)

    @pl.when((step >= n_local) & (pos > half))
    def _():
        body(bk_ref, bv_ref)

    @pl.when(step == pl.num_programs(0) - 1)
    def _():
        for h in range(heads):
            cols = slice(h * HD, (h + 1) * HD)
            o_ref[:, cols] = (acc_sc[h] / l_sc[h]).astype(o_ref.dtype)


def flash(queries, before, earlier, own_pool, same_core, sibling_own, other_core, bias, chosen, state, heads):
    span, width = queries.shape
    n_local = 2
    half = same_core.shape[0] + 1
    steps = n_local + chosen.shape[0]
    blocks = bias.shape[1]

    def local_map(kv):
        return lambda j, c: (jnp.minimum(j, n_local - 1), 0, kv)

    def pool_map(kv, upper):
        def index(j, c):
            pos = c[jnp.maximum(j - n_local, 0)]
            if upper:
                hit = (j >= n_local) & (pos > half)
                return (jnp.where(hit, pos - half - 1, 0), 0, kv)
            hit = (j >= n_local) & (pos > 0) & (pos < half)
            return (jnp.where(hit, pos - 1, 0), 0, kv)

        return index

    keys_len = before.shape[0]
    kv_block = (None, keys_len, width)
    grid_spec = pltpu.PrefetchScalarGridSpec(
        num_scalar_prefetch=1,
        grid=(steps,),
        in_specs=[
            pl.BlockSpec((span, width), lambda j, c: (0, 0)),
            pl.BlockSpec((keys_len, width), lambda j, c: (0, 0)),
            pl.BlockSpec((keys_len, width), lambda j, c: (0, 1)),
            pl.BlockSpec((keys_len, width), lambda j, c: (0, 0)),
            pl.BlockSpec((keys_len, width), lambda j, c: (0, 1)),
            pl.BlockSpec(kv_block, lambda j, c: (0, 0, 0)),
            pl.BlockSpec(kv_block, lambda j, c: (0, 0, 1)),
            pl.BlockSpec(kv_block, pool_map(0, False)),
            pl.BlockSpec(kv_block, pool_map(1, False)),
            pl.BlockSpec(kv_block, lambda j, c: (0, 0, 0)),
            pl.BlockSpec(kv_block, lambda j, c: (0, 0, 1)),
            pl.BlockSpec(kv_block, pool_map(0, True)),
            pl.BlockSpec(kv_block, pool_map(1, True)),
            pl.BlockSpec((None, blocks, keys_len), lambda j, c: (j, 0, 0)),
            pl.BlockSpec((heads, span, 1), lambda j, c: (0, 0, 0)),
            pl.BlockSpec((heads, span, 1), lambda j, c: (0, 0, 0)),
            pl.BlockSpec((heads, span, HD), lambda j, c: (0, 0, 0)),
        ],
        out_specs=pl.BlockSpec((span, width), lambda j, c: (0, 0)),
        scratch_shapes=[
            pltpu.VMEM((heads, span, 1), jnp.float32),
            pltpu.VMEM((heads, span, 1), jnp.float32),
            pltpu.VMEM((heads, span, HD), jnp.float32),
        ],
    )
    kernel = lambda *refs: flash_kernel(*refs, heads=heads, n_local=n_local, half=half)
    return pl.pallas_call(
        kernel,
        grid_spec=grid_spec,
        out_shape=jax.ShapeDtypeStruct((span, width), jnp.bfloat16),
        compiler_params=pltpu.CompilerParams(dimension_semantics=("arbitrary",)),
        cost_estimate=pl.CostEstimate(
            flops=4 * steps * heads * span * span * HD,
            transcendentals=steps * heads * span * span,
            bytes_accessed=2 * steps * span * width * 2,
        ),
    )(chosen, queries, before, before, earlier, earlier, own_pool, own_pool, same_core, same_core, sibling_own, sibling_own, other_core, other_core, bias, *state)


def fetch_out_weight(w_out, head, core):
    groups = lax.axis_size("head")
    columns = w_out.shape[1] // groups
    half = columns // 2
    blocks = jnp.stack([
        lax.dynamic_slice_in_dim(w_out, dest * columns + core * half, half, 1)
        for dest in range(groups)
    ])
    exchanged = lax.all_to_all(blocks, "head", 0, 0)
    mine = exchanged
    own_full = lax.dynamic_slice_in_dim(w_out, head * columns, columns, 1)
    return own_full, mine


def local(
    activations,
    mod_table,
    step_index,
    block_mask,
    cache_index,
    w_qkv,
    q_gain,
    k_gain,
    pool_kv,
    w_out,
):
    slot = lax.axis_index("slot")
    head = lax.axis_index("head")
    core = slot % 2
    groups = lax.axis_size("head")
    span = activations.shape[0]
    heads = q_gain.shape[0] // HD
    blocks_q = span // BLOCK
    cache_len = cache_index.shape[1]

    own_full, mine = fetch_out_weight(w_out, head, core)
    slots = lax.axis_size("slot")
    pool_flat = pool_kv.reshape(1, pool_kv.shape[1], -1)
    same_core = [from_behind(pool_flat, "slot", 2 * k) for k in range(1, slots // 2)]
    same_core = jnp.concatenate(same_core, axis=0)

    onehot = (jnp.arange(mod_table.shape[0], dtype=jnp.int32) == step_index[slot]).astype(
        jnp.float32
    )
    modulation = jnp.einsum("n,nkd->kd", onehot, mod_table.astype(jnp.float32))
    inputs = activations.astype(jnp.float32)
    normed = inputs * lax.rsqrt(jnp.mean(inputs * inputs, axis=-1, keepdims=True) + 1e-06)
    hidden = (normed * (1.0 + modulation[1][None, :]) + modulation[0][None, :]).astype(jnp.bfloat16)
    width = heads * HD
    qkv = jnp.einsum("td,dkh->kth", hidden, w_qkv, preferred_element_type=jnp.float32)
    queries = head_norm(qkv[0], q_gain, heads).astype(jnp.bfloat16)
    keys = head_norm(qkv[1], k_gain, heads).astype(jnp.bfloat16)
    values = qkv[2].astype(jnp.bfloat16)
    local_kv = jnp.concatenate([keys.reshape(span, heads * HD), values], axis=1)
    before = from_behind(local_kv, "slot", 1)
    earlier = from_behind(local_kv, "slot", 2)
    rows = span // 2
    parts = rows // BLOCK
    width = heads * HD
    own_mask = lax.dynamic_index_in_dim(block_mask, slot, 0, keepdims=False)
    flat_queries = queries.reshape(span, width)
    own_bias = jnp.zeros((1, blocks_q, span), jnp.float32)
    states = [
        flash_local(flat_queries[p * rows : (p + 1) * rows], local_kv.reshape(1, span, 2 * width),
                    own_bias[:, p * parts : (p + 1) * parts], heads)
        for p in range(2)
    ]
    sibling_own = lax.ppermute(pool_flat, "slot", [(i, i ^ 1) for i in range(slots)])
    states, queries, before, earlier, same_core, sibling_own, mine = lax.optimization_barrier(
        (states, queries, before, earlier, same_core, sibling_own, mine)
    )
    other_core = lax.ppermute(same_core, "slot", [(i, i ^ 1) for i in range(slots)])
    own_mask = lax.dynamic_index_in_dim(block_mask, slot, 0, keepdims=False)
    own_cache = lax.dynamic_index_in_dim(cache_index, slot, 0, keepdims=False)
    sibling_slot = jnp.bitwise_xor(slot, 1)
    own_cache = jnp.where(
        own_cache % 2 == core,
        ((slot - own_cache) % slots) // 2,
        slots // 2 + ((sibling_slot - own_cache) % slots) // 2,
    ).astype(jnp.int32)
    width = heads * HD
    visible = jnp.concatenate([jnp.ones((blocks_q, blocks_q), jnp.int32), own_mask], axis=1)
    visible = jnp.transpose(visible.reshape(blocks_q, 3 + cache_len, blocks_q), (1, 0, 2))
    visible = jnp.repeat(visible, BLOCK, axis=2)
    bias = jnp.where(visible > 0, 0.0, -1e30).astype(jnp.float32)
    rows = span // 2
    parts = rows // BLOCK
    queries = queries.reshape(span, width)
    mixed_parts = [
        flash(queries[p * rows : (p + 1) * rows], before, earlier, pool_flat, same_core, sibling_own, other_core,
              bias[1:, p * parts : (p + 1) * parts], own_cache, states[p], heads)
        for p in range(2)
    ]
    sibling = lax.ppermute(
        mine, "slot", [(i, i ^ 1) for i in range(slots)]
    )

    received = [
        jnp.concatenate([
            lax.ppermute(part, "head", [(i, (i + shift) % groups) for i in range(groups)])
            for part in mixed_parts
        ], axis=0)
        for shift in range(1, groups)
    ]
    mixed = jnp.concatenate(mixed_parts, axis=0)
    columns = own_full.shape[1]
    half = columns // 2
    attn = jnp.dot(mixed, own_full, preferred_element_type=jnp.float32).astype(jnp.bfloat16).astype(jnp.float32)
    attn_mine = None
    attn_sib = None
    for shift in range(1, groups):
        group_o = received[shift - 1]
        group = (head - shift) % groups
        mine_block = lax.dynamic_index_in_dim(mine, group, 0, keepdims=False)
        part = jnp.dot(group_o, mine_block, preferred_element_type=jnp.float32)
        part = part.astype(jnp.bfloat16).astype(jnp.float32)
        attn_mine = part if attn_mine is None else attn_mine + part
        sibling_block = lax.dynamic_index_in_dim(sibling, group, 0, keepdims=False)
        part = jnp.dot(group_o, sibling_block, preferred_element_type=jnp.float32)
        part = part.astype(jnp.bfloat16).astype(jnp.float32)
        attn_sib = part if attn_sib is None else attn_sib + part
    other = jnp.concatenate([attn_mine, attn_sib], axis=1)
    swapped = jnp.concatenate([attn_sib, attn_mine], axis=1)
    attn = attn + jnp.where(core == 0, other, swapped)

    offset = head * columns
    input_cols = lax.dynamic_slice_in_dim(activations, offset, columns, 1).astype(jnp.float32)
    gate_cols = lax.dynamic_slice_in_dim(modulation[2], offset, columns, 0)
    return input_cols + gate_cols[None, :] * attn


def solution(mesh):
    placed = (
        P("slot", None),
        P(),
        P(),
        P(),
        P(),
        P(None, None, "head"),
        P("head"),
        P("head"),
        P("slot", None, None, "head"),
        P("head", None),
    )
    return jax.shard_map(
        local, mesh=mesh, in_specs=placed, out_specs=P("slot", "head"), check_vma=False
    )
```
